32 devices in a mesh: group: 2 (over y), seq: 16 (over z, x, core).
Axes of the slice: x: 2, y: 2, z: 4, core: 2. Of those that a mesh axis runs over, the one named last changes fastest.
Arguments:
- node_feats: bfloat16 [16384, 1024], P(('group', 'seq')), parts along dimension 0, may hold values from -6 to 6
- struct_feats: float32 [16384, 128], P(('group', 'seq')), parts along dimension 0, may hold values from -6 to 6
- op_blocks: float32 [256, 3, 64, 64], P(('group', 'seq')), parts along dimension 0, may hold values from -0.07 to 0.07
- laplace_index: int32 [256, 3], P(('group', 'seq')), parts along dimension 0, may hold values from 0 to 127, as said below
- graph_links: int32 [256, 3], P(('group', 'seq')), parts along dimension 0, may hold values from 0 to 127, as said below
- expander_slot: int32 [256, 4], P(('group', 'seq')), parts along dimension 0, may hold values from 0 to 7
- series_coef: float32 [9], replicated, may hold values from 0.3 to 1
- encode_weight: bfloat16 [128, 1024], replicated, may hold values from -0.5 to 0.5
- qkv_weight: bfloat16 [1024, 3072], replicated, may hold values from -0.1875 to 0.1875
- out_weight: bfloat16 [1024, 1024], replicated, may hold values from -0.1875 to 0.1875
Outputs:
- mixed: bfloat16 [16384, 1024], P(('group', 'seq')), parts along dimension 0
The draws below stay inside these ranges and needn't reach their ends.
There are 2 independent parts, one for each index of `group`. The reference program is written for one: setup_inputs(seed, part) draws one part's arguments, and reference() takes and returns one part's arrays. A program takes and returns all parts, laid end to end along the dimension named above; an argument that names none is the same for every part. Nothing has to cross between parts.
Inputs may be any that keep to these rules, and one draw needn't show every extreme that they name: `laplace_index`: each entry lies within 2 blocks of its row's block. `graph_links`: each entry lies within 2 blocks of its row's block.
All inputs are finite; a program needn't handle non-finite values.
Results may differ from the reference program's by a relative error of at most 0.012.
The reference program's roundings to bfloat16 on the way count: a program that leaves them out, or rounds other values in their place, can miss the bound.
Values may be sent and summed in bfloat16 or wider, within the bound.
No kernel may reach another device: no remote copies, remote signals or barrier semaphores. Data moves between devices by JAX's collectives and lax.ppermute only.
A program may use at most 192 MiB of HBM per device.

```python
import jax
import jax.numpy as jnp
from jax import lax

D = 1024
HEADS = 16
HD = 64
PCH = 128
BS = 64
BLK_DEV = 8
DEG = 8
NGL = 3
NEXP = 4
REACH = 2
NBLK = 128
NODES = 8192
N_SEQ = 16


def neighbor_blocks(key, columns):
    offsets = jax.random.randint(key, (NBLK, columns), -REACH, REACH + 1)
    offsets = offsets.at[0, 0].set(0)
    offsets = offsets.at[NBLK - 1, 0].set(0)
    blocks = jnp.arange(NBLK, dtype=jnp.int32)[:, None] + offsets
    return jnp.clip(blocks, 0, NBLK - 1).astype(jnp.int32)


def laplace_links(key):
    block_ids = jnp.arange(NBLK, dtype=jnp.int32)
    present = jax.random.randint(jax.random.fold_in(key, 31), (NBLK,), 0, 16) != 0
    forward = jnp.logical_and(present, block_ids + REACH < NBLK)
    backward = jnp.concatenate([jnp.zeros((REACH,), dtype=jnp.bool_), forward[:NBLK - REACH]])
    offsets = jax.random.randint(jax.random.fold_in(key, 37), (NBLK, 3), -REACH, REACH + 1)
    spare = jnp.clip(block_ids[:, None] + offsets, 0, NBLK - 1).astype(jnp.int32)
    first = jnp.where(forward, block_ids + REACH, spare[:, 0])
    second = jnp.where(backward, block_ids - REACH, spare[:, 1])
    stacked = jnp.stack([first, second, spare[:, 2]], axis=1).astype(jnp.int32)
    rotate = jax.random.randint(jax.random.fold_in(key, 41), (NBLK,), 0, 3)
    order = ((jnp.arange(3, dtype=jnp.int32)[None, :] + rotate[:, None]) % 3).astype(jnp.int32)
    return (forward, backward, order, jnp.take_along_axis(stacked, order, axis=1).astype(jnp.int32))


def draw_laplace_index(key, part):
    return laplace_links(jax.random.fold_in(key, 11))[3]


def draw_op_blocks(key, part):
    base = jax.random.fold_in(key, 11)
    forward, backward, order, index = laplace_links(base)
    block_keys = jax.random.split(jax.random.fold_in(base, 43), NBLK)
    perms = jax.vmap(lambda seed_key: jax.random.permutation(seed_key, BS))(block_keys).astype(jnp.int32)
    columns = jnp.arange(BS, dtype=jnp.int32)
    intersection = jnp.bitwise_and(perms[:, :, None], columns[None, None, :])
    parity = jnp.zeros_like(intersection)
    for level in range(BS.bit_length() - 1):
        parity = parity + jnp.bitwise_and(jnp.right_shift(intersection, level), 1)
    hadamard = (1 - 2 * (parity % 2)).astype(jnp.float32) / BS ** 0.5
    row_sign = (jax.random.randint(jax.random.fold_in(base, 47), (NBLK, BS), 0, 2) * 2 - 1).astype(jnp.float32)
    col_sign = (jax.random.randint(jax.random.fold_in(base, 53), (NBLK, BS), 0, 2) * 2 - 1).astype(jnp.float32)
    rotated = row_sign[:, :, None] * col_sign[:, None, :] * hadamard
    noise = jnp.clip(jax.random.normal(jax.random.fold_in(base, 59), (NBLK, 4, BS, BS), jnp.float32), -4.0, 4.0)
    linked = 0.43 * (rotated + 0.00625 * noise[:, 0])
    flipped = jnp.swapaxes(linked, 1, 2)
    behind = jnp.concatenate([jnp.zeros((REACH, BS, BS), jnp.float32), flipped[:NBLK - REACH]], axis=0)
    spare = 0.0025 * noise[:, 1:]
    first = jnp.where(forward[:, None, None], linked, spare[:, 0])
    second = jnp.where(backward[:, None, None], behind, spare[:, 1])
    stacked = jnp.stack([first, second, spare[:, 2]], axis=1)
    return jnp.take_along_axis(stacked, order[:, :, None, None], axis=1).astype(jnp.float32)


def draw_graph_links(key, part):
    return neighbor_blocks(jax.random.fold_in(key, 23), NGL)


def plant(values, own_key, least, top_value):
    dims = values.shape
    place = [jax.random.randint(jax.random.fold_in(own_key, axis), (), 0, dims[axis]) for axis in range(len(dims))]
    values = values.at[tuple(place)].set(least)
    longest = dims.index(max(dims))
    place[longest] = (place[longest] + 1) % dims[longest]
    return values.at[tuple(place)].set(top_value)


def level_of(stream_key, shape, shards, smallest, largest):
    gain, own = 1.0, jax.random.fold_in(stream_key, 6)
    for dim, shards_of in shards:
        steps = jnp.exp(jax.random.uniform(jax.random.fold_in(own, dim), (shards_of,), jnp.float32, smallest / len(shards), largest / len(shards)))
        gain = gain * jnp.repeat(steps, shape[dim] // shards_of).reshape([-1 if axis == dim else 1 for axis in range(len(shape))])
    return gain


def normal_values(stream_key, dims, width, limit, shards=(), held_as=jnp.bfloat16):
    values = jax.random.normal(stream_key, dims, jnp.float32) * width
    if len(shards) > 0:
        values = level_of(stream_key, dims, shards, -0.22, 0.18) * values
    return jnp.clip(values, min=-limit, max=limit).astype(held_as)


def setup_inputs(seed: int = 0, part: int = 0) -> dict:
    key_list = jax.random.split(jax.random.key(seed), 11)
    part_splits = jax.random.split(jax.random.fold_in(key_list[10], part), 11)
    return {
        "node_feats": normal_values(part_splits[0], (NODES, D), 1.0, 6.0, ((0, 16),)),
        "struct_feats": normal_values(part_splits[1], (NODES, PCH), 1.0, 6.0, ((0, 16),), jnp.float32),
        "op_blocks": draw_op_blocks(jax.random.fold_in(jax.random.fold_in(key_list[10], part), 71), part),
        "laplace_index": draw_laplace_index(jax.random.fold_in(jax.random.fold_in(key_list[10], part), 71), part),
        "graph_links": draw_graph_links(jax.random.fold_in(jax.random.fold_in(key_list[10], part), 71), part),
        "expander_slot": plant(jax.random.randint(part_splits[5], (NBLK, NEXP), 0, BLK_DEV), jax.random.fold_in(part_splits[5], 1), 0, BLK_DEV - 1).astype(jnp.int32),
        "series_coef": jnp.clip(jax.random.uniform(key_list[6], (DEG + 1,), jnp.float32, 0.3, 1.0), 0.3, 1.0),
        "encode_weight": normal_values(key_list[7], (PCH, D), PCH ** -0.5, 0.5),
        "qkv_weight": normal_values(key_list[8], (D, 3 * D), D ** -0.5, 0.1875),
        "out_weight": normal_values(key_list[9], (D, D), D ** -0.5, 0.1875),
    }


def apply_operator(field, op_blocks, laplace_index):
    count = op_blocks.shape[0]
    blocks = field.reshape(count, BS, field.shape[1])
    picked = blocks[laplace_index]
    result = jnp.einsum("bjst,bjtc->bsc", op_blocks, picked, precision=lax.Precision.HIGHEST)
    return result.reshape(field.shape)


def attend_block(query_block, picked):
    scale = 1.0 / (HD ** 0.5)
    keys = picked[:, :D].astype(jnp.float32).reshape(-1, HEADS, HD)
    values = picked[:, D:].astype(jnp.float32).reshape(-1, HEADS, HD)
    qheads = query_block.astype(jnp.float32).reshape(-1, HEADS, HD)
    scores = jnp.einsum("qhd,khd->hqk", qheads, keys) * scale
    weights = jax.nn.softmax(scores, axis=-1).astype(jnp.bfloat16)
    result = jnp.einsum("hqk,khd->qhd", weights.astype(jnp.float32), values)
    return result.reshape(-1, D).astype(jnp.bfloat16)


def reference(node_feats, struct_feats, op_blocks, laplace_index, graph_links, expander_slot, series_coef, encode_weight, qkv_weight, out_weight):
    previous = struct_feats
    current = apply_operator(previous, op_blocks, laplace_index)
    encoding = series_coef[0] * previous + series_coef[1] * current
    for degree in range(2, DEG + 1):
        following = 2.0 * apply_operator(current, op_blocks, laplace_index) - previous
        encoding = encoding + series_coef[degree] * following
        previous, current = current, following
    encoded = jnp.dot(encoding.astype(jnp.bfloat16), encode_weight, preferred_element_type=jnp.float32)
    blended = (node_feats.astype(jnp.float32) + encoded).astype(jnp.bfloat16)
    projected = jnp.dot(blended, qkv_weight, preferred_element_type=jnp.float32)
    queries = projected[:, :D].astype(jnp.bfloat16)
    keyvals = projected[:, D:].astype(jnp.bfloat16)
    count = laplace_index.shape[0]
    levels = N_SEQ.bit_length() - 1
    block_ids = jnp.arange(count, dtype=jnp.int32)
    device_of = block_ids // BLK_DEV
    bit_values = jnp.array([1 << (link * (levels - 1) // (NEXP - 1)) for link in range(NEXP)], dtype=jnp.int32)
    partner = jnp.bitwise_xor(device_of[:, None], bit_values[None, :])
    far_blocks = (partner * BLK_DEV + expander_slot).astype(jnp.int32)
    key_index = jnp.concatenate([block_ids[:, None], graph_links.astype(jnp.int32), far_blocks], axis=1).astype(jnp.int32)
    kv_blocks = keyvals.reshape(count, BS, 2 * D)
    query_blocks = queries.reshape(count, BS, D)

    def one_block(item):
        query_block, row = item
        picked = kv_blocks[row].reshape(-1, 2 * D)
        return attend_block(query_block, picked)

    attended = lax.map(one_block, (query_blocks, key_index)).reshape(-1, D)
    return jnp.dot(attended, out_weight, preferred_element_type=jnp.float32).astype(jnp.bfloat16)
```

```python
import functools

import jax
import jax.numpy as jnp
from jax import lax
from jax.experimental import pallas as pl
from jax.experimental.pallas import tpu as pltpu
from jax.sharding import PartitionSpec as P

D = 1024
HEADS = 16
HD = 64
BS = 64
DEG = 8
NEXP = 4
REACH = 2
NKEY = 1 + 3 + NEXP


def shift_rows(x, axis, step):
    peers = lax.axis_size(axis)
    if step > 0:
        pairs = [(i, i + step) for i in range(peers - step)]
    else:
        pairs = [(i, i + step) for i in range(-step, peers)]
    return lax.ppermute(x, axis, pairs)


def extended(x, axis, width):
    length = x.shape[0]
    before = shift_rows(x[length - width:], axis, 1)
    after = shift_rows(x[:width], axis, -1)
    return jnp.concatenate([before, x, after], axis=0)


def partner(value, axis, distance):
    mask = 2**distance
    pairs = [(source, source ^ mask) for source in range(lax.axis_size(axis))]
    return lax.ppermute(value, axis, pairs)


def apply_operator(field, op_blocks, laplace_index, first_block):
    count = op_blocks.shape[0]
    padded = extended(field, "seq", REACH * BS)
    pooled = padded.reshape(count + 2 * REACH, BS, field.shape[1])
    position = laplace_index - first_block + REACH
    picked = pooled[position]
    result = jnp.einsum("bjst,bjtc->bsc", op_blocks, picked, precision=lax.Precision.HIGHEST)
    return result.reshape(field.shape)


def attention_kernel(table_ref, q_ref, *refs):
    kv_refs = refs[:NKEY]
    out_ref = refs[NKEY]
    scale = 1.0 / HD**0.5
    lane = lax.broadcasted_iota(jnp.int32, (1, 2 * HD), 1)
    low = lane < HD
    for pair in range(HEADS // 2):
        cols = slice(pair * 2 * HD, (pair + 1) * 2 * HD)
        vcols = slice(D + pair * 2 * HD, D + (pair + 1) * 2 * HD)
        qs = q_ref[:, cols]
        ks = jnp.concatenate([r[:, cols] for r in kv_refs], axis=0)
        vs = jnp.concatenate([r[:, vcols] for r in kv_refs], axis=0)
        merged = None
        for half in range(2):
            keep = low if half == 0 else jnp.logical_not(low)
            qm = jnp.where(keep, qs, jnp.zeros_like(qs))
            scores = lax.dot_general(
                qm, ks, (((1,), (1,)), ((), ())), preferred_element_type=jnp.float32
            ) * scale
            top = jnp.max(scores, axis=-1, keepdims=True)
            expd = jnp.exp(scores - top)
            total = jnp.sum(expd, axis=-1, keepdims=True)
            weights = (expd / total).astype(jnp.bfloat16)
            part = jnp.dot(weights, vs, preferred_element_type=jnp.float32)
            merged = part if half == 0 else jnp.where(low, merged, part)
        out_ref[:, cols] = merged.astype(jnp.bfloat16)


def attend(queries, kv_sources, table):
    count = table.shape[0]
    in_specs = [pl.BlockSpec((BS, D), lambda b, t: (b, 0))]
    operands = [queries]
    for j, src in enumerate(kv_sources):
        in_specs.append(pl.BlockSpec((BS, 2 * D), lambda b, t, j=j: (t[b, j], 0)))
        operands.append(src)
    grid_spec = pltpu.PrefetchScalarGridSpec(
        num_scalar_prefetch=1,
        grid=(count,),
        in_specs=in_specs,
        out_specs=pl.BlockSpec((BS, D), lambda b, t: (b, 0)),
    )
    return pl.pallas_call(
        attention_kernel,
        grid_spec=grid_spec,
        out_shape=jax.ShapeDtypeStruct((count * BS, D), jnp.bfloat16),
    )(table, *operands)


def on_device(
    node_feats,
    struct_feats,
    op_blocks,
    laplace_index,
    graph_links,
    expander_slot,
    series_coef,
    encode_weight,
    qkv_weight,
    out_weight,
):
    count = op_blocks.shape[0]
    rows = count * BS
    rim = REACH * BS
    first_block = lax.axis_index("seq") * count
    levels = lax.axis_size("seq").bit_length() - 1
    bits = [link * (levels - 1) // (NEXP - 1) for link in range(NEXP)]

    feats_before = shift_rows(node_feats[rows - rim:], "seq", 1)
    feats_after = shift_rows(node_feats[:rim], "seq", -1)
    feats_far = [partner(node_feats, "seq", bit) for bit in bits]

    previous = struct_feats
    current = apply_operator(previous, op_blocks, laplace_index, first_block)
    encoding = series_coef[0] * previous + series_coef[1] * current
    for degree in range(2, DEG + 1):
        following = 2.0 * apply_operator(current, op_blocks, laplace_index, first_block) - previous
        encoding = encoding + series_coef[degree] * following
        previous, current = (current, following)
    encoding_b = encoding.astype(jnp.bfloat16)

    enc_before = shift_rows(encoding_b[rows - rim:], "seq", 1)
    enc_after = shift_rows(encoding_b[:rim], "seq", -1)
    enc_far = [partner(encoding_b, "seq", bit) for bit in bits]

    def blend(feats, enc):
        encoded = jnp.dot(enc, encode_weight, preferred_element_type=jnp.float32)
        return (feats.astype(jnp.float32) + encoded).astype(jnp.bfloat16)

    kv_weight = qkv_weight[:, D:]
    blended = blend(node_feats, encoding_b)
    queries = jnp.dot(blended, qkv_weight[:, :D], preferred_element_type=jnp.float32).astype(
        jnp.bfloat16
    )
    near_blended = jnp.concatenate(
        [blend(feats_before, enc_before), blended, blend(feats_after, enc_after)], axis=0
    )
    kv_near = jnp.dot(near_blended, kv_weight, preferred_element_type=jnp.float32).astype(
        jnp.bfloat16
    )
    kv_far = [
        jnp.dot(blend(f, e), kv_weight, preferred_element_type=jnp.float32).astype(jnp.bfloat16)
        for f, e in zip(feats_far, enc_far)
    ]

    near_blocks = count + 2 * REACH
    own_slot = jnp.arange(count, dtype=jnp.int32)[:, None] + REACH
    graph_slot = jnp.clip(graph_links - first_block + REACH, 0, near_blocks - 1)
    far_slot = jnp.clip(expander_slot, 0, count - 1)
    table = jnp.concatenate([own_slot, graph_slot, far_slot], axis=1).astype(jnp.int32)
    sources = [kv_near] * 4 + kv_far
    attended = attend(queries, sources, table)
    return jnp.dot(attended, out_weight, preferred_element_type=jnp.float32).astype(jnp.bfloat16)


def solution(mesh):
    placed = (
        P(("group", "seq"), None),
        P(("group", "seq"), None),
        P(("group", "seq"), None, None, None),
        P(("group", "seq"), None),
        P(("group", "seq"), None),
        P(("group", "seq"), None),
        P(),
        P(),
        P(),
        P(),
    )
    return jax.shard_map(
        on_device, mesh=mesh, in_specs=placed, out_specs=P(("group", "seq"), None), check_vma=False
    )
```

```python
import functools

import jax
import jax.numpy as jnp
from jax import lax
from jax.experimental import pallas as pl
from jax.experimental.pallas import tpu as pltpu
from jax.sharding import PartitionSpec as P

D = 1024
HEADS = 16
HD = 64
BS = 64
DEG = 8
NEXP = 4
REACH = 2
NKEY = 1 + 3 + NEXP


def shift_rows(x, axis, step):
    peers = lax.axis_size(axis)
    if step > 0:
        pairs = [(i, i + step) for i in range(peers - step)]
    else:
        pairs = [(i, i + step) for i in range(-step, peers)]
    return lax.ppermute(x, axis, pairs)


def extended(x, axis, width):
    length = x.shape[0]
    before = shift_rows(x[length - width:], axis, 1)
    after = shift_rows(x[:width], axis, -1)
    return jnp.concatenate([before, x, after], axis=0)


def partner(value, axis, distance):
    mask = 2**distance
    pairs = [(source, source ^ mask) for source in range(lax.axis_size(axis))]
    return lax.ppermute(value, axis, pairs)


def apply_operator(field, op_blocks, laplace_index, first_block):
    count = op_blocks.shape[0]
    padded = extended(field, "seq", REACH * BS)
    pooled = padded.reshape(count + 2 * REACH, BS, field.shape[1])
    position = laplace_index - first_block + REACH
    picked = pooled[position]
    result = jnp.einsum("bjst,bjtc->bsc", op_blocks, picked, precision=lax.Precision.HIGHEST)
    return result.reshape(field.shape)


def chebyshev(struct_feats, op_blocks, laplace_index, series_coef, first_block):
    count = op_blocks.shape[0]
    chans = struct_feats.shape[1]
    lap_rows = jnp.zeros((count, chans), jnp.float32).at[:, : laplace_index.shape[1]].set(
        laplace_index.astype(jnp.float32)
    )
    payload = jnp.concatenate(
        [struct_feats, op_blocks.reshape(-1, chans), lap_rows], axis=0
    )
    reach_dev = -(-DEG * REACH // count)
    parts = {0: payload}
    for off in range(1, reach_dev + 1):
        parts[-off] = shift_rows(payload, "seq", off)
        parts[off] = shift_rows(payload, "seq", -off)
    order = list(range(-reach_dev, reach_dev + 1))
    rows = count * BS
    n_op = op_blocks.size // chans
    field = jnp.concatenate([parts[o][:rows] for o in order], axis=0)
    field = field.reshape(-1, BS, chans)
    ops = jnp.concatenate(
        [parts[o][rows : rows + n_op].reshape(op_blocks.shape) for o in order], axis=0
    )
    lap = jnp.concatenate(
        [parts[o][rows + n_op : rows + n_op + count, : laplace_index.shape[1]] for o in order],
        axis=0,
    ).astype(jnp.int32)
    width = field.shape[0]
    centre = reach_dev * count
    block_ids = first_block - centre + jnp.arange(width, dtype=jnp.int32)
    offsets = lap - block_ids[:, None] + REACH
    diag = jnp.arange(2 * REACH + 1, dtype=jnp.int32)
    hit = offsets[:, :, None] == diag[None, None, :]
    bands = jnp.sum(
        jnp.where(hit[:, :, :, None, None], ops[:, :, None, :, :], 0.0), axis=1
    )

    def step(values, lo, hi, base):
        stacked = jnp.stack(
            [values[lo - REACH + o - base : hi - REACH + o - base] for o in range(2 * REACH + 1)],
            axis=1,
        )
        return jnp.einsum(
            "wosu,wouc->wsc", bands[lo:hi], stacked, precision=lax.Precision.HIGHEST
        )

    own = slice(centre, centre + count)
    prev, prev_base = field, 0
    lo, hi = REACH, width - REACH
    cur = step(field, lo, hi, 0)
    cur_base = lo
    encoding = series_coef[0] * field[own] + series_coef[1] * cur[centre - cur_base : centre - cur_base + count]
    for degree in range(2, DEG + 1):
        lo, hi = lo + REACH, hi - REACH
        nxt = 2.0 * step(cur, lo, hi, cur_base) - prev[lo - prev_base : hi - prev_base]
        encoding = encoding + series_coef[degree] * nxt[centre - lo : centre - lo + count]
        prev, prev_base = cur, cur_base
        cur, cur_base = nxt, lo
    return encoding.reshape(rows, chans)


def attention_kernel(table_ref, q_ref, *refs):
    kv_refs = refs[:NKEY]
    out_ref = refs[NKEY]
    scale = 1.0 / HD**0.5
    lane = lax.broadcasted_iota(jnp.int32, (1, 2 * HD), 1)
    low = lane < HD
    for pair in range(HEADS // 2):
        cols = slice(pair * 2 * HD, (pair + 1) * 2 * HD)
        vcols = slice(D + pair * 2 * HD, D + (pair + 1) * 2 * HD)
        qs = q_ref[:, cols]
        ks = jnp.concatenate([r[:, cols] for r in kv_refs], axis=0)
        vs = jnp.concatenate([r[:, vcols] for r in kv_refs], axis=0)
        merged = None
        for half in range(2):
            keep = low if half == 0 else jnp.logical_not(low)
            qm = jnp.where(keep, qs, jnp.zeros_like(qs))
            scores = lax.dot_general(
                qm, ks, (((1,), (1,)), ((), ())), preferred_element_type=jnp.float32
            ) * scale
            top = jnp.max(scores, axis=-1, keepdims=True)
            expd = jnp.exp(scores - top)
            total = jnp.sum(expd, axis=-1, keepdims=True)
            weights = (expd / total).astype(jnp.bfloat16)
            part = jnp.dot(weights, vs, preferred_element_type=jnp.float32)
            merged = part if half == 0 else jnp.where(low, merged, part)
        out_ref[:, cols] = merged.astype(jnp.bfloat16)


def attend(queries, kv_sources, table):
    count = table.shape[0]
    in_specs = [pl.BlockSpec((BS, D), lambda b, t: (b, 0))]
    operands = [queries]
    for j, src in enumerate(kv_sources):
        in_specs.append(pl.BlockSpec((BS, 2 * D), lambda b, t, j=j: (t[b, j], 0)))
        operands.append(src)
    grid_spec = pltpu.PrefetchScalarGridSpec(
        num_scalar_prefetch=1,
        grid=(count,),
        in_specs=in_specs,
        out_specs=pl.BlockSpec((BS, D), lambda b, t: (b, 0)),
    )
    return pl.pallas_call(
        attention_kernel,
        grid_spec=grid_spec,
        out_shape=jax.ShapeDtypeStruct((count * BS, D), jnp.bfloat16),
    )(table, *operands)


def on_device(
    node_feats,
    struct_feats,
    op_blocks,
    laplace_index,
    graph_links,
    expander_slot,
    series_coef,
    encode_weight,
    qkv_weight,
    out_weight,
):
    count = op_blocks.shape[0]
    rows = count * BS
    rim = REACH * BS
    first_block = lax.axis_index("seq") * count
    levels = lax.axis_size("seq").bit_length() - 1
    bits = [link * (levels - 1) // (NEXP - 1) for link in range(NEXP)]

    feats_before = shift_rows(node_feats[rows - rim:], "seq", 1)
    feats_after = shift_rows(node_feats[:rim], "seq", -1)
    feats_far = [partner(node_feats, "seq", bit) for bit in bits]

    encoding = chebyshev(struct_feats, op_blocks, laplace_index, series_coef, first_block)
    encoding_b = encoding.astype(jnp.bfloat16)

    enc_before = shift_rows(encoding_b[rows - rim:], "seq", 1)
    enc_after = shift_rows(encoding_b[:rim], "seq", -1)
    enc_far = [partner(encoding_b, "seq", bit) for bit in bits]

    def blend(feats, enc):
        encoded = jnp.dot(enc, encode_weight, preferred_element_type=jnp.float32)
        return (feats.astype(jnp.float32) + encoded).astype(jnp.bfloat16)

    kv_weight = qkv_weight[:, D:]
    blended = blend(node_feats, encoding_b)
    queries = jnp.dot(blended, qkv_weight[:, :D], preferred_element_type=jnp.float32).astype(
        jnp.bfloat16
    )
    near_blended = jnp.concatenate(
        [blend(feats_before, enc_before), blended, blend(feats_after, enc_after)], axis=0
    )
    kv_near = jnp.dot(near_blended, kv_weight, preferred_element_type=jnp.float32).astype(
        jnp.bfloat16
    )
    kv_far = [
        jnp.dot(blend(f, e), kv_weight, preferred_element_type=jnp.float32).astype(jnp.bfloat16)
        for f, e in zip(feats_far, enc_far)
    ]

    near_blocks = count + 2 * REACH
    own_slot = jnp.arange(count, dtype=jnp.int32)[:, None] + REACH
    graph_slot = jnp.clip(graph_links - first_block + REACH, 0, near_blocks - 1)
    far_slot = jnp.clip(expander_slot, 0, count - 1)
    table = jnp.concatenate([own_slot, graph_slot, far_slot], axis=1).astype(jnp.int32)
    sources = [kv_near] * 4 + kv_far
    attended = attend(queries, sources, table)
    return jnp.dot(attended, out_weight, preferred_element_type=jnp.float32).astype(jnp.bfloat16)


def solution(mesh):
    placed = (
        P(("group", "seq"), None),
        P(("group", "seq"), None),
        P(("group", "seq"), None, None, None),
        P(("group", "seq"), None),
        P(("group", "seq"), None),
        P(("group", "seq"), None),
        P(),
        P(),
        P(),
        P(),
    )
    return jax.shard_map(
        on_device, mesh=mesh, in_specs=placed, out_specs=P(("group", "seq"), None), check_vma=False
    )
```

```python
import functools

import jax
import jax.numpy as jnp
from jax import lax
from jax.experimental import pallas as pl
from jax.experimental.pallas import tpu as pltpu
from jax.sharding import PartitionSpec as P

D = 1024
HEADS = 16
HD = 64
BS = 64
DEG = 8
NEXP = 4
REACH = 2
NKEY = 1 + 3 + NEXP


def shift_rows(x, axis, step):
    peers = lax.axis_size(axis)
    if step > 0:
        pairs = [(i, i + step) for i in range(peers - step)]
    else:
        pairs = [(i, i + step) for i in range(-step, peers)]
    return lax.ppermute(x, axis, pairs)


def extended(x, axis, width):
    length = x.shape[0]
    before = shift_rows(x[length - width:], axis, 1)
    after = shift_rows(x[:width], axis, -1)
    return jnp.concatenate([before, x, after], axis=0)


def partner(value, axis, distance):
    mask = 2**distance
    pairs = [(source, source ^ mask) for source in range(lax.axis_size(axis))]
    return lax.ppermute(value, axis, pairs)


def apply_operator(field, op_blocks, laplace_index, first_block):
    count = op_blocks.shape[0]
    padded = extended(field, "seq", REACH * BS)
    pooled = padded.reshape(count + 2 * REACH, BS, field.shape[1])
    position = laplace_index - first_block + REACH
    picked = pooled[position]
    result = jnp.einsum("bjst,bjtc->bsc", op_blocks, picked, precision=lax.Precision.HIGHEST)
    return result.reshape(field.shape)


def chebyshev(struct_feats, op_blocks, laplace_index, series_coef, first_block):
    count = op_blocks.shape[0]
    chans = struct_feats.shape[1]
    reach_dev = -(-DEG * REACH // count)
    payload = (struct_feats, op_blocks, laplace_index)
    parts = {0: payload}
    for off in range(1, reach_dev + 1):
        parts[-off] = shift_rows(payload, "seq", off)
        parts[off] = shift_rows(payload, "seq", -off)
    order = list(range(-reach_dev, reach_dev + 1))
    rows = count * BS
    field = jnp.concatenate([parts[o][0] for o in order], axis=0).reshape(-1, BS, chans)
    ops = jnp.concatenate([parts[o][1] for o in order], axis=0)
    lap = jnp.concatenate([parts[o][2] for o in order], axis=0)
    width = field.shape[0]
    centre = reach_dev * count
    block_ids = first_block - centre + jnp.arange(width, dtype=jnp.int32)
    offsets = lap - block_ids[:, None] + REACH
    diag = jnp.arange(2 * REACH + 1, dtype=jnp.int32)
    hit = offsets[:, :, None] == diag[None, None, :]
    bands = jnp.sum(
        jnp.where(hit[:, :, :, None, None], ops[:, :, None, :, :], 0.0), axis=1
    )

    def step(values, lo, hi, base):
        stacked = jnp.stack(
            [values[lo - REACH + o - base : hi - REACH + o - base] for o in range(2 * REACH + 1)],
            axis=1,
        )
        return jnp.einsum(
            "wosu,wouc->wsc", bands[lo:hi], stacked, precision=lax.Precision.HIGHEST
        )

    own = slice(centre, centre + count)
    prev, prev_base = field, 0
    lo, hi = REACH, width - REACH
    cur = step(field, lo, hi, 0)
    cur_base = lo
    encoding = series_coef[0] * field[own] + series_coef[1] * cur[centre - cur_base : centre - cur_base + count]
    for degree in range(2, DEG + 1):
        lo, hi = lo + REACH, hi - REACH
        nxt = 2.0 * step(cur, lo, hi, cur_base) - prev[lo - prev_base : hi - prev_base]
        encoding = encoding + series_coef[degree] * nxt[centre - lo : centre - lo + count]
        prev, prev_base = cur, cur_base
        cur, cur_base = nxt, lo
    return encoding.reshape(rows, chans), parts


def attention_kernel(table_ref, q_ref, *refs):
    kv_refs = refs[:NKEY]
    out_ref = refs[NKEY]
    scale = 1.0 / HD**0.5
    lane = lax.broadcasted_iota(jnp.int32, (1, 2 * HD), 1)
    low = lane < HD
    for pair in range(HEADS // 2):
        cols = slice(pair * 2 * HD, (pair + 1) * 2 * HD)
        vcols = slice(D + pair * 2 * HD, D + (pair + 1) * 2 * HD)
        qs = q_ref[:, cols]
        ks = jnp.concatenate([r[:, cols] for r in kv_refs], axis=0)
        vs = jnp.concatenate([r[:, vcols] for r in kv_refs], axis=0)
        merged = None
        for half in range(2):
            keep = low if half == 0 else jnp.logical_not(low)
            qm = jnp.where(keep, qs, jnp.zeros_like(qs))
            scores = lax.dot_general(
                qm, ks, (((1,), (1,)), ((), ())), preferred_element_type=jnp.float32
            ) * scale
            top = jnp.max(scores, axis=-1, keepdims=True)
            expd = jnp.exp(scores - top)
            total = jnp.sum(expd, axis=-1, keepdims=True)
            weights = (expd / total).astype(jnp.bfloat16)
            part = jnp.dot(weights, vs, preferred_element_type=jnp.float32)
            merged = part if half == 0 else jnp.where(low, merged, part)
        out_ref[:, cols] = merged.astype(jnp.bfloat16)


def attend(queries, kv_sources, table):
    count = table.shape[0]
    in_specs = [pl.BlockSpec((BS, D), lambda b, t: (b, 0))]
    operands = [queries]
    for j, src in enumerate(kv_sources):
        in_specs.append(pl.BlockSpec((BS, 2 * D), lambda b, t, j=j: (t[b, j], 0)))
        operands.append(src)
    grid_spec = pltpu.PrefetchScalarGridSpec(
        num_scalar_prefetch=1,
        grid=(count,),
        in_specs=in_specs,
        out_specs=pl.BlockSpec((BS, D), lambda b, t: (b, 0)),
    )
    return pl.pallas_call(
        attention_kernel,
        grid_spec=grid_spec,
        out_shape=jax.ShapeDtypeStruct((count * BS, D), jnp.bfloat16),
    )(table, *operands)


def on_device(
    node_feats,
    struct_feats,
    op_blocks,
    laplace_index,
    graph_links,
    expander_slot,
    series_coef,
    encode_weight,
    qkv_weight,
    out_weight,
):
    count = op_blocks.shape[0]
    rows = count * BS
    rim = REACH * BS
    first_block = lax.axis_index("seq") * count
    levels = lax.axis_size("seq").bit_length() - 1
    bits = [link * (levels - 1) // (NEXP - 1) for link in range(NEXP)]

    encoding, parts = chebyshev(struct_feats, op_blocks, laplace_index, series_coef, first_block)
    held = lax.optimization_barrier((node_feats, [p[0] for p in parts.values()]))[0]
    feats_before = shift_rows(held[rows - rim:], "seq", 1)
    feats_after = shift_rows(held[:rim], "seq", -1)
    feats_far = [partner(held, "seq", bit) for bit in bits[1:]]
    encoding, feats_before, feats_after, feats_far = lax.optimization_barrier(
        (encoding, feats_before, feats_after, feats_far)
    )
    encoding_b = encoding.astype(jnp.bfloat16)

    enc_before = shift_rows(encoding_b[rows - rim:], "seq", 1)
    enc_after = shift_rows(encoding_b[:rim], "seq", -1)
    enc_far = [partner(encoding_b, "seq", bit) for bit in bits[1:]]

    def blend(feats, enc):
        encoded = jnp.dot(enc, encode_weight, preferred_element_type=jnp.float32)
        return (feats.astype(jnp.float32) + encoded).astype(jnp.bfloat16)

    kv_weight = qkv_weight[:, D:]
    blended = blend(node_feats, encoding_b)
    queries = jnp.dot(blended, qkv_weight[:, :D], preferred_element_type=jnp.float32).astype(
        jnp.bfloat16
    )
    near_blended = jnp.concatenate(
        [blend(feats_before, enc_before), blended, blend(feats_after, enc_after)], axis=0
    )
    kv_near = jnp.dot(near_blended, kv_weight, preferred_element_type=jnp.float32).astype(
        jnp.bfloat16
    )
    kv_own = kv_near[rim : rim + rows]
    kv_far = [partner(kv_own, "seq", bits[0])] + [
        jnp.dot(blend(f, e), kv_weight, preferred_element_type=jnp.float32).astype(jnp.bfloat16)
        for f, e in zip(feats_far, enc_far)
    ]

    near_blocks = count + 2 * REACH
    own_slot = jnp.arange(count, dtype=jnp.int32)[:, None] + REACH
    graph_slot = jnp.clip(graph_links - first_block + REACH, 0, near_blocks - 1)
    far_slot = jnp.clip(expander_slot, 0, count - 1)
    table = jnp.concatenate([own_slot, graph_slot, far_slot], axis=1).astype(jnp.int32)
    sources = [kv_near] * 4 + kv_far
    attended = attend(queries, sources, table)
    return jnp.dot(attended, out_weight, preferred_element_type=jnp.float32).astype(jnp.bfloat16)


def solution(mesh):
    placed = (
        P(("group", "seq"), None),
        P(("group", "seq"), None),
        P(("group", "seq"), None, None, None),
        P(("group", "seq"), None),
        P(("group", "seq"), None),
        P(("group", "seq"), None),
        P(),
        P(),
        P(),
        P(),
    )
    return jax.shard_map(
        on_device, mesh=mesh, in_specs=placed, out_specs=P(("group", "seq"), None), check_vma=False
    )
```

```python
import functools

import jax
import jax.numpy as jnp
from jax import lax
from jax.experimental import pallas as pl
from jax.experimental.pallas import tpu as pltpu
from jax.sharding import PartitionSpec as P

D = 1024
HEADS = 16
HD = 64
BS = 64
DEG = 8
NEXP = 4
REACH = 2
NKEY = 1 + 3 + NEXP


def shift_rows(x, axis, step):
    peers = lax.axis_size(axis)
    if step > 0:
        pairs = [(i, i + step) for i in range(peers - step)]
    else:
        pairs = [(i, i + step) for i in range(-step, peers)]
    return lax.ppermute(x, axis, pairs)


def extended(x, axis, width):
    length = x.shape[0]
    before = shift_rows(x[length - width:], axis, 1)
    after = shift_rows(x[:width], axis, -1)
    return jnp.concatenate([before, x, after], axis=0)


def partner(value, axis, distance):
    mask = 2**distance
    pairs = [(source, source ^ mask) for source in range(lax.axis_size(axis))]
    return lax.ppermute(value, axis, pairs)


def apply_operator(field, op_blocks, laplace_index, first_block):
    count = op_blocks.shape[0]
    padded = extended(field, "seq", REACH * BS)
    pooled = padded.reshape(count + 2 * REACH, BS, field.shape[1])
    position = laplace_index - first_block + REACH
    picked = pooled[position]
    result = jnp.einsum("bjst,bjtc->bsc", op_blocks, picked, precision=lax.Precision.HIGHEST)
    return result.reshape(field.shape)


def chebyshev(struct_feats, op_blocks, laplace_index, series_coef, first_block):
    count = op_blocks.shape[0]
    chans = struct_feats.shape[1]
    taps = 2 * REACH + 1
    reach_dev = -(-DEG * REACH // count)
    block_ids = first_block + jnp.arange(count, dtype=jnp.int32)
    offsets = laplace_index - block_ids[:, None] + REACH
    hit = offsets[:, :, None] == jnp.arange(taps, dtype=jnp.int32)[None, None, :]
    bands = jnp.sum(jnp.where(hit[:, :, :, None, None], op_blocks[:, :, None], 0.0), axis=1)
    bands = bands.transpose(0, 2, 1, 3).reshape(count, BS, taps * BS)
    payload = jnp.concatenate([struct_feats.reshape(count, BS, chans), bands], axis=2)
    parts = {0: payload}
    for off in range(1, reach_dev + 1):
        parts[-off] = shift_rows(payload, "seq", off)
        parts[off] = shift_rows(payload, "seq", -off)
    window = jnp.concatenate([parts[o] for o in range(-reach_dev, reach_dev + 1)], axis=0)
    field = window[:, :, :chans]
    bands = window[:, :, chans:]
    width = window.shape[0]
    centre = reach_dev * count

    def step(values, lo, hi, base):
        stacked = jnp.stack(
            [values[lo - REACH + o - base : hi - REACH + o - base] for o in range(taps)], axis=1
        ).reshape(hi - lo, taps * BS, chans)
        return jnp.einsum(
            "wsk,wkc->wsc", bands[lo:hi], stacked, precision=lax.Precision.HIGH,
            preferred_element_type=jnp.float32,
        )

    own = slice(centre, centre + count)
    prev, prev_base = field, 0
    lo, hi = REACH, width - REACH
    cur = step(field, lo, hi, 0)
    cur_base = lo
    encoding = series_coef[0] * field[own] + series_coef[1] * cur[centre - cur_base : centre - cur_base + count]
    for degree in range(2, DEG + 1):
        lo, hi = lo + REACH, hi - REACH
        nxt = 2.0 * step(cur, lo, hi, cur_base) - prev[lo - prev_base : hi - prev_base]
        encoding = encoding + series_coef[degree] * nxt[centre - lo : centre - lo + count]
        prev, prev_base = cur, cur_base
        cur, cur_base = nxt, lo
    return encoding.reshape(count * BS, chans), parts


def attention_kernel(table_ref, q_ref, *refs):
    kv_refs = refs[:NKEY]
    out_ref = refs[NKEY]
    scale = 1.0 / HD**0.5
    lane = lax.broadcasted_iota(jnp.int32, (1, 2 * HD), 1)
    low = lane < HD
    for pair in range(HEADS // 2):
        cols = slice(pair * 2 * HD, (pair + 1) * 2 * HD)
        vcols = slice(D + pair * 2 * HD, D + (pair + 1) * 2 * HD)
        qs = q_ref[:, cols]
        ks = jnp.concatenate([r[:, cols] for r in kv_refs], axis=0)
        vs = jnp.concatenate([r[:, vcols] for r in kv_refs], axis=0)
        merged = None
        for half in range(2):
            keep = low if half == 0 else jnp.logical_not(low)
            qm = jnp.where(keep, qs, jnp.zeros_like(qs))
            scores = lax.dot_general(
                qm, ks, (((1,), (1,)), ((), ())), preferred_element_type=jnp.float32
            ) * scale
            top = jnp.max(scores, axis=-1, keepdims=True)
            expd = jnp.exp(scores - top)
            total = jnp.sum(expd, axis=-1, keepdims=True)
            weights = (expd / total).astype(jnp.bfloat16)
            part = jnp.dot(weights, vs, preferred_element_type=jnp.float32)
            merged = part if half == 0 else jnp.where(low, merged, part)
        out_ref[:, cols] = merged.astype(jnp.bfloat16)


def attend(queries, kv_sources, table):
    count = table.shape[0]
    in_specs = [pl.BlockSpec((BS, D), lambda b, t: (b, 0))]
    operands = [queries]
    for j, src in enumerate(kv_sources):
        in_specs.append(pl.BlockSpec((BS, 2 * D), lambda b, t, j=j: (t[b, j], 0)))
        operands.append(src)
    grid_spec = pltpu.PrefetchScalarGridSpec(
        num_scalar_prefetch=1,
        grid=(count,),
        in_specs=in_specs,
        out_specs=pl.BlockSpec((BS, D), lambda b, t: (b, 0)),
    )
    return pl.pallas_call(
        attention_kernel,
        grid_spec=grid_spec,
        out_shape=jax.ShapeDtypeStruct((count * BS, D), jnp.bfloat16),
    )(table, *operands)


def on_device(
    node_feats,
    struct_feats,
    op_blocks,
    laplace_index,
    graph_links,
    expander_slot,
    series_coef,
    encode_weight,
    qkv_weight,
    out_weight,
):
    count = op_blocks.shape[0]
    rows = count * BS
    rim = REACH * BS
    first_block = lax.axis_index("seq") * count
    levels = lax.axis_size("seq").bit_length() - 1
    bits = [link * (levels - 1) // (NEXP - 1) for link in range(NEXP)]

    encoding, parts = chebyshev(struct_feats, op_blocks, laplace_index, series_coef, first_block)
    held = lax.optimization_barrier((node_feats, list(parts.values())))[0]
    feats_before = shift_rows(held[rows - rim:], "seq", 1)
    feats_after = shift_rows(held[:rim], "seq", -1)
    feats_far = [partner(held, "seq", bit) for bit in bits[1:]]
    encoding, feats_before, feats_after, feats_far = lax.optimization_barrier(
        (encoding, feats_before, feats_after, feats_far)
    )
    encoding_b = encoding.astype(jnp.bfloat16)

    enc_before = shift_rows(encoding_b[rows - rim:], "seq", 1)
    enc_after = shift_rows(encoding_b[:rim], "seq", -1)
    enc_far = [partner(encoding_b, "seq", bit) for bit in bits[1:]]

    def blend(feats, enc):
        encoded = jnp.dot(enc, encode_weight, preferred_element_type=jnp.float32)
        return (feats.astype(jnp.float32) + encoded).astype(jnp.bfloat16)

    kv_weight = qkv_weight[:, D:]
    blended = blend(node_feats, encoding_b)
    queries = jnp.dot(blended, qkv_weight[:, :D], preferred_element_type=jnp.float32).astype(
        jnp.bfloat16
    )
    near_blended = jnp.concatenate(
        [blend(feats_before, enc_before), blended, blend(feats_after, enc_after)], axis=0
    )
    kv_near = jnp.dot(near_blended, kv_weight, preferred_element_type=jnp.float32).astype(
        jnp.bfloat16
    )
    kv_own = kv_near[rim : rim + rows]
    kv_far = [partner(kv_own, "seq", bits[0])] + [
        jnp.dot(blend(f, e), kv_weight, preferred_element_type=jnp.float32).astype(jnp.bfloat16)
        for f, e in zip(feats_far, enc_far)
    ]

    near_blocks = count + 2 * REACH
    own_slot = jnp.arange(count, dtype=jnp.int32)[:, None] + REACH
    graph_slot = jnp.clip(graph_links - first_block + REACH, 0, near_blocks - 1)
    far_slot = jnp.clip(expander_slot, 0, count - 1)
    table = jnp.concatenate([own_slot, graph_slot, far_slot], axis=1).astype(jnp.int32)
    sources = [kv_near] * 4 + kv_far
    attended = attend(queries, sources, table)
    return jnp.dot(attended, out_weight, preferred_element_type=jnp.float32).astype(jnp.bfloat16)


def solution(mesh):
    placed = (
        P(("group", "seq"), None),
        P(("group", "seq"), None),
        P(("group", "seq"), None, None, None),
        P(("group", "seq"), None),
        P(("group", "seq"), None),
        P(("group", "seq"), None),
        P(),
        P(),
        P(),
        P(),
    )
    return jax.shard_map(
        on_device, mesh=mesh, in_specs=placed, out_specs=P(("group", "seq"), None), check_vma=False
    )
```

```python
import functools

import jax
import jax.numpy as jnp
from jax import lax
from jax.experimental import pallas as pl
from jax.experimental.pallas import tpu as pltpu
from jax.sharding import PartitionSpec as P

D = 1024
HEADS = 16
HD = 64
BS = 64
DEG = 8
NEXP = 4
REACH = 2
NKEY = 1 + 3 + NEXP
PER_EXCHANGE = 4


def shift_rows(x, axis, step):
    peers = lax.axis_size(axis)
    if step > 0:
        pairs = [(i, i + step) for i in range(peers - step)]
    else:
        pairs = [(i, i + step) for i in range(-step, peers)]
    return lax.ppermute(x, axis, pairs)


def extended(x, axis, width):
    length = x.shape[0]
    before = shift_rows(x[length - width:], axis, 1)
    after = shift_rows(x[:width], axis, -1)
    return jnp.concatenate([before, x, after], axis=0)


def partner(value, axis, distance):
    mask = 2**distance
    pairs = [(source, source ^ mask) for source in range(lax.axis_size(axis))]
    return lax.ppermute(value, axis, pairs)


def apply_operator(field, op_blocks, laplace_index, first_block):
    count = op_blocks.shape[0]
    padded = extended(field, "seq", REACH * BS)
    pooled = padded.reshape(count + 2 * REACH, BS, field.shape[1])
    position = laplace_index - first_block + REACH
    picked = pooled[position]
    result = jnp.einsum("bjst,bjtc->bsc", op_blocks, picked, precision=lax.Precision.HIGHEST)
    return result.reshape(field.shape)


def chebyshev(struct_feats, op_blocks, laplace_index, series_coef, first_block):
    count = op_blocks.shape[0]
    chans = struct_feats.shape[1]
    taps = 2 * REACH + 1
    halo = PER_EXCHANGE * REACH
    block_ids = first_block + jnp.arange(count, dtype=jnp.int32)
    offsets = laplace_index - block_ids[:, None] + REACH
    hit = offsets[:, :, None] == jnp.arange(taps, dtype=jnp.int32)[None, None, :]
    bands = jnp.sum(jnp.where(hit[:, :, :, None, None], op_blocks[:, :, None], 0.0), axis=1)
    bands = bands.transpose(0, 2, 1, 3).reshape(count, BS, taps * BS)
    own_field = struct_feats.reshape(count, BS, chans)
    payload = jnp.concatenate([own_field, bands], axis=2)
    left = shift_rows(payload, "seq", 1)
    right = shift_rows(payload, "seq", -1)
    edge = halo - REACH
    bands = jnp.concatenate(
        [left[count - edge :, :, chans:], bands, right[:edge, :, chans:]], axis=0
    )
    field = jnp.concatenate(
        [left[count - halo :, :, :chans], own_field, right[:halo, :, :chans]], axis=0
    )
    width = field.shape[0]

    def step(values, lo, hi, base):
        stacked = jnp.stack(
            [values[lo - REACH + o - base : hi - REACH + o - base] for o in range(taps)], axis=1
        ).reshape(hi - lo, taps * BS, chans)
        return jnp.einsum(
            "wsk,wkc->wsc", bands[lo - REACH : hi - REACH], stacked,
            precision=lax.Precision.HIGH, preferred_element_type=jnp.float32,
        )

    own = slice(halo, halo + count)
    cur, cur_base = field, 0
    prev, prev_base = None, 0
    encoding = series_coef[0] * field[own]
    for degree in range(1, DEG + 1):
        if degree > 1 and (degree - 1) % PER_EXCHANGE == 0:
            packed = jnp.concatenate([prev[own.start - prev_base : own.stop - prev_base], cur], axis=2)
            left = shift_rows(packed, "seq", 1)
            right = shift_rows(packed, "seq", -1)
            older = prev[own.start - prev_base : own.stop - prev_base]
            prev = jnp.concatenate(
                [left[count - edge :, :, :chans], older, right[:edge, :, :chans]], axis=0
            )
            prev_base = REACH
            cur = jnp.concatenate(
                [left[count - halo :, :, chans:], cur, right[:halo, :, chans:]], axis=0
            )
            cur_base = 0
            lo, hi = 0, width
        if degree == 1 or (degree - 1) % PER_EXCHANGE == 0:
            lo, hi = REACH, width - REACH
        else:
            lo, hi = lo + REACH, hi - REACH
        applied = step(cur, lo, hi, cur_base)
        if degree == 1:
            nxt = applied
        else:
            nxt = 2.0 * applied - prev[lo - prev_base : hi - prev_base]
        encoding = encoding + series_coef[degree] * nxt[own.start - lo : own.stop - lo]
        prev, prev_base = cur, cur_base
        cur, cur_base = nxt, lo
    return encoding.reshape(count * BS, chans), {0: payload, 1: left, -1: right}


def attention_kernel(table_ref, q_ref, *refs):
    kv_refs = refs[:NKEY]
    out_ref = refs[NKEY]
    scale = 1.0 / HD**0.5
    lane = lax.broadcasted_iota(jnp.int32, (1, 2 * HD), 1)
    low = lane < HD
    for pair in range(HEADS // 2):
        cols = slice(pair * 2 * HD, (pair + 1) * 2 * HD)
        vcols = slice(D + pair * 2 * HD, D + (pair + 1) * 2 * HD)
        qs = q_ref[:, cols]
        ks = jnp.concatenate([r[:, cols] for r in kv_refs], axis=0)
        vs = jnp.concatenate([r[:, vcols] for r in kv_refs], axis=0)
        merged = None
        for half in range(2):
            keep = low if half == 0 else jnp.logical_not(low)
            qm = jnp.where(keep, qs, jnp.zeros_like(qs))
            scores = lax.dot_general(
                qm, ks, (((1,), (1,)), ((), ())), preferred_element_type=jnp.float32
            ) * scale
            top = jnp.max(scores, axis=-1, keepdims=True)
            expd = jnp.exp(scores - top)
            total = jnp.sum(expd, axis=-1, keepdims=True)
            weights = (expd / total).astype(jnp.bfloat16)
            part = jnp.dot(weights, vs, preferred_element_type=jnp.float32)
            merged = part if half == 0 else jnp.where(low, merged, part)
        out_ref[:, cols] = merged.astype(jnp.bfloat16)


def attend(queries, kv_sources, table):
    count = table.shape[0]
    in_specs = [pl.BlockSpec((BS, D), lambda b, t: (b, 0))]
    operands = [queries]
    for j, src in enumerate(kv_sources):
        in_specs.append(pl.BlockSpec((BS, 2 * D), lambda b, t, j=j: (t[b, j], 0)))
        operands.append(src)
    grid_spec = pltpu.PrefetchScalarGridSpec(
        num_scalar_prefetch=1,
        grid=(count,),
        in_specs=in_specs,
        out_specs=pl.BlockSpec((BS, D), lambda b, t: (b, 0)),
    )
    return pl.pallas_call(
        attention_kernel,
        grid_spec=grid_spec,
        out_shape=jax.ShapeDtypeStruct((count * BS, D), jnp.bfloat16),
    )(table, *operands)


def on_device(
    node_feats,
    struct_feats,
    op_blocks,
    laplace_index,
    graph_links,
    expander_slot,
    series_coef,
    encode_weight,
    qkv_weight,
    out_weight,
):
    count = op_blocks.shape[0]
    rows = count * BS
    rim = REACH * BS
    first_block = lax.axis_index("seq") * count
    levels = lax.axis_size("seq").bit_length() - 1
    bits = [link * (levels - 1) // (NEXP - 1) for link in range(NEXP)]

    encoding, parts = chebyshev(struct_feats, op_blocks, laplace_index, series_coef, first_block)
    held = lax.optimization_barrier((node_feats, list(parts.values())))[0]
    feats_before = shift_rows(held[rows - rim:], "seq", 1)
    feats_after = shift_rows(held[:rim], "seq", -1)
    feats_far = [partner(held, "seq", bit) for bit in bits[1:]]
    encoding, feats_before, feats_after, feats_far = lax.optimization_barrier(
        (encoding, feats_before, feats_after, feats_far)
    )
    encoding_b = encoding.astype(jnp.bfloat16)

    enc_before = shift_rows(encoding_b[rows - rim:], "seq", 1)
    enc_after = shift_rows(encoding_b[:rim], "seq", -1)
    enc_far = [partner(encoding_b, "seq", bit) for bit in bits[1:]]

    def blend(feats, enc):
        encoded = jnp.dot(enc, encode_weight, preferred_element_type=jnp.float32)
        return (feats.astype(jnp.float32) + encoded).astype(jnp.bfloat16)

    kv_weight = qkv_weight[:, D:]
    blended = blend(node_feats, encoding_b)
    queries = jnp.dot(blended, qkv_weight[:, :D], preferred_element_type=jnp.float32).astype(
        jnp.bfloat16
    )
    near_blended = jnp.concatenate(
        [blend(feats_before, enc_before), blended, blend(feats_after, enc_after)], axis=0
    )
    kv_near = jnp.dot(near_blended, kv_weight, preferred_element_type=jnp.float32).astype(
        jnp.bfloat16
    )
    kv_own = kv_near[rim : rim + rows]
    kv_far = [partner(kv_own, "seq", bits[0])] + [
        jnp.dot(blend(f, e), kv_weight, preferred_element_type=jnp.float32).astype(jnp.bfloat16)
        for f, e in zip(feats_far, enc_far)
    ]

    near_blocks = count + 2 * REACH
    own_slot = jnp.arange(count, dtype=jnp.int32)[:, None] + REACH
    graph_slot = jnp.clip(graph_links - first_block + REACH, 0, near_blocks - 1)
    far_slot = jnp.clip(expander_slot, 0, count - 1)
    table = jnp.concatenate([own_slot, graph_slot, far_slot], axis=1).astype(jnp.int32)
    sources = [kv_near] * 4 + kv_far
    attended = attend(queries, sources, table)
    return jnp.dot(attended, out_weight, preferred_element_type=jnp.float32).astype(jnp.bfloat16)


def solution(mesh):
    placed = (
        P(("group", "seq"), None),
        P(("group", "seq"), None),
        P(("group", "seq"), None, None, None),
        P(("group", "seq"), None),
        P(("group", "seq"), None),
        P(("group", "seq"), None),
        P(),
        P(),
        P(),
        P(),
    )
    return jax.shard_map(
        on_device, mesh=mesh, in_specs=placed, out_specs=P(("group", "seq"), None), check_vma=False
    )
```

```python
import functools

import jax
import jax.numpy as jnp
from jax import lax
from jax.experimental import pallas as pl
from jax.experimental.pallas import tpu as pltpu
from jax.sharding import PartitionSpec as P

D = 1024
HEADS = 16
HD = 64
BS = 64
DEG = 8
NEXP = 4
REACH = 2
NKEY = 1 + 3 + NEXP
PER_EXCHANGE = 4


def shift_rows(x, axis, step):
    peers = lax.axis_size(axis)
    if step > 0:
        pairs = [(i, i + step) for i in range(peers - step)]
    else:
        pairs = [(i, i + step) for i in range(-step, peers)]
    return lax.ppermute(x, axis, pairs)


def extended(x, axis, width):
    length = x.shape[0]
    before = shift_rows(x[length - width:], axis, 1)
    after = shift_rows(x[:width], axis, -1)
    return jnp.concatenate([before, x, after], axis=0)


def partner(value, axis, distance):
    mask = 2**distance
    pairs = [(source, source ^ mask) for source in range(lax.axis_size(axis))]
    return lax.ppermute(value, axis, pairs)


def apply_operator(field, op_blocks, laplace_index, first_block):
    count = op_blocks.shape[0]
    padded = extended(field, "seq", REACH * BS)
    pooled = padded.reshape(count + 2 * REACH, BS, field.shape[1])
    position = laplace_index - first_block + REACH
    picked = pooled[position]
    result = jnp.einsum("bjst,bjtc->bsc", op_blocks, picked, precision=lax.Precision.HIGHEST)
    return result.reshape(field.shape)


def chebyshev(struct_feats, op_blocks, laplace_index, series_coef, first_block):
    count = op_blocks.shape[0]
    chans = struct_feats.shape[1]
    taps = 2 * REACH + 1
    halo = PER_EXCHANGE * REACH
    block_ids = first_block + jnp.arange(count, dtype=jnp.int32)
    offsets = laplace_index - block_ids[:, None] + REACH
    hit = offsets[:, :, None] == jnp.arange(taps, dtype=jnp.int32)[None, None, :]
    bands = jnp.sum(jnp.where(hit[:, :, :, None, None], op_blocks[:, :, None], 0.0), axis=1)
    bands = bands.transpose(0, 2, 1, 3).reshape(count, BS, taps * BS)
    own_field = struct_feats.reshape(count, BS, chans)
    payload = jnp.concatenate([own_field, bands], axis=2)
    left = shift_rows(payload, "seq", 1)
    right = shift_rows(payload, "seq", -1)
    edge = halo - REACH
    bands = jnp.concatenate(
        [left[count - edge :, :, chans:], bands, right[:edge, :, chans:]], axis=0
    )
    field = jnp.concatenate(
        [left[count - halo :, :, :chans], own_field, right[:halo, :, :chans]], axis=0
    )
    width = field.shape[0]

    def step(values, lo, hi, base):
        stacked = jnp.stack(
            [values[lo - REACH + o - base : hi - REACH + o - base] for o in range(taps)], axis=1
        ).reshape(hi - lo, taps * BS, chans)
        return jnp.einsum(
            "wsk,wkc->wsc", bands[lo - REACH : hi - REACH], stacked,
            precision=lax.Precision.HIGH, preferred_element_type=jnp.float32,
        )

    own = slice(halo, halo + count)
    cur, cur_base = field, 0
    prev, prev_base = None, 0
    encoding = series_coef[0] * field[own]
    for degree in range(1, DEG + 1):
        if degree > 1 and (degree - 1) % PER_EXCHANGE == 0:
            packed = jnp.concatenate([prev[own.start - prev_base : own.stop - prev_base], cur], axis=2)
            left = shift_rows(packed, "seq", 1)
            right = shift_rows(packed, "seq", -1)
            older = prev[own.start - prev_base : own.stop - prev_base]
            prev = jnp.concatenate(
                [left[count - edge :, :, :chans], older, right[:edge, :, :chans]], axis=0
            )
            prev_base = REACH
            cur = jnp.concatenate(
                [left[count - halo :, :, chans:], cur, right[:halo, :, chans:]], axis=0
            )
            cur_base = 0
            lo, hi = 0, width
        if degree == 1 or (degree - 1) % PER_EXCHANGE == 0:
            lo, hi = REACH, width - REACH
        else:
            lo, hi = lo + REACH, hi - REACH
        applied = step(cur, lo, hi, cur_base)
        if degree == 1:
            nxt = applied
        else:
            nxt = 2.0 * applied - prev[lo - prev_base : hi - prev_base]
        encoding = encoding + series_coef[degree] * nxt[own.start - lo : own.stop - lo]
        prev, prev_base = cur, cur_base
        cur, cur_base = nxt, lo
    return encoding.reshape(count * BS, chans), {0: payload, 1: left, -1: right}


def attention_kernel(table_ref, q_ref, *refs):
    kv_refs = refs[:NKEY]
    out_ref = refs[NKEY]
    lane = lax.broadcasted_iota(jnp.int32, (1, 2 * HD), 1)
    low = lane < HD
    for pair in range(HEADS // 2):
        cols = slice(pair * 2 * HD, (pair + 1) * 2 * HD)
        vcols = slice(D + pair * 2 * HD, D + (pair + 1) * 2 * HD)
        ks = jnp.concatenate([r[:, cols] for r in kv_refs], axis=0)
        vs = jnp.concatenate([r[:, vcols] for r in kv_refs], axis=0)
        scores = jnp.dot(ks, q_ref[0, pair], preferred_element_type=jnp.float32)
        top = jnp.max(scores, axis=0, keepdims=True)
        expd = jnp.exp(scores - top)
        total = jnp.sum(expd, axis=0, keepdims=True)
        weights = (expd * (1.0 / total)).astype(jnp.bfloat16)
        both = lax.dot_general(
            weights, vs, (((0,), (0,)), ((), ())), preferred_element_type=jnp.float32
        )
        merged = jnp.where(low, both[:BS], both[BS:])
        out_ref[:, cols] = merged.astype(jnp.bfloat16)


def split_queries(queries):
    count = queries.shape[0] // BS
    pairs = HEADS // 2
    qt = queries.reshape(count, BS, pairs, 2 * HD).transpose(0, 2, 3, 1)
    qt = jnp.concatenate([qt, qt], axis=3)
    d_head = lax.broadcasted_iota(jnp.int32, (2 * HD, 2 * BS), 0) // HD
    j_head = lax.broadcasted_iota(jnp.int32, (2 * HD, 2 * BS), 1) // BS
    scale = jnp.asarray(1.0 / HD**0.5, jnp.bfloat16)
    return jnp.where(d_head == j_head, qt * scale, jnp.zeros_like(qt))


def attend(queries, kv_sources, table):
    count = table.shape[0]
    pairs = HEADS // 2
    in_specs = [pl.BlockSpec((1, pairs, 2 * HD, 2 * BS), lambda b, t: (b, 0, 0, 0))]
    operands = [split_queries(queries)]
    for j, src in enumerate(kv_sources):
        in_specs.append(pl.BlockSpec((BS, 2 * D), lambda b, t, j=j: (t[b, j], 0)))
        operands.append(src)
    grid_spec = pltpu.PrefetchScalarGridSpec(
        num_scalar_prefetch=1,
        grid=(count,),
        in_specs=in_specs,
        out_specs=pl.BlockSpec((BS, D), lambda b, t: (b, 0)),
    )
    return pl.pallas_call(
        attention_kernel,
        grid_spec=grid_spec,
        out_shape=jax.ShapeDtypeStruct((count * BS, D), jnp.bfloat16),
    )(table, *operands)


def on_device(
    node_feats,
    struct_feats,
    op_blocks,
    laplace_index,
    graph_links,
    expander_slot,
    series_coef,
    encode_weight,
    qkv_weight,
    out_weight,
):
    count = op_blocks.shape[0]
    rows = count * BS
    rim = REACH * BS
    first_block = lax.axis_index("seq") * count
    levels = lax.axis_size("seq").bit_length() - 1
    bits = [link * (levels - 1) // (NEXP - 1) for link in range(NEXP)]

    encoding, parts = chebyshev(struct_feats, op_blocks, laplace_index, series_coef, first_block)
    held = lax.optimization_barrier((node_feats, list(parts.values())))[0]
    feats_before = shift_rows(held[rows - rim:], "seq", 1)
    feats_after = shift_rows(held[:rim], "seq", -1)
    feats_far = [partner(held, "seq", bit) for bit in bits[1:]]
    encoding, feats_before, feats_after, feats_far = lax.optimization_barrier(
        (encoding, feats_before, feats_after, feats_far)
    )
    encoding_b = encoding.astype(jnp.bfloat16)

    enc_before = shift_rows(encoding_b[rows - rim:], "seq", 1)
    enc_after = shift_rows(encoding_b[:rim], "seq", -1)
    enc_far = [partner(encoding_b, "seq", bit) for bit in bits[1:]]

    def blend(feats, enc):
        encoded = jnp.dot(enc, encode_weight, preferred_element_type=jnp.float32)
        return (feats.astype(jnp.float32) + encoded).astype(jnp.bfloat16)

    kv_weight = qkv_weight[:, D:]
    blended = blend(node_feats, encoding_b)
    queries = jnp.dot(blended, qkv_weight[:, :D], preferred_element_type=jnp.float32).astype(
        jnp.bfloat16
    )
    near_blended = jnp.concatenate(
        [blend(feats_before, enc_before), blended, blend(feats_after, enc_after)], axis=0
    )
    kv_near = jnp.dot(near_blended, kv_weight, preferred_element_type=jnp.float32).astype(
        jnp.bfloat16
    )
    kv_own = kv_near[rim : rim + rows]
    kv_far = [partner(kv_own, "seq", bits[0])] + [
        jnp.dot(blend(f, e), kv_weight, preferred_element_type=jnp.float32).astype(jnp.bfloat16)
        for f, e in zip(feats_far, enc_far)
    ]

    near_blocks = count + 2 * REACH
    own_slot = jnp.arange(count, dtype=jnp.int32)[:, None] + REACH
    graph_slot = jnp.clip(graph_links - first_block + REACH, 0, near_blocks - 1)
    far_slot = jnp.clip(expander_slot, 0, count - 1)
    table = jnp.concatenate([own_slot, graph_slot, far_slot], axis=1).astype(jnp.int32)
    sources = [kv_near] * 4 + kv_far
    attended = attend(queries, sources, table)
    return jnp.dot(attended, out_weight, preferred_element_type=jnp.float32).astype(jnp.bfloat16)


def solution(mesh):
    placed = (
        P(("group", "seq"), None),
        P(("group", "seq"), None),
        P(("group", "seq"), None, None, None),
        P(("group", "seq"), None),
        P(("group", "seq"), None),
        P(("group", "seq"), None),
        P(),
        P(),
        P(),
        P(),
    )
    return jax.shard_map(
        on_device, mesh=mesh, in_specs=placed, out_specs=P(("group", "seq"), None), check_vma=False
    )
```

```python
import functools

import jax
import jax.numpy as jnp
from jax import lax
from jax.experimental import pallas as pl
from jax.experimental.pallas import tpu as pltpu
from jax.sharding import PartitionSpec as P

D = 1024
HEADS = 16
HD = 64
BS = 64
DEG = 8
NEXP = 4
REACH = 2
NKEY = 1 + 3 + NEXP
PER_EXCHANGE = 2


def shift_rows(x, axis, step):
    peers = lax.axis_size(axis)
    if step > 0:
        pairs = [(i, i + step) for i in range(peers - step)]
    else:
        pairs = [(i, i + step) for i in range(-step, peers)]
    return lax.ppermute(x, axis, pairs)


def extended(x, axis, width):
    length = x.shape[0]
    before = shift_rows(x[length - width:], axis, 1)
    after = shift_rows(x[:width], axis, -1)
    return jnp.concatenate([before, x, after], axis=0)


def partner(value, axis, distance):
    mask = 2**distance
    pairs = [(source, source ^ mask) for source in range(lax.axis_size(axis))]
    return lax.ppermute(value, axis, pairs)


def apply_operator(field, op_blocks, laplace_index, first_block):
    count = op_blocks.shape[0]
    padded = extended(field, "seq", REACH * BS)
    pooled = padded.reshape(count + 2 * REACH, BS, field.shape[1])
    position = laplace_index - first_block + REACH
    picked = pooled[position]
    result = jnp.einsum("bjst,bjtc->bsc", op_blocks, picked, precision=lax.Precision.HIGHEST)
    return result.reshape(field.shape)


def chebyshev(struct_feats, op_blocks, laplace_index, series_coef, first_block):
    count = op_blocks.shape[0]
    chans = struct_feats.shape[1]
    taps = 2 * REACH + 1
    halo = PER_EXCHANGE * REACH
    block_ids = first_block + jnp.arange(count, dtype=jnp.int32)
    offsets = laplace_index - block_ids[:, None] + REACH
    hit = offsets[:, :, None] == jnp.arange(taps, dtype=jnp.int32)[None, None, :]
    bands = jnp.sum(jnp.where(hit[:, :, :, None, None], op_blocks[:, :, None], 0.0), axis=1)
    bands = bands.transpose(0, 2, 1, 3).reshape(count, BS, taps * BS)
    own_field = struct_feats.reshape(count, BS, chans)
    payload = jnp.concatenate([own_field, bands], axis=2)
    left = shift_rows(payload[count - halo :], "seq", 1)
    right = shift_rows(payload[:halo], "seq", -1)
    edge = halo - REACH
    bands = jnp.concatenate(
        [left[halo - edge :, :, chans:], bands, right[:edge, :, chans:]], axis=0
    )
    field = jnp.concatenate([left[:, :, :chans], own_field, right[:, :, :chans]], axis=0)
    width = field.shape[0]

    def step(values, lo, hi, base):
        stacked = jnp.stack(
            [values[lo - REACH + o - base : hi - REACH + o - base] for o in range(taps)], axis=1
        ).reshape(hi - lo, taps * BS, chans)
        return jnp.einsum(
            "wsk,wkc->wsc", bands[lo - REACH : hi - REACH], stacked,
            precision=lax.Precision.HIGH, preferred_element_type=jnp.float32,
        )

    own = slice(halo, halo + count)
    cur, cur_base = field, 0
    prev, prev_base = None, 0
    encoding = series_coef[0] * field[own]
    for degree in range(1, DEG + 1):
        if degree > 1 and (degree - 1) % PER_EXCHANGE == 0:
            older = prev[own.start - prev_base : own.stop - prev_base]
            packed = jnp.concatenate([older, cur], axis=2)
            left = shift_rows(packed[count - halo :], "seq", 1)
            right = shift_rows(packed[:halo], "seq", -1)
            prev = jnp.concatenate(
                [left[halo - edge :, :, :chans], older, right[:edge, :, :chans]], axis=0
            )
            prev_base = REACH
            cur = jnp.concatenate([left[:, :, chans:], cur, right[:, :, chans:]], axis=0)
            cur_base = 0
            lo, hi = 0, width
        if degree == 1 or (degree - 1) % PER_EXCHANGE == 0:
            lo, hi = REACH, width - REACH
        else:
            lo, hi = lo + REACH, hi - REACH
        applied = step(cur, lo, hi, cur_base)
        if degree == 1:
            nxt = applied
        else:
            nxt = 2.0 * applied - prev[lo - prev_base : hi - prev_base]
        encoding = encoding + series_coef[degree] * nxt[own.start - lo : own.stop - lo]
        prev, prev_base = cur, cur_base
        cur, cur_base = nxt, lo
    return encoding.reshape(count * BS, chans), {0: payload, 1: left, -1: right}


def attention_kernel(table_ref, q_ref, *refs):
    kv_refs = refs[:NKEY]
    out_ref = refs[NKEY]
    lane = lax.broadcasted_iota(jnp.int32, (1, 2 * HD), 1)
    low = lane < HD
    for pair in range(HEADS // 2):
        cols = slice(pair * 2 * HD, (pair + 1) * 2 * HD)
        vcols = slice(D + pair * 2 * HD, D + (pair + 1) * 2 * HD)
        ks = jnp.concatenate([r[:, cols] for r in kv_refs], axis=0)
        vs = jnp.concatenate([r[:, vcols] for r in kv_refs], axis=0)
        scores = jnp.dot(ks, q_ref[0, pair], preferred_element_type=jnp.float32)
        top = jnp.max(scores, axis=0, keepdims=True)
        expd = jnp.exp(scores - top)
        total = jnp.sum(expd, axis=0, keepdims=True)
        weights = (expd * (1.0 / total)).astype(jnp.bfloat16)
        both = lax.dot_general(
            weights, vs, (((0,), (0,)), ((), ())), preferred_element_type=jnp.float32
        )
        merged = jnp.where(low, both[:BS], both[BS:])
        out_ref[:, cols] = merged.astype(jnp.bfloat16)


def split_queries(queries):
    count = queries.shape[0] // BS
    pairs = HEADS // 2
    qt = queries.reshape(count, BS, pairs, 2 * HD).transpose(0, 2, 3, 1)
    qt = jnp.concatenate([qt, qt], axis=3)
    d_head = lax.broadcasted_iota(jnp.int32, (2 * HD, 2 * BS), 0) // HD
    j_head = lax.broadcasted_iota(jnp.int32, (2 * HD, 2 * BS), 1) // BS
    scale = jnp.asarray(1.0 / HD**0.5, jnp.bfloat16)
    return jnp.where(d_head == j_head, qt * scale, jnp.zeros_like(qt))


def attend(queries, kv_sources, table):
    count = table.shape[0]
    pairs = HEADS // 2
    in_specs = [pl.BlockSpec((1, pairs, 2 * HD, 2 * BS), lambda b, t: (b, 0, 0, 0))]
    operands = [split_queries(queries)]
    for j, src in enumerate(kv_sources):
        in_specs.append(pl.BlockSpec((BS, 2 * D), lambda b, t, j=j: (t[b, j], 0)))
        operands.append(src)
    grid_spec = pltpu.PrefetchScalarGridSpec(
        num_scalar_prefetch=1,
        grid=(count,),
        in_specs=in_specs,
        out_specs=pl.BlockSpec((BS, D), lambda b, t: (b, 0)),
    )
    return pl.pallas_call(
        attention_kernel,
        grid_spec=grid_spec,
        out_shape=jax.ShapeDtypeStruct((count * BS, D), jnp.bfloat16),
    )(table, *operands)


def on_device(
    node_feats,
    struct_feats,
    op_blocks,
    laplace_index,
    graph_links,
    expander_slot,
    series_coef,
    encode_weight,
    qkv_weight,
    out_weight,
):
    count = op_blocks.shape[0]
    rows = count * BS
    rim = REACH * BS
    first_block = lax.axis_index("seq") * count
    levels = lax.axis_size("seq").bit_length() - 1
    bits = [link * (levels - 1) // (NEXP - 1) for link in range(NEXP)]

    encoding, parts = chebyshev(struct_feats, op_blocks, laplace_index, series_coef, first_block)
    held = node_feats
    feats_before = shift_rows(held[rows - rim:], "seq", 1)
    feats_after = shift_rows(held[:rim], "seq", -1)
    feats_far = [partner(held, "seq", bit) for bit in bits[1:]]
    encoding, feats_before, feats_after, feats_far = lax.optimization_barrier(
        (encoding, feats_before, feats_after, feats_far)
    )
    encoding_b = encoding.astype(jnp.bfloat16)

    enc_before = shift_rows(encoding_b[rows - rim:], "seq", 1)
    enc_after = shift_rows(encoding_b[:rim], "seq", -1)
    enc_far = [partner(encoding_b, "seq", bit) for bit in bits[1:]]

    def blend(feats, enc):
        encoded = jnp.dot(enc, encode_weight, preferred_element_type=jnp.float32)
        return (feats.astype(jnp.float32) + encoded).astype(jnp.bfloat16)

    kv_weight = qkv_weight[:, D:]
    blended = blend(node_feats, encoding_b)
    queries = jnp.dot(blended, qkv_weight[:, :D], preferred_element_type=jnp.float32).astype(
        jnp.bfloat16
    )
    near_blended = jnp.concatenate(
        [blend(feats_before, enc_before), blended, blend(feats_after, enc_after)], axis=0
    )
    kv_near = jnp.dot(near_blended, kv_weight, preferred_element_type=jnp.float32).astype(
        jnp.bfloat16
    )
    kv_own = kv_near[rim : rim + rows]
    kv_far = [partner(kv_own, "seq", bits[0])] + [
        jnp.dot(blend(f, e), kv_weight, preferred_element_type=jnp.float32).astype(jnp.bfloat16)
        for f, e in zip(feats_far, enc_far)
    ]

    near_blocks = count + 2 * REACH
    own_slot = jnp.arange(count, dtype=jnp.int32)[:, None] + REACH
    graph_slot = jnp.clip(graph_links - first_block + REACH, 0, near_blocks - 1)
    far_slot = jnp.clip(expander_slot, 0, count - 1)
    table = jnp.concatenate([own_slot, graph_slot, far_slot], axis=1).astype(jnp.int32)
    sources = [kv_near] * 4 + kv_far
    attended = attend(queries, sources, table)
    return jnp.dot(attended, out_weight, preferred_element_type=jnp.float32).astype(jnp.bfloat16)


def solution(mesh):
    placed = (
        P(("group", "seq"), None),
        P(("group", "seq"), None),
        P(("group", "seq"), None, None, None),
        P(("group", "seq"), None),
        P(("group", "seq"), None),
        P(("group", "seq"), None),
        P(),
        P(),
        P(),
        P(),
    )
    return jax.shard_map(
        on_device, mesh=mesh, in_specs=placed, out_specs=P(("group", "seq"), None), check_vma=False
    )
```

```python
import functools

import jax
import jax.numpy as jnp
from jax import lax
from jax.experimental import pallas as pl
from jax.experimental.pallas import tpu as pltpu
from jax.sharding import PartitionSpec as P

D = 1024
HEADS = 16
HD = 64
BS = 64
DEG = 8
NEXP = 4
REACH = 2
NKEY = 1 + 3 + NEXP
PER_EXCHANGE = 4


def shift_rows(x, axis, step):
    peers = lax.axis_size(axis)
    if step > 0:
        pairs = [(i, i + step) for i in range(peers - step)]
    else:
        pairs = [(i, i + step) for i in range(-step, peers)]
    return lax.ppermute(x, axis, pairs)


def extended(x, axis, width):
    length = x.shape[0]
    before = shift_rows(x[length - width:], axis, 1)
    after = shift_rows(x[:width], axis, -1)
    return jnp.concatenate([before, x, after], axis=0)


def partner(value, axis, distance):
    mask = 2**distance
    pairs = [(source, source ^ mask) for source in range(lax.axis_size(axis))]
    return lax.ppermute(value, axis, pairs)


def apply_operator(field, op_blocks, laplace_index, first_block):
    count = op_blocks.shape[0]
    padded = extended(field, "seq", REACH * BS)
    pooled = padded.reshape(count + 2 * REACH, BS, field.shape[1])
    position = laplace_index - first_block + REACH
    picked = pooled[position]
    result = jnp.einsum("bjst,bjtc->bsc", op_blocks, picked, precision=lax.Precision.HIGHEST)
    return result.reshape(field.shape)


def chebyshev(struct_feats, op_blocks, laplace_index, series_coef, first_block, riders):
    count = op_blocks.shape[0]
    chans = struct_feats.shape[1]
    taps = 2 * REACH + 1
    halo = PER_EXCHANGE * REACH
    block_ids = first_block + jnp.arange(count, dtype=jnp.int32)
    offsets = laplace_index - block_ids[:, None] + REACH
    hit = offsets[:, :, None] == jnp.arange(taps, dtype=jnp.int32)[None, None, :]
    bands = jnp.sum(jnp.where(hit[:, :, :, None, None], op_blocks[:, :, None], 0.0), axis=1)
    bands = bands.transpose(0, 2, 1, 3).reshape(count, BS, taps * BS)
    own_field = struct_feats.reshape(count, BS, chans)
    payload = jnp.concatenate([own_field, bands], axis=2)
    left = shift_rows(payload[count - halo :], "seq", 1)
    right = shift_rows(payload[:halo], "seq", -1)
    left, right, riders = lax.optimization_barrier((left, right, riders))
    edge = halo - REACH
    bands = jnp.concatenate(
        [left[halo - edge :, :, chans:], bands, right[:edge, :, chans:]], axis=0
    )
    field = jnp.concatenate([left[:, :, :chans], own_field, right[:, :, :chans]], axis=0)
    width = field.shape[0]

    def step(values, lo, hi, base):
        stacked = jnp.stack(
            [values[lo - REACH + o - base : hi - REACH + o - base] for o in range(taps)], axis=1
        ).reshape(hi - lo, taps * BS, chans)
        return jnp.einsum(
            "wsk,wkc->wsc", bands[lo - REACH : hi - REACH], stacked,
            precision=lax.Precision.HIGH, preferred_element_type=jnp.float32,
        )

    own = slice(halo, halo + count)
    cur, cur_base = field, 0
    prev, prev_base = None, 0
    encoding = series_coef[0] * field[own]
    for degree in range(1, DEG + 1):
        if degree > 1 and (degree - 1) % PER_EXCHANGE == 0:
            older = prev[own.start - prev_base : own.stop - prev_base]
            packed = jnp.concatenate([older, cur], axis=2)
            left = shift_rows(packed[count - halo :], "seq", 1)
            right = shift_rows(packed[:halo], "seq", -1)
            prev = jnp.concatenate(
                [left[halo - edge :, :, :chans], older, right[:edge, :, :chans]], axis=0
            )
            prev_base = REACH
            cur = jnp.concatenate([left[:, :, chans:], cur, right[:, :, chans:]], axis=0)
            cur_base = 0
            lo, hi = 0, width
        if degree == 1 or (degree - 1) % PER_EXCHANGE == 0:
            lo, hi = REACH, width - REACH
        else:
            lo, hi = lo + REACH, hi - REACH
        applied = step(cur, lo, hi, cur_base)
        if degree == 1:
            nxt = applied
        else:
            nxt = 2.0 * applied - prev[lo - prev_base : hi - prev_base]
        encoding = encoding + series_coef[degree] * nxt[own.start - lo : own.stop - lo]
        prev, prev_base = cur, cur_base
        cur, cur_base = nxt, lo
    return encoding.reshape(count * BS, chans), riders


def attention_kernel(table_ref, q_ref, *refs):
    kv_refs = refs[:NKEY]
    out_ref = refs[NKEY]
    lane = lax.broadcasted_iota(jnp.int32, (1, 2 * HD), 1)
    low = lane < HD
    for pair in range(HEADS // 2):
        cols = slice(pair * 2 * HD, (pair + 1) * 2 * HD)
        vcols = slice(D + pair * 2 * HD, D + (pair + 1) * 2 * HD)
        ks = jnp.concatenate([r[:, cols] for r in kv_refs], axis=0)
        vs = jnp.concatenate([r[:, vcols] for r in kv_refs], axis=0)
        scores = jnp.dot(ks, q_ref[0, pair], preferred_element_type=jnp.float32)
        top = jnp.max(scores, axis=0, keepdims=True)
        expd = jnp.exp(scores - top)
        total = jnp.sum(expd, axis=0, keepdims=True)
        weights = (expd * (1.0 / total)).astype(jnp.bfloat16)
        both = lax.dot_general(
            weights, vs, (((0,), (0,)), ((), ())), preferred_element_type=jnp.float32
        )
        merged = jnp.where(low, both[:BS], both[BS:])
        out_ref[:, cols] = merged.astype(jnp.bfloat16)


def split_queries(queries):
    count = queries.shape[0] // BS
    pairs = HEADS // 2
    qt = queries.reshape(count, BS, pairs, 2 * HD).transpose(0, 2, 3, 1)
    qt = jnp.concatenate([qt, qt], axis=3)
    d_head = lax.broadcasted_iota(jnp.int32, (2 * HD, 2 * BS), 0) // HD
    j_head = lax.broadcasted_iota(jnp.int32, (2 * HD, 2 * BS), 1) // BS
    scale = jnp.asarray(1.0 / HD**0.5, jnp.bfloat16)
    return jnp.where(d_head == j_head, qt * scale, jnp.zeros_like(qt))


def attend(queries, kv_sources, table):
    count = table.shape[0]
    pairs = HEADS // 2
    in_specs = [pl.BlockSpec((1, pairs, 2 * HD, 2 * BS), lambda b, t: (b, 0, 0, 0))]
    operands = [split_queries(queries)]
    for j, src in enumerate(kv_sources):
        in_specs.append(pl.BlockSpec((BS, 2 * D), lambda b, t, j=j: (t[b, j], 0)))
        operands.append(src)
    grid_spec = pltpu.PrefetchScalarGridSpec(
        num_scalar_prefetch=1,
        grid=(count,),
        in_specs=in_specs,
        out_specs=pl.BlockSpec((BS, D), lambda b, t: (b, 0)),
    )
    return pl.pallas_call(
        attention_kernel,
        grid_spec=grid_spec,
        out_shape=jax.ShapeDtypeStruct((count * BS, D), jnp.bfloat16),
    )(table, *operands)


def on_device(
    node_feats,
    struct_feats,
    op_blocks,
    laplace_index,
    graph_links,
    expander_slot,
    series_coef,
    encode_weight,
    qkv_weight,
    out_weight,
):
    count = op_blocks.shape[0]
    rows = count * BS
    rim = REACH * BS
    first_block = lax.axis_index("seq") * count
    levels = lax.axis_size("seq").bit_length() - 1
    bits = [link * (levels - 1) // (NEXP - 1) for link in range(NEXP)]

    feats_before = shift_rows(node_feats[rows - rim:], "seq", 1)
    feats_after = shift_rows(node_feats[:rim], "seq", -1)
    encoding, (feats_before, feats_after, held) = chebyshev(
        struct_feats, op_blocks, laplace_index, series_coef, first_block,
        (feats_before, feats_after, node_feats),
    )
    feats_far = [partner(held, "seq", bit) for bit in bits[1:]]
    encoding, feats_far = lax.optimization_barrier((encoding, feats_far))
    encoding_b = encoding.astype(jnp.bfloat16)

    enc_before = shift_rows(encoding_b[rows - rim:], "seq", 1)
    enc_after = shift_rows(encoding_b[:rim], "seq", -1)
    enc_far = [partner(encoding_b, "seq", bit) for bit in bits[1:]]

    def blend(feats, enc):
        encoded = jnp.dot(enc, encode_weight, preferred_element_type=jnp.float32)
        return (feats.astype(jnp.float32) + encoded).astype(jnp.bfloat16)

    kv_weight = qkv_weight[:, D:]
    blended = blend(node_feats, encoding_b)
    queries = jnp.dot(blended, qkv_weight[:, :D], preferred_element_type=jnp.float32).astype(
        jnp.bfloat16
    )
    all_blended = jnp.concatenate(
        [blend(feats_before, enc_before), blended, blend(feats_after, enc_after)]
        + [blend(f, e) for f, e in zip(feats_far, enc_far)],
        axis=0,
    )
    kv_all = jnp.dot(all_blended, kv_weight, preferred_element_type=jnp.float32).astype(
        jnp.bfloat16
    )
    kv_own = kv_all[rim : rim + rows]
    kv_chip = partner(kv_own, "seq", bits[0])

    near_blocks = count + 2 * REACH
    own_slot = jnp.arange(count, dtype=jnp.int32)[:, None] + REACH
    graph_slot = jnp.clip(graph_links - first_block + REACH, 0, near_blocks - 1)
    far_slot = jnp.clip(expander_slot, 0, count - 1)
    far_base = jnp.asarray([0] + [near_blocks + k * count for k in range(NEXP - 1)], jnp.int32)
    table = jnp.concatenate([own_slot, graph_slot, far_slot + far_base[None, :]], axis=1)
    table = table.astype(jnp.int32)
    sources = [kv_all] * 4 + [kv_chip] + [kv_all] * (NEXP - 1)
    attended = attend(queries, sources, table)
    return jnp.dot(attended, out_weight, preferred_element_type=jnp.float32).astype(jnp.bfloat16)


def solution(mesh):
    placed = (
        P(("group", "seq"), None),
        P(("group", "seq"), None),
        P(("group", "seq"), None, None, None),
        P(("group", "seq"), None),
        P(("group", "seq"), None),
        P(("group", "seq"), None),
        P(),
        P(),
        P(),
        P(),
    )
    return jax.shard_map(
        on_device, mesh=mesh, in_specs=placed, out_specs=P(("group", "seq"), None), check_vma=False
    )
```

```python
import functools

import jax
import jax.numpy as jnp
from jax import lax
from jax.experimental import pallas as pl
from jax.experimental.pallas import tpu as pltpu
from jax.sharding import PartitionSpec as P

D = 1024
HEADS = 16
HD = 64
BS = 64
DEG = 8
NEXP = 4
REACH = 2
NKEY = 1 + 3 + NEXP
PER_EXCHANGE = 4


def shift_rows(x, axis, step):
    peers = lax.axis_size(axis)
    if step > 0:
        pairs = [(i, i + step) for i in range(peers - step)]
    else:
        pairs = [(i, i + step) for i in range(-step, peers)]
    return lax.ppermute(x, axis, pairs)


def extended(x, axis, width):
    length = x.shape[0]
    before = shift_rows(x[length - width:], axis, 1)
    after = shift_rows(x[:width], axis, -1)
    return jnp.concatenate([before, x, after], axis=0)


def partner(value, axis, distance):
    mask = 2**distance
    pairs = [(source, source ^ mask) for source in range(lax.axis_size(axis))]
    return lax.ppermute(value, axis, pairs)


def apply_operator(field, op_blocks, laplace_index, first_block):
    count = op_blocks.shape[0]
    padded = extended(field, "seq", REACH * BS)
    pooled = padded.reshape(count + 2 * REACH, BS, field.shape[1])
    position = laplace_index - first_block + REACH
    picked = pooled[position]
    result = jnp.einsum("bjst,bjtc->bsc", op_blocks, picked, precision=lax.Precision.HIGHEST)
    return result.reshape(field.shape)


def chebyshev(struct_feats, op_blocks, laplace_index, series_coef, first_block, riders, later):
    count = op_blocks.shape[0]
    chans = struct_feats.shape[1]
    taps = 2 * REACH + 1
    halo = PER_EXCHANGE * REACH
    block_ids = first_block + jnp.arange(count, dtype=jnp.int32)
    offsets = laplace_index - block_ids[:, None] + REACH
    hit = offsets[:, :, None] == jnp.arange(taps, dtype=jnp.int32)[None, None, :]
    bands = jnp.sum(jnp.where(hit[:, :, :, None, None], op_blocks[:, :, None], 0.0), axis=1)
    bands = bands.transpose(0, 2, 1, 3).reshape(count, BS, taps * BS)
    own_field = struct_feats.reshape(count, BS, chans)
    payload = jnp.concatenate([own_field, bands], axis=2)
    left = shift_rows(payload[count - halo :], "seq", 1)
    right = shift_rows(payload[:halo], "seq", -1)
    left, right, riders = lax.optimization_barrier((left, right, riders))
    edge = halo - REACH
    bands = jnp.concatenate(
        [left[halo - edge :, :, chans:], bands, right[:edge, :, chans:]], axis=0
    )
    field = jnp.concatenate([left[:, :, :chans], own_field, right[:, :, :chans]], axis=0)
    width = field.shape[0]

    def step(values, lo, hi, base):
        stacked = jnp.stack(
            [values[lo - REACH + o - base : hi - REACH + o - base] for o in range(taps)], axis=1
        ).reshape(hi - lo, taps * BS, chans)
        return jnp.einsum(
            "wsk,wkc->wsc", bands[lo - REACH : hi - REACH], stacked,
            precision=lax.Precision.HIGH, preferred_element_type=jnp.float32,
        )

    own = slice(halo, halo + count)
    cur, cur_base = field, 0
    prev, prev_base = None, 0
    encoding = series_coef[0] * field[own]
    for degree in range(1, DEG + 1):
        if degree > 1 and (degree - 1) % PER_EXCHANGE == 0:
            older = prev[own.start - prev_base : own.stop - prev_base]
            packed = jnp.concatenate([older, cur], axis=2)
            left = shift_rows(packed[count - halo :], "seq", 1)
            right = shift_rows(packed[:halo], "seq", -1)
            if later is not None:
                left, right, later = lax.optimization_barrier((left, right, later))
                riders = riders + (later,)
                later = None
            prev = jnp.concatenate(
                [left[halo - edge :, :, :chans], older, right[:edge, :, :chans]], axis=0
            )
            prev_base = REACH
            cur = jnp.concatenate([left[:, :, chans:], cur, right[:, :, chans:]], axis=0)
            cur_base = 0
            lo, hi = 0, width
        if degree == 1 or (degree - 1) % PER_EXCHANGE == 0:
            lo, hi = REACH, width - REACH
        else:
            lo, hi = lo + REACH, hi - REACH
        applied = step(cur, lo, hi, cur_base)
        if degree == 1:
            nxt = applied
        else:
            nxt = 2.0 * applied - prev[lo - prev_base : hi - prev_base]
        encoding = encoding + series_coef[degree] * nxt[own.start - lo : own.stop - lo]
        prev, prev_base = cur, cur_base
        cur, cur_base = nxt, lo
    return encoding.reshape(count * BS, chans), riders


def attention_kernel(table_ref, q_ref, *refs):
    kv_refs = refs[:NKEY]
    out_ref = refs[NKEY]
    lane = lax.broadcasted_iota(jnp.int32, (1, 2 * HD), 1)
    low = lane < HD
    for pair in range(HEADS // 2):
        cols = slice(pair * 2 * HD, (pair + 1) * 2 * HD)
        vcols = slice(D + pair * 2 * HD, D + (pair + 1) * 2 * HD)
        ks = jnp.concatenate([r[:, cols] for r in kv_refs], axis=0)
        vs = jnp.concatenate([r[:, vcols] for r in kv_refs], axis=0)
        scores = jnp.dot(ks, q_ref[0, pair], preferred_element_type=jnp.float32)
        top = jnp.max(scores, axis=0, keepdims=True)
        expd = jnp.exp(scores - top)
        total = jnp.sum(expd, axis=0, keepdims=True)
        weights = (expd * (1.0 / total)).astype(jnp.bfloat16)
        both = lax.dot_general(
            weights, vs, (((0,), (0,)), ((), ())), preferred_element_type=jnp.float32
        )
        merged = jnp.where(low, both[:BS], both[BS:])
        out_ref[:, cols] = merged.astype(jnp.bfloat16)


def split_queries(queries):
    count = queries.shape[0] // BS
    pairs = HEADS // 2
    qt = queries.reshape(count, BS, pairs, 2 * HD).transpose(0, 2, 3, 1)
    qt = jnp.concatenate([qt, qt], axis=3)
    d_head = lax.broadcasted_iota(jnp.int32, (2 * HD, 2 * BS), 0) // HD
    j_head = lax.broadcasted_iota(jnp.int32, (2 * HD, 2 * BS), 1) // BS
    scale = jnp.asarray(1.0 / HD**0.5, jnp.bfloat16)
    return jnp.where(d_head == j_head, qt * scale, jnp.zeros_like(qt))


def attend(queries, kv_sources, table):
    count = table.shape[0]
    pairs = HEADS // 2
    in_specs = [pl.BlockSpec((1, pairs, 2 * HD, 2 * BS), lambda b, t: (b, 0, 0, 0))]
    operands = [split_queries(queries)]
    for j, src in enumerate(kv_sources):
        in_specs.append(pl.BlockSpec((BS, 2 * D), lambda b, t, j=j: (t[b, j], 0)))
        operands.append(src)
    grid_spec = pltpu.PrefetchScalarGridSpec(
        num_scalar_prefetch=1,
        grid=(count,),
        in_specs=in_specs,
        out_specs=pl.BlockSpec((BS, D), lambda b, t: (b, 0)),
    )
    return pl.pallas_call(
        attention_kernel,
        grid_spec=grid_spec,
        out_shape=jax.ShapeDtypeStruct((count * BS, D), jnp.bfloat16),
    )(table, *operands)


def on_device(
    node_feats,
    struct_feats,
    op_blocks,
    laplace_index,
    graph_links,
    expander_slot,
    series_coef,
    encode_weight,
    qkv_weight,
    out_weight,
):
    count = op_blocks.shape[0]
    rows = count * BS
    rim = REACH * BS
    first_block = lax.axis_index("seq") * count
    levels = lax.axis_size("seq").bit_length() - 1
    bits = [link * (levels - 1) // (NEXP - 1) for link in range(NEXP)]

    feats_before = shift_rows(node_feats[rows - rim:], "seq", 1)
    feats_after = shift_rows(node_feats[:rim], "seq", -1)
    half = rows // 2
    early = [partner(node_feats[:half], "seq", bit) for bit in bits[1:]]
    encoding, (feats_before, feats_after, early) = chebyshev(
        struct_feats, op_blocks, laplace_index, series_coef, first_block,
        (feats_before, feats_after), early,
    )
    late = [partner(node_feats[half:], "seq", bit) for bit in bits[1:]]
    encoding, late = lax.optimization_barrier((encoding, late))
    feats_far = [jnp.concatenate([a, b], axis=0) for a, b in zip(early, late)]
    encoding_b = encoding.astype(jnp.bfloat16)

    enc_before = shift_rows(encoding_b[rows - rim:], "seq", 1)
    enc_after = shift_rows(encoding_b[:rim], "seq", -1)
    enc_far = [partner(encoding_b, "seq", bit) for bit in bits[1:]]

    def blend(feats, enc):
        encoded = jnp.dot(enc, encode_weight, preferred_element_type=jnp.float32)
        return (feats.astype(jnp.float32) + encoded).astype(jnp.bfloat16)

    kv_weight = qkv_weight[:, D:]
    blended = blend(node_feats, encoding_b)
    queries = jnp.dot(blended, qkv_weight[:, :D], preferred_element_type=jnp.float32).astype(
        jnp.bfloat16
    )
    all_blended = jnp.concatenate(
        [blend(feats_before, enc_before), blended, blend(feats_after, enc_after)]
        + [blend(f, e) for f, e in zip(feats_far, enc_far)],
        axis=0,
    )
    kv_all = jnp.dot(all_blended, kv_weight, preferred_element_type=jnp.float32).astype(
        jnp.bfloat16
    )
    kv_own = kv_all[rim : rim + rows]
    kv_chip = partner(kv_own, "seq", bits[0])

    near_blocks = count + 2 * REACH
    own_slot = jnp.arange(count, dtype=jnp.int32)[:, None] + REACH
    graph_slot = jnp.clip(graph_links - first_block + REACH, 0, near_blocks - 1)
    far_slot = jnp.clip(expander_slot, 0, count - 1)
    far_base = jnp.asarray([0] + [near_blocks + k * count for k in range(NEXP - 1)], jnp.int32)
    table = jnp.concatenate([own_slot, graph_slot, far_slot + far_base[None, :]], axis=1)
    table = table.astype(jnp.int32)
    sources = [kv_all] * 4 + [kv_chip] + [kv_all] * (NEXP - 1)
    attended = attend(queries, sources, table)
    return jnp.dot(attended, out_weight, preferred_element_type=jnp.float32).astype(jnp.bfloat16)


def solution(mesh):
    placed = (
        P(("group", "seq"), None),
        P(("group", "seq"), None),
        P(("group", "seq"), None, None, None),
        P(("group", "seq"), None),
        P(("group", "seq"), None),
        P(("group", "seq"), None),
        P(),
        P(),
        P(),
        P(),
    )
    return jax.shard_map(
        on_device, mesh=mesh, in_specs=placed, out_specs=P(("group", "seq"), None), check_vma=False
    )
```

```python
import functools

import jax
import jax.numpy as jnp
from jax import lax
from jax.experimental import pallas as pl
from jax.experimental.pallas import tpu as pltpu
from jax.sharding import PartitionSpec as P

D = 1024
HEADS = 16
HD = 64
BS = 64
DEG = 8
NEXP = 4
REACH = 2
NKEY = 1 + 3 + NEXP
PER_EXCHANGE = 4


def shift_rows(x, axis, step):
    peers = lax.axis_size(axis)
    if step > 0:
        pairs = [(i, i + step) for i in range(peers - step)]
    else:
        pairs = [(i, i + step) for i in range(-step, peers)]
    return lax.ppermute(x, axis, pairs)


def extended(x, axis, width):
    length = x.shape[0]
    before = shift_rows(x[length - width:], axis, 1)
    after = shift_rows(x[:width], axis, -1)
    return jnp.concatenate([before, x, after], axis=0)


def partner(value, axis, distance):
    mask = 2**distance
    pairs = [(source, source ^ mask) for source in range(lax.axis_size(axis))]
    return lax.ppermute(value, axis, pairs)


def apply_operator(field, op_blocks, laplace_index, first_block):
    count = op_blocks.shape[0]
    padded = extended(field, "seq", REACH * BS)
    pooled = padded.reshape(count + 2 * REACH, BS, field.shape[1])
    position = laplace_index - first_block + REACH
    picked = pooled[position]
    result = jnp.einsum("bjst,bjtc->bsc", op_blocks, picked, precision=lax.Precision.HIGHEST)
    return result.reshape(field.shape)


def chebyshev(struct_feats, op_blocks, laplace_index, series_coef, first_block, riders, later):
    count = op_blocks.shape[0]
    chans = struct_feats.shape[1]
    taps = 2 * REACH + 1
    halo = PER_EXCHANGE * REACH
    block_ids = first_block + jnp.arange(count, dtype=jnp.int32)
    offsets = laplace_index - block_ids[:, None] + REACH
    hit = offsets[:, :, None] == jnp.arange(taps, dtype=jnp.int32)[None, None, :]
    bands = jnp.sum(jnp.where(hit[:, :, :, None, None], op_blocks[:, :, None], 0.0), axis=1)
    bands = bands.transpose(0, 2, 1, 3).reshape(count, BS, taps * BS)
    own_field = struct_feats.reshape(count, BS, chans)
    payload = jnp.concatenate([own_field, bands], axis=2)
    left = shift_rows(payload[count - halo :], "seq", 1)
    right = shift_rows(payload[:halo], "seq", -1)
    edge = halo - REACH
    bands = jnp.concatenate(
        [left[halo - edge :, :, chans:], bands, right[:edge, :, chans:]], axis=0
    )
    field = jnp.concatenate([left[:, :, :chans], own_field, right[:, :, :chans]], axis=0)
    width = field.shape[0]

    def step(values, lo, hi, base):
        stacked = jnp.stack(
            [values[lo - REACH + o - base : hi - REACH + o - base] for o in range(taps)], axis=1
        ).reshape(hi - lo, taps * BS, chans)
        return jnp.einsum(
            "wsk,wkc->wsc", bands[lo - REACH : hi - REACH], stacked,
            precision=lax.Precision.HIGH, preferred_element_type=jnp.float32,
        )

    own = slice(halo, halo + count)
    cur, cur_base = field, 0
    prev, prev_base = None, 0
    encoding = series_coef[0] * field[own]
    for degree in range(1, DEG + 1):
        if degree > 1 and (degree - 1) % PER_EXCHANGE == 0:
            older = prev[own.start - prev_base : own.stop - prev_base]
            packed = jnp.concatenate([older, cur], axis=2)
            left = shift_rows(packed[count - halo :], "seq", 1)
            right = shift_rows(packed[:halo], "seq", -1)
            if later is not None:
                left, right, later = lax.optimization_barrier((left, right, later))
                riders = riders + (later,)
                later = None
            prev = jnp.concatenate(
                [left[halo - edge :, :, :chans], older, right[:edge, :, :chans]], axis=0
            )
            prev_base = REACH
            cur = jnp.concatenate([left[:, :, chans:], cur, right[:, :, chans:]], axis=0)
            cur_base = 0
            lo, hi = 0, width
        if degree == 1 or (degree - 1) % PER_EXCHANGE == 0:
            lo, hi = REACH, width - REACH
        else:
            lo, hi = lo + REACH, hi - REACH
        applied = step(cur, lo, hi, cur_base)
        if degree == 1:
            nxt = applied
        else:
            nxt = 2.0 * applied - prev[lo - prev_base : hi - prev_base]
        encoding = encoding + series_coef[degree] * nxt[own.start - lo : own.stop - lo]
        prev, prev_base = cur, cur_base
        cur, cur_base = nxt, lo
    return encoding.reshape(count * BS, chans), riders


def attention_kernel(table_ref, q_ref, *refs):
    kv_refs = refs[:NKEY]
    out_ref = refs[NKEY]
    lane = lax.broadcasted_iota(jnp.int32, (1, 2 * HD), 1)
    low = lane < HD
    for pair in range(HEADS // 2):
        cols = slice(pair * 2 * HD, (pair + 1) * 2 * HD)
        vcols = slice(D + pair * 2 * HD, D + (pair + 1) * 2 * HD)
        ks = jnp.concatenate([r[:, cols] for r in kv_refs], axis=0)
        vs = jnp.concatenate([r[:, vcols] for r in kv_refs], axis=0)
        scores = jnp.dot(ks, q_ref[0, pair], preferred_element_type=jnp.float32)
        top = jnp.max(scores, axis=0, keepdims=True)
        expd = jnp.exp(scores - top)
        total = jnp.sum(expd, axis=0, keepdims=True)
        weights = (expd * (1.0 / total)).astype(jnp.bfloat16)
        both = lax.dot_general(
            weights, vs, (((0,), (0,)), ((), ())), preferred_element_type=jnp.float32
        )
        merged = jnp.where(low, both[:BS], both[BS:])
        out_ref[:, cols] = merged.astype(jnp.bfloat16)


def split_queries(queries):
    count = queries.shape[0] // BS
    pairs = HEADS // 2
    qt = queries.reshape(count, BS, pairs, 2 * HD).transpose(0, 2, 3, 1)
    qt = jnp.concatenate([qt, qt], axis=3)
    d_head = lax.broadcasted_iota(jnp.int32, (2 * HD, 2 * BS), 0) // HD
    j_head = lax.broadcasted_iota(jnp.int32, (2 * HD, 2 * BS), 1) // BS
    scale = jnp.asarray(1.0 / HD**0.5, jnp.bfloat16)
    return jnp.where(d_head == j_head, qt * scale, jnp.zeros_like(qt))


def attend(queries, kv_sources, table):
    count = table.shape[0]
    pairs = HEADS // 2
    in_specs = [pl.BlockSpec((1, pairs, 2 * HD, 2 * BS), lambda b, t: (b, 0, 0, 0))]
    operands = [split_queries(queries)]
    for j, src in enumerate(kv_sources):
        in_specs.append(pl.BlockSpec((BS, 2 * D), lambda b, t, j=j: (t[b, j], 0)))
        operands.append(src)
    grid_spec = pltpu.PrefetchScalarGridSpec(
        num_scalar_prefetch=1,
        grid=(count,),
        in_specs=in_specs,
        out_specs=pl.BlockSpec((BS, D), lambda b, t: (b, 0)),
    )
    return pl.pallas_call(
        attention_kernel,
        grid_spec=grid_spec,
        out_shape=jax.ShapeDtypeStruct((count * BS, D), jnp.bfloat16),
    )(table, *operands)


def on_device(
    node_feats,
    struct_feats,
    op_blocks,
    laplace_index,
    graph_links,
    expander_slot,
    series_coef,
    encode_weight,
    qkv_weight,
    out_weight,
):
    count = op_blocks.shape[0]
    rows = count * BS
    rim = REACH * BS
    first_block = lax.axis_index("seq") * count
    levels = lax.axis_size("seq").bit_length() - 1
    bits = [link * (levels - 1) // (NEXP - 1) for link in range(NEXP)]

    half = rows // 2
    early = [partner(node_feats[:half], "seq", bit) for bit in bits[1:]]
    encoding, (early,) = chebyshev(
        struct_feats, op_blocks, laplace_index, series_coef, first_block, (), early,
    )
    late = [partner(node_feats[half:], "seq", bit) for bit in bits[1:]]
    feats_before = shift_rows(node_feats[rows - rim:], "seq", 1)
    feats_after = shift_rows(node_feats[:rim], "seq", -1)
    encoding, late, feats_before, feats_after = lax.optimization_barrier(
        (encoding, late, feats_before, feats_after)
    )
    feats_far = [jnp.concatenate([a, b], axis=0) for a, b in zip(early, late)]
    encoding_b = encoding.astype(jnp.bfloat16)

    enc_before = shift_rows(encoding_b[rows - rim:], "seq", 1)
    enc_after = shift_rows(encoding_b[:rim], "seq", -1)
    enc_far = [partner(encoding_b, "seq", bit) for bit in bits[1:]]

    def blend(feats, enc):
        encoded = jnp.dot(enc, encode_weight, preferred_element_type=jnp.float32)
        return (feats.astype(jnp.float32) + encoded).astype(jnp.bfloat16)

    kv_weight = qkv_weight[:, D:]
    blended = blend(node_feats, encoding_b)
    queries = jnp.dot(blended, qkv_weight[:, :D], preferred_element_type=jnp.float32).astype(
        jnp.bfloat16
    )
    all_blended = jnp.concatenate(
        [blend(feats_before, enc_before), blended, blend(feats_after, enc_after)]
        + [blend(f, e) for f, e in zip(feats_far, enc_far)],
        axis=0,
    )
    kv_all = jnp.dot(all_blended, kv_weight, preferred_element_type=jnp.float32).astype(
        jnp.bfloat16
    )
    kv_own = kv_all[rim : rim + rows]
    kv_chip = partner(kv_own, "seq", bits[0])

    near_blocks = count + 2 * REACH
    own_slot = jnp.arange(count, dtype=jnp.int32)[:, None] + REACH
    graph_slot = jnp.clip(graph_links - first_block + REACH, 0, near_blocks - 1)
    far_slot = jnp.clip(expander_slot, 0, count - 1)
    far_base = jnp.asarray([0] + [near_blocks + k * count for k in range(NEXP - 1)], jnp.int32)
    table = jnp.concatenate([own_slot, graph_slot, far_slot + far_base[None, :]], axis=1)
    table = table.astype(jnp.int32)
    sources = [kv_all] * 4 + [kv_chip] + [kv_all] * (NEXP - 1)
    attended = attend(queries, sources, table)
    return jnp.dot(attended, out_weight, preferred_element_type=jnp.float32).astype(jnp.bfloat16)


def solution(mesh):
    placed = (
        P(("group", "seq"), None),
        P(("group", "seq"), None),
        P(("group", "seq"), None, None, None),
        P(("group", "seq"), None),
        P(("group", "seq"), None),
        P(("group", "seq"), None),
        P(),
        P(),
        P(),
        P(),
    )
    return jax.shard_map(
        on_device, mesh=mesh, in_specs=placed, out_specs=P(("group", "seq"), None), check_vma=False
    )
```

```python
import functools

import jax
import jax.numpy as jnp
from jax import lax
from jax.experimental import pallas as pl
from jax.experimental.pallas import tpu as pltpu
from jax.sharding import PartitionSpec as P

D = 1024
HEADS = 16
HD = 64
BS = 64
DEG = 8
NEXP = 4
REACH = 2
NKEY = 1 + 3 + NEXP
PER_EXCHANGE = 4


def shift_rows(x, axis, step):
    peers = lax.axis_size(axis)
    if step > 0:
        pairs = [(i, i + step) for i in range(peers - step)]
    else:
        pairs = [(i, i + step) for i in range(-step, peers)]
    return lax.ppermute(x, axis, pairs)


def extended(x, axis, width):
    length = x.shape[0]
    before = shift_rows(x[length - width:], axis, 1)
    after = shift_rows(x[:width], axis, -1)
    return jnp.concatenate([before, x, after], axis=0)


def partner(value, axis, distance):
    mask = 2**distance
    pairs = [(source, source ^ mask) for source in range(lax.axis_size(axis))]
    return lax.ppermute(value, axis, pairs)


def apply_operator(field, op_blocks, laplace_index, first_block):
    count = op_blocks.shape[0]
    padded = extended(field, "seq", REACH * BS)
    pooled = padded.reshape(count + 2 * REACH, BS, field.shape[1])
    position = laplace_index - first_block + REACH
    picked = pooled[position]
    result = jnp.einsum("bjst,bjtc->bsc", op_blocks, picked, precision=lax.Precision.HIGHEST)
    return result.reshape(field.shape)


def chebyshev(struct_feats, op_blocks, laplace_index, series_coef, first_block, riders, later):
    count = op_blocks.shape[0]
    chans = struct_feats.shape[1]
    taps = 2 * REACH + 1
    halo = PER_EXCHANGE * REACH
    block_ids = first_block + jnp.arange(count, dtype=jnp.int32)
    offsets = laplace_index - block_ids[:, None] + REACH
    hit = offsets[:, :, None] == jnp.arange(taps, dtype=jnp.int32)[None, None, :]
    bands = jnp.sum(jnp.where(hit[:, :, :, None, None], op_blocks[:, :, None], 0.0), axis=1)
    bands = bands.transpose(0, 2, 1, 3).reshape(count, BS, taps * BS)
    own_field = struct_feats.reshape(count, BS, chans)
    payload = jnp.concatenate([own_field, bands], axis=2)
    left = shift_rows(payload[count - halo :], "seq", 1)
    right = shift_rows(payload[:halo], "seq", -1)
    edge = halo - REACH
    bands = jnp.concatenate(
        [left[halo - edge :, :, chans:], bands, right[:edge, :, chans:]], axis=0
    )
    field = jnp.concatenate([left[:, :, :chans], own_field, right[:, :, :chans]], axis=0)
    width = field.shape[0]

    def step(values, lo, hi, base):
        stacked = jnp.stack(
            [values[lo - REACH + o - base : hi - REACH + o - base] for o in range(taps)], axis=1
        ).reshape(hi - lo, taps * BS, chans)
        return jnp.einsum(
            "wsk,wkc->wsc", bands[lo - REACH : hi - REACH], stacked,
            precision=lax.Precision.HIGH, preferred_element_type=jnp.float32,
        )

    own = slice(halo, halo + count)
    cur, cur_base = field, 0
    prev, prev_base = None, 0
    encoding = series_coef[0] * field[own]
    for degree in range(1, DEG + 1):
        if degree > 1 and (degree - 1) % PER_EXCHANGE == 0:
            older = prev[own.start - prev_base : own.stop - prev_base]
            packed = jnp.concatenate([older, cur], axis=2)
            left = shift_rows(packed[count - halo :], "seq", 1)
            right = shift_rows(packed[:halo], "seq", -1)
            if later is not None:
                left, right, later = lax.optimization_barrier((left, right, later))
                riders = riders + (later,)
                later = None
            prev = jnp.concatenate(
                [left[halo - edge :, :, :chans], older, right[:edge, :, :chans]], axis=0
            )
            prev_base = REACH
            cur = jnp.concatenate([left[:, :, chans:], cur, right[:, :, chans:]], axis=0)
            cur_base = 0
            lo, hi = 0, width
        if degree == 1 or (degree - 1) % PER_EXCHANGE == 0:
            lo, hi = REACH, width - REACH
        else:
            lo, hi = lo + REACH, hi - REACH
        applied = step(cur, lo, hi, cur_base)
        if degree == 1:
            nxt = applied
        else:
            nxt = 2.0 * applied - prev[lo - prev_base : hi - prev_base]
        encoding = encoding + series_coef[degree] * nxt[own.start - lo : own.stop - lo]
        prev, prev_base = cur, cur_base
        cur, cur_base = nxt, lo
    return encoding.reshape(count * BS, chans), riders


def attention_kernel(table_ref, q_ref, *refs):
    kv_refs = refs[:NKEY]
    out_ref = refs[NKEY]
    lane = lax.broadcasted_iota(jnp.int32, (1, 2 * HD), 1)
    low = lane < HD
    row = lax.broadcasted_iota(jnp.int32, (BS, 2 * BS), 0)
    col = lax.broadcasted_iota(jnp.int32, (BS, 2 * BS), 1)
    spread = jnp.where(col % BS == row, 1.0 / HD**0.5, 0.0).astype(jnp.bfloat16)
    d_head = lax.broadcasted_iota(jnp.int32, (2 * HD, 2 * BS), 0) // HD
    j_head = lax.broadcasted_iota(jnp.int32, (2 * HD, 2 * BS), 1) // BS
    same = d_head == j_head
    for pair in range(HEADS // 2):
        cols = slice(pair * 2 * HD, (pair + 1) * 2 * HD)
        vcols = slice(D + pair * 2 * HD, D + (pair + 1) * 2 * HD)
        ks = jnp.concatenate([r[:, cols] for r in kv_refs], axis=0)
        vs = jnp.concatenate([r[:, vcols] for r in kv_refs], axis=0)
        spread_q = lax.dot_general(
            q_ref[:, cols], spread, (((0,), (0,)), ((), ())), preferred_element_type=jnp.float32
        )
        qbd = jnp.where(same, spread_q, 0.0).astype(jnp.bfloat16)
        scores = jnp.dot(ks, qbd, preferred_element_type=jnp.float32)
        top = jnp.max(scores, axis=0, keepdims=True)
        expd = jnp.exp(scores - top)
        total = jnp.sum(expd, axis=0, keepdims=True)
        weights = (expd * (1.0 / total)).astype(jnp.bfloat16)
        both = lax.dot_general(
            weights, vs, (((0,), (0,)), ((), ())), preferred_element_type=jnp.float32
        )
        merged = jnp.where(low, both[:BS], both[BS:])
        out_ref[:, cols] = merged.astype(jnp.bfloat16)


def attend(queries, kv_sources, table):
    count = table.shape[0]
    pairs = HEADS // 2
    in_specs = [pl.BlockSpec((BS, D), lambda b, t: (b, 0))]
    operands = [queries]
    for j, src in enumerate(kv_sources):
        in_specs.append(pl.BlockSpec((BS, 2 * D), lambda b, t, j=j: (t[b, j], 0)))
        operands.append(src)
    grid_spec = pltpu.PrefetchScalarGridSpec(
        num_scalar_prefetch=1,
        grid=(count,),
        in_specs=in_specs,
        out_specs=pl.BlockSpec((BS, D), lambda b, t: (b, 0)),
    )
    return pl.pallas_call(
        attention_kernel,
        grid_spec=grid_spec,
        out_shape=jax.ShapeDtypeStruct((count * BS, D), jnp.bfloat16),
    )(table, *operands)


def on_device(
    node_feats,
    struct_feats,
    op_blocks,
    laplace_index,
    graph_links,
    expander_slot,
    series_coef,
    encode_weight,
    qkv_weight,
    out_weight,
):
    count = op_blocks.shape[0]
    rows = count * BS
    rim = REACH * BS
    first_block = lax.axis_index("seq") * count
    levels = lax.axis_size("seq").bit_length() - 1
    bits = [link * (levels - 1) // (NEXP - 1) for link in range(NEXP)]

    half = rows // 2
    early = [partner(node_feats[:half], "seq", bit) for bit in bits[1:]]
    encoding, (early,) = chebyshev(
        struct_feats, op_blocks, laplace_index, series_coef, first_block, (), early,
    )
    late = [partner(node_feats[half:], "seq", bit) for bit in bits[1:]]
    feats_before = shift_rows(node_feats[rows - rim:], "seq", 1)
    feats_after = shift_rows(node_feats[:rim], "seq", -1)
    encoding, late, feats_before, feats_after = lax.optimization_barrier(
        (encoding, late, feats_before, feats_after)
    )
    feats_far = [jnp.concatenate([a, b], axis=0) for a, b in zip(early, late)]
    encoding_b = encoding.astype(jnp.bfloat16)

    enc_before = shift_rows(encoding_b[rows - rim:], "seq", 1)
    enc_after = shift_rows(encoding_b[:rim], "seq", -1)
    enc_far = [partner(encoding_b, "seq", bit) for bit in bits[1:]]

    def blend(feats, enc):
        encoded = jnp.dot(enc, encode_weight, preferred_element_type=jnp.float32)
        return (feats.astype(jnp.float32) + encoded).astype(jnp.bfloat16)

    kv_weight = qkv_weight[:, D:]
    blended = blend(node_feats, encoding_b)
    queries = jnp.dot(blended, qkv_weight[:, :D], preferred_element_type=jnp.float32).astype(
        jnp.bfloat16
    )
    all_blended = jnp.concatenate(
        [blend(feats_before, enc_before), blended, blend(feats_after, enc_after)]
        + [blend(f, e) for f, e in zip(feats_far, enc_far)],
        axis=0,
    )
    kv_all = jnp.dot(all_blended, kv_weight, preferred_element_type=jnp.float32).astype(
        jnp.bfloat16
    )
    kv_own = kv_all[rim : rim + rows]
    kv_chip = partner(kv_own, "seq", bits[0])

    near_blocks = count + 2 * REACH
    own_slot = jnp.arange(count, dtype=jnp.int32)[:, None] + REACH
    graph_slot = jnp.clip(graph_links - first_block + REACH, 0, near_blocks - 1)
    far_slot = jnp.clip(expander_slot, 0, count - 1)
    far_base = jnp.asarray([0] + [near_blocks + k * count for k in range(NEXP - 1)], jnp.int32)
    table = jnp.concatenate([own_slot, graph_slot, far_slot + far_base[None, :]], axis=1)
    table = table.astype(jnp.int32)
    sources = [kv_all] * 4 + [kv_chip] + [kv_all] * (NEXP - 1)
    attended = attend(queries, sources, table)
    return jnp.dot(attended, out_weight, preferred_element_type=jnp.float32).astype(jnp.bfloat16)


def solution(mesh):
    placed = (
        P(("group", "seq"), None),
        P(("group", "seq"), None),
        P(("group", "seq"), None, None, None),
        P(("group", "seq"), None),
        P(("group", "seq"), None),
        P(("group", "seq"), None),
        P(),
        P(),
        P(),
        P(),
    )
    return jax.shard_map(
        on_device, mesh=mesh, in_specs=placed, out_specs=P(("group", "seq"), None), check_vma=False
    )
```

```python
import functools

import jax
import jax.numpy as jnp
from jax import lax
from jax.experimental import pallas as pl
from jax.experimental.pallas import tpu as pltpu
from jax.sharding import PartitionSpec as P

D = 1024
HEADS = 16
HD = 64
BS = 64
DEG = 8
NEXP = 4
REACH = 2
NKEY = 1 + 3 + NEXP
PER_EXCHANGE = 4


def shift_rows(x, axis, step):
    peers = lax.axis_size(axis)
    if step > 0:
        pairs = [(i, i + step) for i in range(peers - step)]
    else:
        pairs = [(i, i + step) for i in range(-step, peers)]
    return lax.ppermute(x, axis, pairs)


def extended(x, axis, width):
    length = x.shape[0]
    before = shift_rows(x[length - width:], axis, 1)
    after = shift_rows(x[:width], axis, -1)
    return jnp.concatenate([before, x, after], axis=0)


def partner(value, axis, distance):
    mask = 2**distance
    pairs = [(source, source ^ mask) for source in range(lax.axis_size(axis))]
    return lax.ppermute(value, axis, pairs)


def apply_operator(field, op_blocks, laplace_index, first_block):
    count = op_blocks.shape[0]
    padded = extended(field, "seq", REACH * BS)
    pooled = padded.reshape(count + 2 * REACH, BS, field.shape[1])
    position = laplace_index - first_block + REACH
    picked = pooled[position]
    result = jnp.einsum("bjst,bjtc->bsc", op_blocks, picked, precision=lax.Precision.HIGHEST)
    return result.reshape(field.shape)


def chebyshev(struct_feats, op_blocks, laplace_index, series_coef, first_block, riders, later):
    count = op_blocks.shape[0]
    chans = struct_feats.shape[1]
    taps = 2 * REACH + 1
    halo = PER_EXCHANGE * REACH
    block_ids = first_block + jnp.arange(count, dtype=jnp.int32)
    offsets = laplace_index - block_ids[:, None] + REACH
    hit = offsets[:, :, None] == jnp.arange(taps, dtype=jnp.int32)[None, None, :]
    bands = jnp.sum(jnp.where(hit[:, :, :, None, None], op_blocks[:, :, None], 0.0), axis=1)
    bands = bands.transpose(0, 2, 1, 3).reshape(count, BS, taps * BS)
    own_field = struct_feats.reshape(count, BS, chans)
    payload = jnp.concatenate([own_field, bands], axis=2)
    left = shift_rows(payload[count - halo :], "seq", 1)
    right = shift_rows(payload[:halo], "seq", -1)
    edge = halo - REACH
    bands = jnp.concatenate(
        [left[halo - edge :, :, chans:], bands, right[:edge, :, chans:]], axis=0
    )
    field = jnp.concatenate([left[:, :, :chans], own_field, right[:, :, :chans]], axis=0)
    width = field.shape[0]

    def step(values, lo, hi, base):
        stacked = jnp.stack(
            [values[lo - REACH + o - base : hi - REACH + o - base] for o in range(taps)], axis=1
        ).reshape(hi - lo, taps * BS, chans)
        return jnp.einsum(
            "wsk,wkc->wsc", bands[lo - REACH : hi - REACH], stacked,
            precision=lax.Precision.HIGH, preferred_element_type=jnp.float32,
        )

    own = slice(halo, halo + count)
    cur, cur_base = field, 0
    prev, prev_base = None, 0
    encoding = series_coef[0] * field[own]
    for degree in range(1, DEG + 1):
        if degree > 1 and (degree - 1) % PER_EXCHANGE == 0:
            older = prev[own.start - prev_base : own.stop - prev_base]
            packed = jnp.concatenate([older, cur], axis=2)
            left = shift_rows(packed[count - halo :], "seq", 1)
            right = shift_rows(packed[:halo], "seq", -1)
            if later is not None:
                left, right, later = lax.optimization_barrier((left, right, later))
                riders = riders + (later,)
                later = None
            prev = jnp.concatenate(
                [left[halo - edge :, :, :chans], older, right[:edge, :, :chans]], axis=0
            )
            prev_base = REACH
            cur = jnp.concatenate([left[:, :, chans:], cur, right[:, :, chans:]], axis=0)
            cur_base = 0
            lo, hi = 0, width
        if degree == 1 or (degree - 1) % PER_EXCHANGE == 0:
            lo, hi = REACH, width - REACH
        else:
            lo, hi = lo + REACH, hi - REACH
        applied = step(cur, lo, hi, cur_base)
        if degree == 1:
            nxt = applied
        else:
            nxt = 2.0 * applied - prev[lo - prev_base : hi - prev_base]
        encoding = encoding + series_coef[degree] * nxt[own.start - lo : own.stop - lo]
        prev, prev_base = cur, cur_base
        cur, cur_base = nxt, lo
    return encoding.reshape(count * BS, chans), riders


def attention_kernel(table_ref, q_ref, *refs):
    kv_refs = refs[:NKEY]
    out_ref = refs[NKEY]
    lane = lax.broadcasted_iota(jnp.int32, (1, 2 * HD), 1)
    low = lane < HD
    for pair in range(HEADS // 2):
        cols = slice(pair * 2 * HD, (pair + 1) * 2 * HD)
        vcols = slice(D + pair * 2 * HD, D + (pair + 1) * 2 * HD)
        ks = jnp.concatenate([r[:, cols] for r in kv_refs], axis=0)
        vs = jnp.concatenate([r[:, vcols] for r in kv_refs], axis=0)
        scores = jnp.dot(ks, q_ref[0, pair], preferred_element_type=jnp.float32)
        top = jnp.max(scores, axis=0, keepdims=True)
        expd = jnp.exp(scores - top)
        total = jnp.sum(expd, axis=0, keepdims=True)
        weights = (expd * (1.0 / total)).astype(jnp.bfloat16)
        both = lax.dot_general(
            weights, vs, (((0,), (0,)), ((), ())), preferred_element_type=jnp.float32
        )
        merged = jnp.where(low, both[:BS], both[BS:])
        out_ref[:, cols] = merged.astype(jnp.bfloat16)


def split_queries(queries):
    count = queries.shape[0] // BS
    pairs = HEADS // 2
    qt = queries.reshape(count, BS, pairs, 2 * HD).transpose(0, 2, 3, 1)
    qt = jnp.concatenate([qt, qt], axis=3)
    d_head = lax.broadcasted_iota(jnp.int32, (2 * HD, 2 * BS), 0) // HD
    j_head = lax.broadcasted_iota(jnp.int32, (2 * HD, 2 * BS), 1) // BS
    scale = jnp.asarray(1.0 / HD**0.5, jnp.bfloat16)
    return jnp.where(d_head == j_head, qt * scale, jnp.zeros_like(qt))


def attend(queries, kv_sources, table):
    count = table.shape[0]
    pairs = HEADS // 2
    in_specs = [pl.BlockSpec((1, pairs, 2 * HD, 2 * BS), lambda b, t: (b, 0, 0, 0))]
    operands = [split_queries(queries)]
    for j, src in enumerate(kv_sources):
        in_specs.append(pl.BlockSpec((BS, 2 * D), lambda b, t, j=j: (t[b, j], 0)))
        operands.append(src)
    grid_spec = pltpu.PrefetchScalarGridSpec(
        num_scalar_prefetch=1,
        grid=(count,),
        in_specs=in_specs,
        out_specs=pl.BlockSpec((BS, D), lambda b, t: (b, 0)),
    )
    return pl.pallas_call(
        attention_kernel,
        grid_spec=grid_spec,
        out_shape=jax.ShapeDtypeStruct((count * BS, D), jnp.bfloat16),
    )(table, *operands)


def on_device(
    node_feats,
    struct_feats,
    op_blocks,
    laplace_index,
    graph_links,
    expander_slot,
    series_coef,
    encode_weight,
    qkv_weight,
    out_weight,
):
    count = op_blocks.shape[0]
    rows = count * BS
    rim = REACH * BS
    first_block = lax.axis_index("seq") * count
    levels = lax.axis_size("seq").bit_length() - 1
    bits = [link * (levels - 1) // (NEXP - 1) for link in range(NEXP)]

    half = rows // 2
    early = [partner(node_feats[:half], "seq", bit) for bit in bits[2:]]
    encoding, (early,) = chebyshev(
        struct_feats, op_blocks, laplace_index, series_coef, first_block, (), early,
    )
    late = [partner(node_feats[half:], "seq", bit) for bit in bits[2:]]
    near_far = partner(node_feats, "seq", bits[1])
    feats_before = shift_rows(node_feats[rows - rim:], "seq", 1)
    feats_after = shift_rows(node_feats[:rim], "seq", -1)
    encoding, late, near_far, feats_before, feats_after = lax.optimization_barrier(
        (encoding, late, near_far, feats_before, feats_after)
    )
    feats_far = [near_far] + [jnp.concatenate([a, b], axis=0) for a, b in zip(early, late)]
    encoding_b = encoding.astype(jnp.bfloat16)

    enc_before = shift_rows(encoding_b[rows - rim:], "seq", 1)
    enc_after = shift_rows(encoding_b[:rim], "seq", -1)
    enc_far = [partner(encoding_b, "seq", bit) for bit in bits[1:]]

    def blend(feats, enc):
        encoded = jnp.dot(enc, encode_weight, preferred_element_type=jnp.float32)
        return (feats.astype(jnp.float32) + encoded).astype(jnp.bfloat16)

    kv_weight = qkv_weight[:, D:]
    blended = blend(node_feats, encoding_b)
    queries = jnp.dot(blended, qkv_weight[:, :D], preferred_element_type=jnp.float32).astype(
        jnp.bfloat16
    )
    all_blended = jnp.concatenate(
        [blend(feats_before, enc_before), blended, blend(feats_after, enc_after)]
        + [blend(f, e) for f, e in zip(feats_far, enc_far)],
        axis=0,
    )
    kv_all = jnp.dot(all_blended, kv_weight, preferred_element_type=jnp.float32).astype(
        jnp.bfloat16
    )
    kv_own = kv_all[rim : rim + rows]
    kv_chip = partner(kv_own, "seq", bits[0])

    near_blocks = count + 2 * REACH
    own_slot = jnp.arange(count, dtype=jnp.int32)[:, None] + REACH
    graph_slot = jnp.clip(graph_links - first_block + REACH, 0, near_blocks - 1)
    far_slot = jnp.clip(expander_slot, 0, count - 1)
    far_base = jnp.asarray([0] + [near_blocks + k * count for k in range(NEXP - 1)], jnp.int32)
    table = jnp.concatenate([own_slot, graph_slot, far_slot + far_base[None, :]], axis=1)
    table = table.astype(jnp.int32)
    sources = [kv_all] * 4 + [kv_chip] + [kv_all] * (NEXP - 1)
    attended = attend(queries, sources, table)
    return jnp.dot(attended, out_weight, preferred_element_type=jnp.float32).astype(jnp.bfloat16)


def solution(mesh):
    placed = (
        P(("group", "seq"), None),
        P(("group", "seq"), None),
        P(("group", "seq"), None, None, None),
        P(("group", "seq"), None),
        P(("group", "seq"), None),
        P(("group", "seq"), None),
        P(),
        P(),
        P(),
        P(),
    )
    return jax.shard_map(
        on_device, mesh=mesh, in_specs=placed, out_specs=P(("group", "seq"), None), check_vma=False
    )
```

```python
import functools

import jax
import jax.numpy as jnp
from jax import lax
from jax.experimental import pallas as pl
from jax.experimental.pallas import tpu as pltpu
from jax.sharding import PartitionSpec as P

D = 1024
HEADS = 16
HD = 64
BS = 64
DEG = 8
NEXP = 4
REACH = 2
NKEY = 1 + 3 + NEXP
PER_EXCHANGE = 4


def shift_rows(x, axis, step):
    peers = lax.axis_size(axis)
    if step > 0:
        pairs = [(i, i + step) for i in range(peers - step)]
    else:
        pairs = [(i, i + step) for i in range(-step, peers)]
    return lax.ppermute(x, axis, pairs)


def extended(x, axis, width):
    length = x.shape[0]
    before = shift_rows(x[length - width:], axis, 1)
    after = shift_rows(x[:width], axis, -1)
    return jnp.concatenate([before, x, after], axis=0)


def partner(value, axis, distance):
    mask = 2**distance
    pairs = [(source, source ^ mask) for source in range(lax.axis_size(axis))]
    return lax.ppermute(value, axis, pairs)


def apply_operator(field, op_blocks, laplace_index, first_block):
    count = op_blocks.shape[0]
    padded = extended(field, "seq", REACH * BS)
    pooled = padded.reshape(count + 2 * REACH, BS, field.shape[1])
    position = laplace_index - first_block + REACH
    picked = pooled[position]
    result = jnp.einsum("bjst,bjtc->bsc", op_blocks, picked, precision=lax.Precision.HIGHEST)
    return result.reshape(field.shape)


def chebyshev(struct_feats, op_blocks, laplace_index, series_coef, first_block, riders, later):
    count = op_blocks.shape[0]
    chans = struct_feats.shape[1]
    taps = 2 * REACH + 1
    halo = PER_EXCHANGE * REACH
    block_ids = first_block + jnp.arange(count, dtype=jnp.int32)
    offsets = laplace_index - block_ids[:, None] + REACH
    hit = offsets[:, :, None] == jnp.arange(taps, dtype=jnp.int32)[None, None, :]
    bands = jnp.sum(jnp.where(hit[:, :, :, None, None], op_blocks[:, :, None], 0.0), axis=1)
    bands = bands.transpose(0, 2, 1, 3).reshape(count, BS, taps * BS)
    own_field = struct_feats.reshape(count, BS, chans)
    payload = jnp.concatenate([own_field, bands], axis=2)
    left = shift_rows(payload[count - halo :], "seq", 1)
    right = shift_rows(payload[:halo], "seq", -1)
    edge = halo - REACH
    bands = jnp.concatenate(
        [left[halo - edge :, :, chans:], bands, right[:edge, :, chans:]], axis=0
    )
    field = jnp.concatenate([left[:, :, :chans], own_field, right[:, :, :chans]], axis=0)
    width = field.shape[0]

    def step(values, lo, hi, base):
        stacked = jnp.stack(
            [values[lo - REACH + o - base : hi - REACH + o - base] for o in range(taps)], axis=1
        ).reshape(hi - lo, taps * BS, chans)
        return jnp.einsum(
            "wsk,wkc->wsc", bands[lo - REACH : hi - REACH], stacked,
            precision=lax.Precision.HIGH, preferred_element_type=jnp.float32,
        )

    own = slice(halo, halo + count)
    cur, cur_base = field, 0
    prev, prev_base = None, 0
    encoding = series_coef[0] * field[own]
    for degree in range(1, DEG + 1):
        if degree > 1 and (degree - 1) % PER_EXCHANGE == 0:
            older = prev[own.start - prev_base : own.stop - prev_base]
            packed = jnp.concatenate([older, cur], axis=2)
            left = shift_rows(packed[count - halo :], "seq", 1)
            right = shift_rows(packed[:halo], "seq", -1)
            if later is not None:
                left, right, later = lax.optimization_barrier((left, right, later))
                riders = riders + (later,)
                later = None
            prev = jnp.concatenate(
                [left[halo - edge :, :, :chans], older, right[:edge, :, :chans]], axis=0
            )
            prev_base = REACH
            cur = jnp.concatenate([left[:, :, chans:], cur, right[:, :, chans:]], axis=0)
            cur_base = 0
            lo, hi = 0, width
        if degree == 1 or (degree - 1) % PER_EXCHANGE == 0:
            lo, hi = REACH, width - REACH
        else:
            lo, hi = lo + REACH, hi - REACH
        applied = step(cur, lo, hi, cur_base)
        if degree == 1:
            nxt = applied
        else:
            nxt = 2.0 * applied - prev[lo - prev_base : hi - prev_base]
        encoding = encoding + series_coef[degree] * nxt[own.start - lo : own.stop - lo]
        prev, prev_base = cur, cur_base
        cur, cur_base = nxt, lo
    return encoding.reshape(count * BS, chans), riders


def attention_kernel(table_ref, q_ref, *refs):
    kv_refs = refs[:NKEY]
    out_ref = refs[NKEY]
    lane = lax.broadcasted_iota(jnp.int32, (1, 2 * HD), 1)
    low = lane < HD
    for pair in range(HEADS // 2):
        cols = slice(pair * 2 * HD, (pair + 1) * 2 * HD)
        vcols = slice(D + pair * 2 * HD, D + (pair + 1) * 2 * HD)
        ks = jnp.concatenate([r[:, cols] for r in kv_refs], axis=0)
        vs = jnp.concatenate([r[:, vcols] for r in kv_refs], axis=0)
        scores = jnp.dot(ks, q_ref[0, pair], preferred_element_type=jnp.float32)
        top = jnp.max(scores, axis=0, keepdims=True)
        expd = jnp.exp(scores - top)
        total = jnp.sum(expd, axis=0, keepdims=True)
        weights = (expd * (1.0 / total)).astype(jnp.bfloat16)
        both = lax.dot_general(
            weights, vs, (((0,), (0,)), ((), ())), preferred_element_type=jnp.float32
        )
        merged = jnp.where(low, both[:BS], both[BS:])
        out_ref[:, cols] = merged.astype(jnp.bfloat16)


def split_queries(queries):
    count = queries.shape[0] // BS
    pairs = HEADS // 2
    qt = queries.reshape(count, BS, pairs, 2 * HD).transpose(0, 2, 3, 1)
    qt = jnp.concatenate([qt, qt], axis=3)
    d_head = lax.broadcasted_iota(jnp.int32, (2 * HD, 2 * BS), 0) // HD
    j_head = lax.broadcasted_iota(jnp.int32, (2 * HD, 2 * BS), 1) // BS
    scale = jnp.asarray(1.0 / HD**0.5, jnp.bfloat16)
    return jnp.where(d_head == j_head, qt * scale, jnp.zeros_like(qt))


def attend(queries, kv_sources, table):
    count = table.shape[0]
    pairs = HEADS // 2
    in_specs = [pl.BlockSpec((1, pairs, 2 * HD, 2 * BS), lambda b, t: (b, 0, 0, 0))]
    operands = [split_queries(queries)]
    for j, src in enumerate(kv_sources):
        in_specs.append(pl.BlockSpec((BS, 2 * D), lambda b, t, j=j: (t[b, j], 0)))
        operands.append(src)
    grid_spec = pltpu.PrefetchScalarGridSpec(
        num_scalar_prefetch=1,
        grid=(count,),
        in_specs=in_specs,
        out_specs=pl.BlockSpec((BS, D), lambda b, t: (b, 0)),
    )
    return pl.pallas_call(
        attention_kernel,
        grid_spec=grid_spec,
        out_shape=jax.ShapeDtypeStruct((count * BS, D), jnp.bfloat16),
    )(table, *operands)


def on_device(
    node_feats,
    struct_feats,
    op_blocks,
    laplace_index,
    graph_links,
    expander_slot,
    series_coef,
    encode_weight,
    qkv_weight,
    out_weight,
):
    count = op_blocks.shape[0]
    rows = count * BS
    rim = REACH * BS
    first_block = lax.axis_index("seq") * count
    levels = lax.axis_size("seq").bit_length() - 1
    bits = [link * (levels - 1) // (NEXP - 1) for link in range(NEXP)]

    half = rows // 2
    early = [partner(node_feats[:half], "seq", bit) for bit in bits[2:]]
    encoding, (early,) = chebyshev(
        struct_feats, op_blocks, laplace_index, series_coef, first_block, (), early,
    )
    late = [partner(node_feats[half:], "seq", bit) for bit in bits[2:]]
    near_far = partner(node_feats, "seq", bits[1])
    encoding, late, near_far = lax.optimization_barrier((encoding, late, near_far))
    feats_far = [near_far] + [jnp.concatenate([a, b], axis=0) for a, b in zip(early, late)]
    encoding_b = encoding.astype(jnp.bfloat16)

    enc_far = [partner(encoding_b, "seq", bit) for bit in bits[1:]]

    def blend(feats, enc):
        encoded = jnp.dot(enc, encode_weight, preferred_element_type=jnp.float32)
        return (feats.astype(jnp.float32) + encoded).astype(jnp.bfloat16)

    kv_weight = qkv_weight[:, D:]
    blended = blend(node_feats, encoding_b)
    queries = jnp.dot(blended, qkv_weight[:, :D], preferred_element_type=jnp.float32).astype(
        jnp.bfloat16
    )
    all_blended = jnp.concatenate(
        [shift_rows(blended[rows - rim:], "seq", 1), blended, shift_rows(blended[:rim], "seq", -1)]
        + [blend(f, e) for f, e in zip(feats_far, enc_far)],
        axis=0,
    )
    kv_all = jnp.dot(all_blended, kv_weight, preferred_element_type=jnp.float32).astype(
        jnp.bfloat16
    )
    kv_own = kv_all[rim : rim + rows]
    kv_chip = partner(kv_own, "seq", bits[0])

    near_blocks = count + 2 * REACH
    own_slot = jnp.arange(count, dtype=jnp.int32)[:, None] + REACH
    graph_slot = jnp.clip(graph_links - first_block + REACH, 0, near_blocks - 1)
    far_slot = jnp.clip(expander_slot, 0, count - 1)
    far_base = jnp.asarray([0] + [near_blocks + k * count for k in range(NEXP - 1)], jnp.int32)
    table = jnp.concatenate([own_slot, graph_slot, far_slot + far_base[None, :]], axis=1)
    table = table.astype(jnp.int32)
    sources = [kv_all] * 4 + [kv_chip] + [kv_all] * (NEXP - 1)
    attended = attend(queries, sources, table)
    return jnp.dot(attended, out_weight, preferred_element_type=jnp.float32).astype(jnp.bfloat16)


def solution(mesh):
    placed = (
        P(("group", "seq"), None),
        P(("group", "seq"), None),
        P(("group", "seq"), None, None, None),
        P(("group", "seq"), None),
        P(("group", "seq"), None),
        P(("group", "seq"), None),
        P(),
        P(),
        P(),
        P(),
    )
    return jax.shard_map(
        on_device, mesh=mesh, in_specs=placed, out_specs=P(("group", "seq"), None), check_vma=False
    )
```

```python
import functools

import jax
import jax.numpy as jnp
from jax import lax
from jax.experimental import pallas as pl
from jax.experimental.pallas import tpu as pltpu
from jax.sharding import PartitionSpec as P

D = 1024
HEADS = 16
HD = 64
BS = 64
DEG = 8
NEXP = 4
REACH = 2
NKEY = 1 + 3 + NEXP
PER_EXCHANGE = 4


def shift_rows(x, axis, step):
    peers = lax.axis_size(axis)
    if step > 0:
        pairs = [(i, i + step) for i in range(peers - step)]
    else:
        pairs = [(i, i + step) for i in range(-step, peers)]
    return lax.ppermute(x, axis, pairs)


def extended(x, axis, width):
    length = x.shape[0]
    before = shift_rows(x[length - width:], axis, 1)
    after = shift_rows(x[:width], axis, -1)
    return jnp.concatenate([before, x, after], axis=0)


def partner(value, axis, distance):
    mask = 2**distance
    pairs = [(source, source ^ mask) for source in range(lax.axis_size(axis))]
    return lax.ppermute(value, axis, pairs)


def apply_operator(field, op_blocks, laplace_index, first_block):
    count = op_blocks.shape[0]
    padded = extended(field, "seq", REACH * BS)
    pooled = padded.reshape(count + 2 * REACH, BS, field.shape[1])
    position = laplace_index - first_block + REACH
    picked = pooled[position]
    result = jnp.einsum("bjst,bjtc->bsc", op_blocks, picked, precision=lax.Precision.HIGHEST)
    return result.reshape(field.shape)


def chebyshev(struct_feats, op_blocks, laplace_index, series_coef, first_block, riders, later):
    count = op_blocks.shape[0]
    chans = struct_feats.shape[1]
    taps = 2 * REACH + 1
    halo = PER_EXCHANGE * REACH
    block_ids = first_block + jnp.arange(count, dtype=jnp.int32)
    offsets = laplace_index - block_ids[:, None] + REACH
    hit = offsets[:, :, None] == jnp.arange(taps, dtype=jnp.int32)[None, None, :]
    bands = jnp.sum(jnp.where(hit[:, :, :, None, None], op_blocks[:, :, None], 0.0), axis=1)
    bands = bands.transpose(0, 2, 1, 3).reshape(count, BS, taps * BS)
    own_field = struct_feats.reshape(count, BS, chans)
    payload = jnp.concatenate([own_field, bands], axis=2)
    left = shift_rows(payload[count - halo :], "seq", 1)
    right = shift_rows(payload[:halo], "seq", -1)
    edge = halo - REACH
    bands = jnp.concatenate(
        [left[halo - edge :, :, chans:], bands, right[:edge, :, chans:]], axis=0
    )
    field = jnp.concatenate([left[:, :, :chans], own_field, right[:, :, :chans]], axis=0)
    width = field.shape[0]

    def step(values, lo, hi, base):
        stacked = jnp.stack(
            [values[lo - REACH + o - base : hi - REACH + o - base] for o in range(taps)], axis=1
        ).reshape(hi - lo, taps * BS, chans)
        return jnp.einsum(
            "wsk,wkc->wsc", bands[lo - REACH : hi - REACH], stacked,
            precision=lax.Precision.HIGH, preferred_element_type=jnp.float32,
        )

    own = slice(halo, halo + count)
    cur, cur_base = field, 0
    prev, prev_base = None, 0
    encoding = series_coef[0] * field[own]
    for degree in range(1, DEG + 1):
        if degree > 1 and (degree - 1) % PER_EXCHANGE == 0:
            older = prev[own.start - prev_base : own.stop - prev_base]
            packed = jnp.concatenate([older, cur], axis=2)
            left = shift_rows(packed[count - halo :], "seq", 1)
            right = shift_rows(packed[:halo], "seq", -1)
            if later is not None:
                left, right, later = lax.optimization_barrier((left, right, later))
                riders = riders + (later,)
                later = None
            prev = jnp.concatenate(
                [left[halo - edge :, :, :chans], older, right[:edge, :, :chans]], axis=0
            )
            prev_base = REACH
            cur = jnp.concatenate([left[:, :, chans:], cur, right[:, :, chans:]], axis=0)
            cur_base = 0
            lo, hi = 0, width
        if degree == 1 or (degree - 1) % PER_EXCHANGE == 0:
            lo, hi = REACH, width - REACH
        else:
            lo, hi = lo + REACH, hi - REACH
        applied = step(cur, lo, hi, cur_base)
        if degree == 1:
            nxt = applied
        else:
            nxt = 2.0 * applied - prev[lo - prev_base : hi - prev_base]
        encoding = encoding + series_coef[degree] * nxt[own.start - lo : own.stop - lo]
        prev, prev_base = cur, cur_base
        cur, cur_base = nxt, lo
    return encoding.reshape(count * BS, chans), riders


def attention_kernel(table_ref, q_ref, *refs):
    kv_refs = refs[:NKEY]
    out_ref = refs[NKEY]
    lane = lax.broadcasted_iota(jnp.int32, (1, 2 * HD), 1)
    low = lane < HD
    for pair in range(HEADS // 2):
        cols = slice(pair * 2 * HD, (pair + 1) * 2 * HD)
        vcols = slice(D + pair * 2 * HD, D + (pair + 1) * 2 * HD)
        ks = jnp.concatenate([r[:, cols] for r in kv_refs], axis=0)
        vs = jnp.concatenate([r[:, vcols] for r in kv_refs], axis=0)
        scores = jnp.dot(ks, q_ref[0, pair], preferred_element_type=jnp.float32)
        top = jnp.max(scores, axis=0, keepdims=True)
        expd = jnp.exp(scores - top)
        total = jnp.sum(expd, axis=0, keepdims=True)
        weights = (expd * (1.0 / total)).astype(jnp.bfloat16)
        both = lax.dot_general(
            weights, vs, (((0,), (0,)), ((), ())), preferred_element_type=jnp.float32
        )
        merged = jnp.where(low, both[:BS], both[BS:])
        out_ref[:, cols] = merged.astype(jnp.bfloat16)


def split_queries(queries):
    count = queries.shape[0] // BS
    pairs = HEADS // 2
    qt = queries.reshape(count, BS, pairs, 2 * HD).transpose(0, 2, 3, 1)
    qt = jnp.concatenate([qt, qt], axis=3)
    d_head = lax.broadcasted_iota(jnp.int32, (2 * HD, 2 * BS), 0) // HD
    j_head = lax.broadcasted_iota(jnp.int32, (2 * HD, 2 * BS), 1) // BS
    scale = jnp.asarray(1.0 / HD**0.5, jnp.bfloat16)
    return jnp.where(d_head == j_head, qt * scale, jnp.zeros_like(qt))


def attend(queries, kv_sources, table):
    count = table.shape[0]
    pairs = HEADS // 2
    in_specs = [pl.BlockSpec((1, pairs, 2 * HD, 2 * BS), lambda b, t: (b, 0, 0, 0))]
    operands = [queries]
    for j, src in enumerate(kv_sources):
        in_specs.append(pl.BlockSpec((BS, 2 * D), lambda b, t, j=j: (t[b, j], 0)))
        operands.append(src)
    grid_spec = pltpu.PrefetchScalarGridSpec(
        num_scalar_prefetch=1,
        grid=(count,),
        in_specs=in_specs,
        out_specs=pl.BlockSpec((BS, D), lambda b, t: (b, 0)),
    )
    return pl.pallas_call(
        attention_kernel,
        grid_spec=grid_spec,
        out_shape=jax.ShapeDtypeStruct((count * BS, D), jnp.bfloat16),
    )(table, *operands)


def on_device(
    node_feats,
    struct_feats,
    op_blocks,
    laplace_index,
    graph_links,
    expander_slot,
    series_coef,
    encode_weight,
    qkv_weight,
    out_weight,
):
    count = op_blocks.shape[0]
    rows = count * BS
    rim = REACH * BS
    first_block = lax.axis_index("seq") * count
    levels = lax.axis_size("seq").bit_length() - 1
    bits = [link * (levels - 1) // (NEXP - 1) for link in range(NEXP)]

    half = rows // 2
    early = [partner(node_feats[:half], "seq", bit) for bit in bits[2:]]
    encoding, (early,) = chebyshev(
        struct_feats, op_blocks, laplace_index, series_coef, first_block, (), early,
    )
    late = [partner(node_feats[half:], "seq", bit) for bit in bits[2:]]
    near_far = partner(node_feats, "seq", bits[1])
    encoding, late, near_far = lax.optimization_barrier((encoding, late, near_far))
    feats_far = [near_far] + [jnp.concatenate([a, b], axis=0) for a, b in zip(early, late)]
    encoding_b = encoding.astype(jnp.bfloat16)

    enc_far = [partner(encoding_b, "seq", bit) for bit in bits[1:]]

    def blend(feats, enc):
        encoded = jnp.dot(enc, encode_weight, preferred_element_type=jnp.float32)
        return (feats.astype(jnp.float32) + encoded).astype(jnp.bfloat16)

    kv_weight = qkv_weight[:, D:]
    blended = blend(node_feats, encoding_b)
    queries = jnp.dot(blended, qkv_weight[:, :D], preferred_element_type=jnp.float32).astype(
        jnp.bfloat16
    )
    queries, enc_far = lax.optimization_barrier((split_queries(queries), enc_far))
    all_blended = jnp.concatenate(
        [shift_rows(blended[rows - rim:], "seq", 1), blended, shift_rows(blended[:rim], "seq", -1)]
        + [blend(f, e) for f, e in zip(feats_far, enc_far)],
        axis=0,
    )
    kv_all = jnp.dot(all_blended, kv_weight, preferred_element_type=jnp.float32).astype(
        jnp.bfloat16
    )
    kv_own = kv_all[rim : rim + rows]
    kv_chip = partner(kv_own, "seq", bits[0])

    near_blocks = count + 2 * REACH
    own_slot = jnp.arange(count, dtype=jnp.int32)[:, None] + REACH
    graph_slot = jnp.clip(graph_links - first_block + REACH, 0, near_blocks - 1)
    far_slot = jnp.clip(expander_slot, 0, count - 1)
    far_base = jnp.asarray([0] + [near_blocks + k * count for k in range(NEXP - 1)], jnp.int32)
    table = jnp.concatenate([own_slot, graph_slot, far_slot + far_base[None, :]], axis=1)
    table = table.astype(jnp.int32)
    sources = [kv_all] * 4 + [kv_chip] + [kv_all] * (NEXP - 1)
    attended = attend(queries, sources, table)
    return jnp.dot(attended, out_weight, preferred_element_type=jnp.float32).astype(jnp.bfloat16)


def solution(mesh):
    placed = (
        P(("group", "seq"), None),
        P(("group", "seq"), None),
        P(("group", "seq"), None, None, None),
        P(("group", "seq"), None),
        P(("group", "seq"), None),
        P(("group", "seq"), None),
        P(),
        P(),
        P(),
        P(),
    )
    return jax.shard_map(
        on_device, mesh=mesh, in_specs=placed, out_specs=P(("group", "seq"), None), check_vma=False
    )
```

```python
import functools

import jax
import jax.numpy as jnp
from jax import lax
from jax.experimental import pallas as pl
from jax.experimental.pallas import tpu as pltpu
from jax.sharding import PartitionSpec as P

D = 1024
HEADS = 16
HD = 64
BS = 64
DEG = 8
NEXP = 4
REACH = 2
NKEY = 1 + 3 + NEXP
PER_EXCHANGE = 4


def shift_rows(x, axis, step):
    peers = lax.axis_size(axis)
    if step > 0:
        pairs = [(i, i + step) for i in range(peers - step)]
    else:
        pairs = [(i, i + step) for i in range(-step, peers)]
    return lax.ppermute(x, axis, pairs)


def extended(x, axis, width):
    length = x.shape[0]
    before = shift_rows(x[length - width:], axis, 1)
    after = shift_rows(x[:width], axis, -1)
    return jnp.concatenate([before, x, after], axis=0)


def partner(value, axis, distance):
    mask = 2**distance
    pairs = [(source, source ^ mask) for source in range(lax.axis_size(axis))]
    return lax.ppermute(value, axis, pairs)


def apply_operator(field, op_blocks, laplace_index, first_block):
    count = op_blocks.shape[0]
    padded = extended(field, "seq", REACH * BS)
    pooled = padded.reshape(count + 2 * REACH, BS, field.shape[1])
    position = laplace_index - first_block + REACH
    picked = pooled[position]
    result = jnp.einsum("bjst,bjtc->bsc", op_blocks, picked, precision=lax.Precision.HIGHEST)
    return result.reshape(field.shape)


def chebyshev(struct_feats, op_blocks, laplace_index, series_coef, first_block, riders, later):
    count = op_blocks.shape[0]
    chans = struct_feats.shape[1]
    taps = 2 * REACH + 1
    halo = PER_EXCHANGE * REACH
    block_ids = first_block + jnp.arange(count, dtype=jnp.int32)
    offsets = laplace_index - block_ids[:, None] + REACH
    hit = offsets[:, :, None] == jnp.arange(taps, dtype=jnp.int32)[None, None, :]
    bands = jnp.sum(jnp.where(hit[:, :, :, None, None], op_blocks[:, :, None], 0.0), axis=1)
    bands = bands.transpose(0, 2, 1, 3).reshape(count, BS, taps * BS)
    own_field = struct_feats.reshape(count, BS, chans)
    payload = jnp.concatenate([own_field, bands], axis=2)
    left = shift_rows(payload[count - halo :], "seq", 1)
    right = shift_rows(payload[:halo], "seq", -1)
    edge = halo - REACH
    bands = jnp.concatenate(
        [left[halo - edge :, :, chans:], bands, right[:edge, :, chans:]], axis=0
    )
    field = jnp.concatenate([left[:, :, :chans], own_field, right[:, :, :chans]], axis=0)
    width = field.shape[0]

    def step(values, lo, hi, base):
        stacked = jnp.stack(
            [values[lo - REACH + o - base : hi - REACH + o - base] for o in range(taps)], axis=1
        ).reshape(hi - lo, taps * BS, chans)
        return jnp.einsum(
            "wsk,wkc->wsc", bands[lo - REACH : hi - REACH], stacked,
            precision=lax.Precision.HIGH, preferred_element_type=jnp.float32,
        )

    own = slice(halo, halo + count)
    cur, cur_base = field, 0
    prev, prev_base = None, 0
    encoding = series_coef[0] * field[own]
    for degree in range(1, DEG + 1):
        if degree > 1 and (degree - 1) % PER_EXCHANGE == 0:
            older = prev[own.start - prev_base : own.stop - prev_base]
            packed = jnp.concatenate([older, cur], axis=2)
            left = shift_rows(packed[count - halo :], "seq", 1)
            right = shift_rows(packed[:halo], "seq", -1)
            if later is not None:
                left, right, later = lax.optimization_barrier((left, right, later))
                riders = riders + (later,)
                later = None
            prev = jnp.concatenate(
                [left[halo - edge :, :, :chans], older, right[:edge, :, :chans]], axis=0
            )
            prev_base = REACH
            cur = jnp.concatenate([left[:, :, chans:], cur, right[:, :, chans:]], axis=0)
            cur_base = 0
            lo, hi = 0, width
        if degree == 1 or (degree - 1) % PER_EXCHANGE == 0:
            lo, hi = REACH, width - REACH
        else:
            lo, hi = lo + REACH, hi - REACH
        applied = step(cur, lo, hi, cur_base)
        if degree == 1:
            nxt = applied
        else:
            nxt = 2.0 * applied - prev[lo - prev_base : hi - prev_base]
        encoding = encoding + series_coef[degree] * nxt[own.start - lo : own.stop - lo]
        prev, prev_base = cur, cur_base
        cur, cur_base = nxt, lo
    return encoding.reshape(count * BS, chans), riders


def attention_kernel(table_ref, q_ref, *refs):
    kv_refs = refs[:NKEY]
    w_ref, out_ref, att_ref = refs[NKEY:]
    lane = lax.broadcasted_iota(jnp.int32, (1, 2 * HD), 1)
    low = lane < HD
    for pair in range(HEADS // 2):
        cols = slice(pair * 2 * HD, (pair + 1) * 2 * HD)
        vcols = slice(D + pair * 2 * HD, D + (pair + 1) * 2 * HD)
        ks = jnp.concatenate([r[:, cols] for r in kv_refs], axis=0)
        vs = jnp.concatenate([r[:, vcols] for r in kv_refs], axis=0)
        scores = jnp.dot(ks, q_ref[0, pair], preferred_element_type=jnp.float32)
        top = jnp.max(scores, axis=0, keepdims=True)
        expd = jnp.exp(scores - top)
        total = jnp.sum(expd, axis=0, keepdims=True)
        weights = (expd * (1.0 / total)).astype(jnp.bfloat16)
        both = lax.dot_general(
            weights, vs, (((0,), (0,)), ((), ())), preferred_element_type=jnp.float32
        )
        merged = jnp.where(low, both[:BS], both[BS:])
        att_ref[:, cols] = merged.astype(jnp.bfloat16)
    out_ref[...] = jnp.dot(att_ref[...], w_ref[...], preferred_element_type=jnp.float32).astype(
        jnp.bfloat16
    )


def split_queries(queries):
    count = queries.shape[0] // BS
    pairs = HEADS // 2
    qt = queries.reshape(count, BS, pairs, 2 * HD).transpose(0, 2, 3, 1)
    qt = jnp.concatenate([qt, qt], axis=3)
    d_head = lax.broadcasted_iota(jnp.int32, (2 * HD, 2 * BS), 0) // HD
    j_head = lax.broadcasted_iota(jnp.int32, (2 * HD, 2 * BS), 1) // BS
    scale = jnp.asarray(1.0 / HD**0.5, jnp.bfloat16)
    return jnp.where(d_head == j_head, qt * scale, jnp.zeros_like(qt))


def attend(queries, kv_sources, table, out_weight):
    count = table.shape[0]
    pairs = HEADS // 2
    in_specs = [pl.BlockSpec((1, pairs, 2 * HD, 2 * BS), lambda b, t: (b, 0, 0, 0))]
    operands = [split_queries(queries)]
    for j, src in enumerate(kv_sources):
        in_specs.append(pl.BlockSpec((BS, 2 * D), lambda b, t, j=j: (t[b, j], 0)))
        operands.append(src)
    in_specs.append(pl.BlockSpec(out_weight.shape, lambda b, t: (0, 0)))
    operands.append(out_weight)
    grid_spec = pltpu.PrefetchScalarGridSpec(
        num_scalar_prefetch=1,
        grid=(count,),
        in_specs=in_specs,
        out_specs=pl.BlockSpec((BS, D), lambda b, t: (b, 0)),
        scratch_shapes=[pltpu.VMEM((BS, D), jnp.bfloat16)],
    )
    return pl.pallas_call(
        attention_kernel,
        grid_spec=grid_spec,
        out_shape=jax.ShapeDtypeStruct((count * BS, D), jnp.bfloat16),
    )(table, *operands)


def on_device(
    node_feats,
    struct_feats,
    op_blocks,
    laplace_index,
    graph_links,
    expander_slot,
    series_coef,
    encode_weight,
    qkv_weight,
    out_weight,
):
    count = op_blocks.shape[0]
    rows = count * BS
    rim = REACH * BS
    first_block = lax.axis_index("seq") * count
    levels = lax.axis_size("seq").bit_length() - 1
    bits = [link * (levels - 1) // (NEXP - 1) for link in range(NEXP)]

    half = rows // 2
    early = [partner(node_feats[:half], "seq", bit) for bit in bits[2:]]
    encoding, (early,) = chebyshev(
        struct_feats, op_blocks, laplace_index, series_coef, first_block, (), early,
    )
    late = [partner(node_feats[half:], "seq", bit) for bit in bits[2:]]
    near_far = partner(node_feats, "seq", bits[1])
    encoding, late, near_far = lax.optimization_barrier((encoding, late, near_far))
    feats_far = [near_far] + [jnp.concatenate([a, b], axis=0) for a, b in zip(early, late)]
    encoding_b = encoding.astype(jnp.bfloat16)

    enc_far = [partner(encoding_b, "seq", bit) for bit in bits[1:]]

    def blend(feats, enc):
        encoded = jnp.dot(enc, encode_weight, preferred_element_type=jnp.float32)
        return (feats.astype(jnp.float32) + encoded).astype(jnp.bfloat16)

    kv_weight = qkv_weight[:, D:]
    blended = blend(node_feats, encoding_b)
    queries = jnp.dot(blended, qkv_weight[:, :D], preferred_element_type=jnp.float32).astype(
        jnp.bfloat16
    )
    all_blended = jnp.concatenate(
        [shift_rows(blended[rows - rim:], "seq", 1), blended, shift_rows(blended[:rim], "seq", -1)]
        + [blend(f, e) for f, e in zip(feats_far, enc_far)],
        axis=0,
    )
    kv_all = jnp.dot(all_blended, kv_weight, preferred_element_type=jnp.float32).astype(
        jnp.bfloat16
    )
    kv_own = kv_all[rim : rim + rows]
    kv_chip = partner(kv_own, "seq", bits[0])

    near_blocks = count + 2 * REACH
    own_slot = jnp.arange(count, dtype=jnp.int32)[:, None] + REACH
    graph_slot = jnp.clip(graph_links - first_block + REACH, 0, near_blocks - 1)
    far_slot = jnp.clip(expander_slot, 0, count - 1)
    far_base = jnp.asarray([0] + [near_blocks + k * count for k in range(NEXP - 1)], jnp.int32)
    table = jnp.concatenate([own_slot, graph_slot, far_slot + far_base[None, :]], axis=1)
    table = table.astype(jnp.int32)
    sources = [kv_all] * 4 + [kv_chip] + [kv_all] * (NEXP - 1)
    return attend(queries, sources, table, out_weight)


def solution(mesh):
    placed = (
        P(("group", "seq"), None),
        P(("group", "seq"), None),
        P(("group", "seq"), None, None, None),
        P(("group", "seq"), None),
        P(("group", "seq"), None),
        P(("group", "seq"), None),
        P(),
        P(),
        P(),
        P(),
    )
    return jax.shard_map(
        on_device, mesh=mesh, in_specs=placed, out_specs=P(("group", "seq"), None), check_vma=False
    )
```

```python
import functools

import jax
import jax.numpy as jnp
from jax import lax
from jax.experimental import pallas as pl
from jax.experimental.pallas import tpu as pltpu
from jax.sharding import PartitionSpec as P

D = 1024
HEADS = 16
HD = 64
BS = 64
DEG = 8
NEXP = 4
REACH = 2
NKEY = 1 + 3 + NEXP
PER_EXCHANGE = 4


def shift_rows(x, axis, step):
    peers = lax.axis_size(axis)
    if step > 0:
        pairs = [(i, i + step) for i in range(peers - step)]
    else:
        pairs = [(i, i + step) for i in range(-step, peers)]
    return lax.ppermute(x, axis, pairs)


def extended(x, axis, width):
    length = x.shape[0]
    before = shift_rows(x[length - width:], axis, 1)
    after = shift_rows(x[:width], axis, -1)
    return jnp.concatenate([before, x, after], axis=0)


def partner(value, axis, distance):
    mask = 2**distance
    pairs = [(source, source ^ mask) for source in range(lax.axis_size(axis))]
    return lax.ppermute(value, axis, pairs)


def apply_operator(field, op_blocks, laplace_index, first_block):
    count = op_blocks.shape[0]
    padded = extended(field, "seq", REACH * BS)
    pooled = padded.reshape(count + 2 * REACH, BS, field.shape[1])
    position = laplace_index - first_block + REACH
    picked = pooled[position]
    result = jnp.einsum("bjst,bjtc->bsc", op_blocks, picked, precision=lax.Precision.HIGHEST)
    return result.reshape(field.shape)


def chebyshev(struct_feats, op_blocks, laplace_index, series_coef, first_block, riders, later):
    count = op_blocks.shape[0]
    chans = struct_feats.shape[1]
    taps = 2 * REACH + 1
    halo = PER_EXCHANGE * REACH
    block_ids = first_block + jnp.arange(count, dtype=jnp.int32)
    offsets = laplace_index - block_ids[:, None] + REACH
    hit = offsets[:, :, None] == jnp.arange(taps, dtype=jnp.int32)[None, None, :]
    bands = jnp.sum(jnp.where(hit[:, :, :, None, None], op_blocks[:, :, None], 0.0), axis=1)
    bands = bands.transpose(0, 2, 1, 3).reshape(count, BS, taps * BS)
    own_field = struct_feats.reshape(count, BS, chans)
    payload = jnp.concatenate([own_field, bands], axis=2)
    left = shift_rows(payload[count - halo :], "seq", 1)
    right = shift_rows(payload[:halo], "seq", -1)
    edge = halo - REACH
    bands = jnp.concatenate(
        [left[halo - edge :, :, chans:], bands, right[:edge, :, chans:]], axis=0
    )
    field = jnp.concatenate([left[:, :, :chans], own_field, right[:, :, :chans]], axis=0)
    width = field.shape[0]

    def step(values, lo, hi, base):
        stacked = jnp.stack(
            [values[lo - REACH + o - base : hi - REACH + o - base] for o in range(taps)], axis=1
        ).reshape(hi - lo, taps * BS, chans)
        return jnp.einsum(
            "wsk,wkc->wsc", bands[lo - REACH : hi - REACH], stacked,
            precision=lax.Precision.HIGH, preferred_element_type=jnp.float32,
        )

    own = slice(halo, halo + count)
    cur, cur_base = field, 0
    prev, prev_base = None, 0
    encoding = series_coef[0] * field[own]
    for degree in range(1, DEG + 1):
        if degree > 1 and (degree - 1) % PER_EXCHANGE == 0:
            older = prev[own.start - prev_base : own.stop - prev_base]
            packed = jnp.concatenate([older, cur], axis=2)
            left = shift_rows(packed[count - halo :], "seq", 1)
            right = shift_rows(packed[:halo], "seq", -1)
            if later is not None:
                left, right, later = lax.optimization_barrier((left, right, later))
                riders = riders + (later,)
                later = None
            prev = jnp.concatenate(
                [left[halo - edge :, :, :chans], older, right[:edge, :, :chans]], axis=0
            )
            prev_base = REACH
            cur = jnp.concatenate([left[:, :, chans:], cur, right[:, :, chans:]], axis=0)
            cur_base = 0
            lo, hi = 0, width
        if degree == 1 or (degree - 1) % PER_EXCHANGE == 0:
            lo, hi = REACH, width - REACH
        else:
            lo, hi = lo + REACH, hi - REACH
        applied = step(cur, lo, hi, cur_base)
        if degree == 1:
            nxt = applied
        else:
            nxt = 2.0 * applied - prev[lo - prev_base : hi - prev_base]
        encoding = encoding + series_coef[degree] * nxt[own.start - lo : own.stop - lo]
        prev, prev_base = cur, cur_base
        cur, cur_base = nxt, lo
    return encoding.reshape(count * BS, chans), riders


def attention_kernel(table_ref, q_ref, *refs):
    kv_refs = refs[:NKEY]
    w_ref, out_ref, att_ref = refs[NKEY:]
    lane = lax.broadcasted_iota(jnp.int32, (1, 2 * HD), 1)
    low = lane < HD
    for pair in range(HEADS // 2):
        cols = slice(pair * 2 * HD, (pair + 1) * 2 * HD)
        vcols = slice(D + pair * 2 * HD, D + (pair + 1) * 2 * HD)
        qbd = q_ref[0, pair]
        scores = [jnp.dot(r[:, cols], qbd, preferred_element_type=jnp.float32) for r in kv_refs]
        top = functools.reduce(jnp.maximum, scores).max(axis=0, keepdims=True)
        expd = [jnp.exp(s - top) for s in scores]
        total = functools.reduce(jnp.add, expd).sum(axis=0, keepdims=True)
        scale = 1.0 / total
        both = None
        for r, e in zip(kv_refs, expd):
            part = lax.dot_general(
                (e * scale).astype(jnp.bfloat16), r[:, vcols], (((0,), (0,)), ((), ())),
                preferred_element_type=jnp.float32,
            )
            both = part if both is None else both + part
        merged = jnp.where(low, both[:BS], both[BS:])
        att_ref[:, cols] = merged.astype(jnp.bfloat16)
    out_ref[...] = jnp.dot(att_ref[...], w_ref[...], preferred_element_type=jnp.float32).astype(
        jnp.bfloat16
    )


def split_queries(queries):
    count = queries.shape[0] // BS
    pairs = HEADS // 2
    qt = queries.reshape(count, BS, pairs, 2 * HD).transpose(0, 2, 3, 1)
    qt = jnp.concatenate([qt, qt], axis=3)
    d_head = lax.broadcasted_iota(jnp.int32, (2 * HD, 2 * BS), 0) // HD
    j_head = lax.broadcasted_iota(jnp.int32, (2 * HD, 2 * BS), 1) // BS
    scale = jnp.asarray(1.0 / HD**0.5, jnp.bfloat16)
    return jnp.where(d_head == j_head, qt * scale, jnp.zeros_like(qt))


def attend(queries, kv_sources, table, out_weight):
    count = table.shape[0]
    pairs = HEADS // 2
    in_specs = [pl.BlockSpec((1, pairs, 2 * HD, 2 * BS), lambda b, t: (b, 0, 0, 0))]
    operands = [split_queries(queries)]
    for j, src in enumerate(kv_sources):
        in_specs.append(pl.BlockSpec((BS, 2 * D), lambda b, t, j=j: (t[b, j], 0)))
        operands.append(src)
    in_specs.append(pl.BlockSpec(out_weight.shape, lambda b, t: (0, 0)))
    operands.append(out_weight)
    grid_spec = pltpu.PrefetchScalarGridSpec(
        num_scalar_prefetch=1,
        grid=(count,),
        in_specs=in_specs,
        out_specs=pl.BlockSpec((BS, D), lambda b, t: (b, 0)),
        scratch_shapes=[pltpu.VMEM((BS, D), jnp.bfloat16)],
    )
    return pl.pallas_call(
        attention_kernel,
        grid_spec=grid_spec,
        out_shape=jax.ShapeDtypeStruct((count * BS, D), jnp.bfloat16),
    )(table, *operands)


def on_device(
    node_feats,
    struct_feats,
    op_blocks,
    laplace_index,
    graph_links,
    expander_slot,
    series_coef,
    encode_weight,
    qkv_weight,
    out_weight,
):
    count = op_blocks.shape[0]
    rows = count * BS
    rim = REACH * BS
    first_block = lax.axis_index("seq") * count
    levels = lax.axis_size("seq").bit_length() - 1
    bits = [link * (levels - 1) // (NEXP - 1) for link in range(NEXP)]

    half = rows // 2
    early = [partner(node_feats[:half], "seq", bit) for bit in bits[2:]]
    encoding, (early,) = chebyshev(
        struct_feats, op_blocks, laplace_index, series_coef, first_block, (), early,
    )
    late = [partner(node_feats[half:], "seq", bit) for bit in bits[2:]]
    near_far = partner(node_feats, "seq", bits[1])
    encoding, late, near_far = lax.optimization_barrier((encoding, late, near_far))
    feats_far = [near_far] + [jnp.concatenate([a, b], axis=0) for a, b in zip(early, late)]
    encoding_b = encoding.astype(jnp.bfloat16)

    enc_far = [partner(encoding_b, "seq", bit) for bit in bits[1:]]

    def blend(feats, enc):
        encoded = jnp.dot(enc, encode_weight, preferred_element_type=jnp.float32)
        return (feats.astype(jnp.float32) + encoded).astype(jnp.bfloat16)

    kv_weight = qkv_weight[:, D:]
    blended = blend(node_feats, encoding_b)
    queries = jnp.dot(blended, qkv_weight[:, :D], preferred_element_type=jnp.float32).astype(
        jnp.bfloat16
    )
    all_blended = jnp.concatenate(
        [shift_rows(blended[rows - rim:], "seq", 1), blended, shift_rows(blended[:rim], "seq", -1)]
        + [blend(f, e) for f, e in zip(feats_far, enc_far)],
        axis=0,
    )
    kv_all = jnp.dot(all_blended, kv_weight, preferred_element_type=jnp.float32).astype(
        jnp.bfloat16
    )
    kv_own = kv_all[rim : rim + rows]
    kv_chip = partner(kv_own, "seq", bits[0])

    near_blocks = count + 2 * REACH
    own_slot = jnp.arange(count, dtype=jnp.int32)[:, None] + REACH
    graph_slot = jnp.clip(graph_links - first_block + REACH, 0, near_blocks - 1)
    far_slot = jnp.clip(expander_slot, 0, count - 1)
    far_base = jnp.asarray([0] + [near_blocks + k * count for k in range(NEXP - 1)], jnp.int32)
    table = jnp.concatenate([own_slot, graph_slot, far_slot + far_base[None, :]], axis=1)
    table = table.astype(jnp.int32)
    sources = [kv_all] * 4 + [kv_chip] + [kv_all] * (NEXP - 1)
    return attend(queries, sources, table, out_weight)


def solution(mesh):
    placed = (
        P(("group", "seq"), None),
        P(("group", "seq"), None),
        P(("group", "seq"), None, None, None),
        P(("group", "seq"), None),
        P(("group", "seq"), None),
        P(("group", "seq"), None),
        P(),
        P(),
        P(),
        P(),
    )
    return jax.shard_map(
        on_device, mesh=mesh, in_specs=placed, out_specs=P(("group", "seq"), None), check_vma=False
    )
```

```python
import functools

import jax
import jax.numpy as jnp
from jax import lax
from jax.experimental import pallas as pl
from jax.experimental.pallas import tpu as pltpu
from jax.sharding import PartitionSpec as P

D = 1024
HEADS = 16
HD = 64
BS = 64
DEG = 8
NEXP = 4
REACH = 2
NKEY = 1 + 3 + NEXP
PER_EXCHANGE = 4


def shift_rows(x, axis, step):
    peers = lax.axis_size(axis)
    if step > 0:
        pairs = [(i, i + step) for i in range(peers - step)]
    else:
        pairs = [(i, i + step) for i in range(-step, peers)]
    return lax.ppermute(x, axis, pairs)


def extended(x, axis, width):
    length = x.shape[0]
    before = shift_rows(x[length - width:], axis, 1)
    after = shift_rows(x[:width], axis, -1)
    return jnp.concatenate([before, x, after], axis=0)


def partner(value, axis, distance):
    mask = 2**distance
    pairs = [(source, source ^ mask) for source in range(lax.axis_size(axis))]
    return lax.ppermute(value, axis, pairs)


def apply_operator(field, op_blocks, laplace_index, first_block):
    count = op_blocks.shape[0]
    padded = extended(field, "seq", REACH * BS)
    pooled = padded.reshape(count + 2 * REACH, BS, field.shape[1])
    position = laplace_index - first_block + REACH
    picked = pooled[position]
    result = jnp.einsum("bjst,bjtc->bsc", op_blocks, picked, precision=lax.Precision.HIGHEST)
    return result.reshape(field.shape)


def chebyshev(struct_feats, op_blocks, laplace_index, series_coef, first_block, riders, later):
    count = op_blocks.shape[0]
    chans = struct_feats.shape[1]
    taps = 2 * REACH + 1
    halo = PER_EXCHANGE * REACH
    block_ids = first_block + jnp.arange(count, dtype=jnp.int32)
    offsets = laplace_index - block_ids[:, None] + REACH
    hit = offsets[:, :, None] == jnp.arange(taps, dtype=jnp.int32)[None, None, :]
    bands = jnp.sum(jnp.where(hit[:, :, :, None, None], op_blocks[:, :, None], 0.0), axis=1)
    bands = bands.transpose(0, 2, 1, 3).reshape(count, BS, taps * BS)
    own_field = struct_feats.reshape(count, BS, chans)
    payload = jnp.concatenate([own_field, bands], axis=2)
    left = shift_rows(payload[count - halo :], "seq", 1)
    right = shift_rows(payload[:halo], "seq", -1)
    edge = halo - REACH
    bands = jnp.concatenate(
        [left[halo - edge :, :, chans:], bands, right[:edge, :, chans:]], axis=0
    )
    field = jnp.concatenate([left[:, :, :chans], own_field, right[:, :, :chans]], axis=0)
    width = field.shape[0]

    def step(values, lo, hi, base):
        stacked = jnp.stack(
            [values[lo - REACH + o - base : hi - REACH + o - base] for o in range(taps)], axis=1
        ).reshape(hi - lo, taps * BS, chans)
        return jnp.einsum(
            "wsk,wkc->wsc", bands[lo - REACH : hi - REACH], stacked,
            precision=lax.Precision.HIGH, preferred_element_type=jnp.float32,
        )

    own = slice(halo, halo + count)
    cur, cur_base = field, 0
    prev, prev_base = None, 0
    encoding = series_coef[0] * field[own]
    for degree in range(1, DEG + 1):
        if degree > 1 and (degree - 1) % PER_EXCHANGE == 0:
            older = prev[own.start - prev_base : own.stop - prev_base]
            packed = jnp.concatenate([older, cur], axis=2)
            left = shift_rows(packed[count - halo :], "seq", 1)
            right = shift_rows(packed[:halo], "seq", -1)
            if later is not None:
                left, right, later = lax.optimization_barrier((left, right, later))
                riders = riders + (later,)
                later = None
            prev = jnp.concatenate(
                [left[halo - edge :, :, :chans], older, right[:edge, :, :chans]], axis=0
            )
            prev_base = REACH
            cur = jnp.concatenate([left[:, :, chans:], cur, right[:, :, chans:]], axis=0)
            cur_base = 0
            lo, hi = 0, width
        if degree == 1 or (degree - 1) % PER_EXCHANGE == 0:
            lo, hi = REACH, width - REACH
        else:
            lo, hi = lo + REACH, hi - REACH
        applied = step(cur, lo, hi, cur_base)
        if degree == 1:
            nxt = applied
        else:
            nxt = 2.0 * applied - prev[lo - prev_base : hi - prev_base]
        encoding = encoding + series_coef[degree] * nxt[own.start - lo : own.stop - lo]
        prev, prev_base = cur, cur_base
        cur, cur_base = nxt, lo
    return encoding.reshape(count * BS, chans), riders


def attention_kernel(table_ref, q_ref, *refs):
    kv_refs = refs[:NKEY]
    w_ref, out_ref, att_ref = refs[NKEY:]
    lane = lax.broadcasted_iota(jnp.int32, (1, 2 * HD), 1)
    low = lane < HD
    for pair in range(HEADS // 2):
        cols = slice(pair * 2 * HD, (pair + 1) * 2 * HD)
        vcols = slice(D + pair * 2 * HD, D + (pair + 1) * 2 * HD)
        ks = jnp.concatenate([r[:, cols] for r in kv_refs], axis=0)
        vs = jnp.concatenate([r[:, vcols] for r in kv_refs], axis=0)
        scores = jnp.dot(ks, q_ref[0, pair], preferred_element_type=jnp.float32)
        top = jnp.max(scores, axis=0, keepdims=True)
        expd = jnp.exp(scores - top)
        total = jnp.sum(expd, axis=0, keepdims=True)
        weights = (expd * (1.0 / total)).astype(jnp.bfloat16)
        both = lax.dot_general(
            weights, vs, (((0,), (0,)), ((), ())), preferred_element_type=jnp.float32
        )
        merged = jnp.where(low, both[:BS], both[BS:])
        att_ref[:, cols] = merged.astype(jnp.bfloat16)
    out_ref[...] = jnp.dot(att_ref[...], w_ref[...], preferred_element_type=jnp.float32).astype(
        jnp.bfloat16
    )


def split_queries(queries):
    count = queries.shape[0] // BS
    pairs = HEADS // 2
    qt = queries.reshape(count, BS, pairs, 2 * HD).transpose(0, 2, 3, 1)
    qt = jnp.concatenate([qt, qt], axis=3)
    d_head = lax.broadcasted_iota(jnp.int32, (2 * HD, 2 * BS), 0) // HD
    j_head = lax.broadcasted_iota(jnp.int32, (2 * HD, 2 * BS), 1) // BS
    scale = jnp.asarray(1.0 / HD**0.5, jnp.bfloat16)
    return jnp.where(d_head == j_head, qt * scale, jnp.zeros_like(qt))


def attend(queries, kv_sources, table, out_weight):
    count = table.shape[0]
    pairs = HEADS // 2
    in_specs = [pl.BlockSpec((1, pairs, 2 * HD, 2 * BS), lambda b, t: (b, 0, 0, 0))]
    operands = [split_queries(queries)]
    for j, src in enumerate(kv_sources):
        in_specs.append(pl.BlockSpec((BS, 2 * D), lambda b, t, j=j: (t[b, j], 0)))
        operands.append(src)
    in_specs.append(pl.BlockSpec(out_weight.shape, lambda b, t: (0, 0)))
    operands.append(out_weight)
    grid_spec = pltpu.PrefetchScalarGridSpec(
        num_scalar_prefetch=1,
        grid=(count,),
        in_specs=in_specs,
        out_specs=pl.BlockSpec((BS, D), lambda b, t: (b, 0)),
        scratch_shapes=[pltpu.VMEM((BS, D), jnp.bfloat16)],
    )
    return pl.pallas_call(
        attention_kernel,
        grid_spec=grid_spec,
        out_shape=jax.ShapeDtypeStruct((count * BS, D), jnp.bfloat16),
    )(table, *operands)


def on_device(
    node_feats,
    struct_feats,
    op_blocks,
    laplace_index,
    graph_links,
    expander_slot,
    series_coef,
    encode_weight,
    qkv_weight,
    out_weight,
):
    count = op_blocks.shape[0]
    rows = count * BS
    rim = REACH * BS
    first_block = lax.axis_index("seq") * count
    levels = lax.axis_size("seq").bit_length() - 1
    bits = [link * (levels - 1) // (NEXP - 1) for link in range(NEXP)]

    half = rows // 2
    early = [partner(node_feats[:half], "seq", bit) for bit in bits[2:]]
    encoding, (early,) = chebyshev(
        struct_feats, op_blocks, laplace_index, series_coef, first_block, (), early,
    )
    late = [partner(node_feats[half:], "seq", bit) for bit in bits[2:]]
    near_far = partner(node_feats, "seq", bits[1])
    encoding, late, near_far = lax.optimization_barrier((encoding, late, near_far))
    feats_far = [near_far] + [jnp.concatenate([a, b], axis=0) for a, b in zip(early, late)]
    encoding_b = encoding.astype(jnp.bfloat16)

    enc_far = [partner(encoding_b, "seq", bit) for bit in bits[1:]]

    def blend(feats, enc):
        encoded = jnp.dot(enc, encode_weight, preferred_element_type=jnp.float32)
        return (feats.astype(jnp.float32) + encoded).astype(jnp.bfloat16)

    kv_weight = qkv_weight[:, D:]
    blended = blend(node_feats, encoding_b)
    queries = jnp.dot(blended, qkv_weight[:, :D], preferred_element_type=jnp.float32).astype(
        jnp.bfloat16
    )
    all_blended = jnp.concatenate(
        [shift_rows(blended[rows - rim:], "seq", 1), blended, shift_rows(blended[:rim], "seq", -1)]
        + [partner(blended, "seq", bits[0])]
        + [blend(f, e) for f, e in zip(feats_far, enc_far)],
        axis=0,
    )
    kv_all = jnp.dot(all_blended, kv_weight, preferred_element_type=jnp.float32).astype(
        jnp.bfloat16
    )

    near_blocks = count + 2 * REACH
    own_slot = jnp.arange(count, dtype=jnp.int32)[:, None] + REACH
    graph_slot = jnp.clip(graph_links - first_block + REACH, 0, near_blocks - 1)
    far_slot = jnp.clip(expander_slot, 0, count - 1)
    far_base = jnp.asarray([near_blocks + k * count for k in range(NEXP)], jnp.int32)
    table = jnp.concatenate([own_slot, graph_slot, far_slot + far_base[None, :]], axis=1)
    table = table.astype(jnp.int32)
    sources = [kv_all] * NKEY
    return attend(queries, sources, table, out_weight)


def solution(mesh):
    placed = (
        P(("group", "seq"), None),
        P(("group", "seq"), None),
        P(("group", "seq"), None, None, None),
        P(("group", "seq"), None),
        P(("group", "seq"), None),
        P(("group", "seq"), None),
        P(),
        P(),
        P(),
        P(),
    )
    return jax.shard_map(
        on_device, mesh=mesh, in_specs=placed, out_specs=P(("group", "seq"), None), check_vma=False
    )
```

```python
import functools

import jax
import jax.numpy as jnp
from jax import lax
from jax.experimental import pallas as pl
from jax.experimental.pallas import tpu as pltpu
from jax.sharding import PartitionSpec as P

D = 1024
HEADS = 16
HD = 64
BS = 64
DEG = 8
NEXP = 4
REACH = 2
NKEY = 1 + 3 + NEXP
PER_EXCHANGE = 4


def shift_rows(x, axis, step):
    peers = lax.axis_size(axis)
    if step > 0:
        pairs = [(i, i + step) for i in range(peers - step)]
    else:
        pairs = [(i, i + step) for i in range(-step, peers)]
    return lax.ppermute(x, axis, pairs)


def extended(x, axis, width):
    length = x.shape[0]
    before = shift_rows(x[length - width:], axis, 1)
    after = shift_rows(x[:width], axis, -1)
    return jnp.concatenate([before, x, after], axis=0)


def partner(value, axis, distance):
    mask = 2**distance
    pairs = [(source, source ^ mask) for source in range(lax.axis_size(axis))]
    return lax.ppermute(value, axis, pairs)


def apply_operator(field, op_blocks, laplace_index, first_block):
    count = op_blocks.shape[0]
    padded = extended(field, "seq", REACH * BS)
    pooled = padded.reshape(count + 2 * REACH, BS, field.shape[1])
    position = laplace_index - first_block + REACH
    picked = pooled[position]
    result = jnp.einsum("bjst,bjtc->bsc", op_blocks, picked, precision=lax.Precision.HIGHEST)
    return result.reshape(field.shape)


def chebyshev(struct_feats, op_blocks, laplace_index, series_coef, first_block, riders, later):
    count = op_blocks.shape[0]
    chans = struct_feats.shape[1]
    taps = 2 * REACH + 1
    halo = PER_EXCHANGE * REACH
    block_ids = first_block + jnp.arange(count, dtype=jnp.int32)
    offsets = laplace_index - block_ids[:, None] + REACH
    hit = offsets[:, :, None] == jnp.arange(taps, dtype=jnp.int32)[None, None, :]
    bands = jnp.sum(jnp.where(hit[:, :, :, None, None], op_blocks[:, :, None], 0.0), axis=1)
    bands = bands.transpose(0, 2, 1, 3).reshape(count, BS, taps * BS)
    own_field = struct_feats.reshape(count, BS, chans)
    payload = jnp.concatenate([own_field, bands], axis=2)
    left = shift_rows(payload[count - halo :], "seq", 1)
    right = shift_rows(payload[:halo], "seq", -1)
    edge = halo - REACH
    bands = jnp.concatenate(
        [left[halo - edge :, :, chans:], bands, right[:edge, :, chans:]], axis=0
    )
    field = jnp.concatenate([left[:, :, :chans], own_field, right[:, :, :chans]], axis=0)
    width = field.shape[0]

    def step(values, lo, hi, base):
        stacked = jnp.stack(
            [values[lo - REACH + o - base : hi - REACH + o - base] for o in range(taps)], axis=1
        ).reshape(hi - lo, taps * BS, chans)
        return jnp.einsum(
            "wsk,wkc->wsc", bands[lo - REACH : hi - REACH], stacked,
            precision=lax.Precision.HIGH, preferred_element_type=jnp.float32,
        )

    own = slice(halo, halo + count)
    cur, cur_base = field, 0
    prev, prev_base = None, 0
    encoding = series_coef[0] * field[own]
    for degree in range(1, DEG + 1):
        if degree > 1 and (degree - 1) % PER_EXCHANGE == 0:
            older = prev[own.start - prev_base : own.stop - prev_base]
            packed = jnp.concatenate([older, cur], axis=2)
            left = shift_rows(packed[count - halo :], "seq", 1)
            right = shift_rows(packed[:halo], "seq", -1)
            if later is not None:
                left, right, later = lax.optimization_barrier((left, right, later))
                riders = riders + (later,)
                later = None
            prev = jnp.concatenate(
                [left[halo - edge :, :, :chans], older, right[:edge, :, :chans]], axis=0
            )
            prev_base = REACH
            cur = jnp.concatenate([left[:, :, chans:], cur, right[:, :, chans:]], axis=0)
            cur_base = 0
            lo, hi = 0, width
        if degree == 1 or (degree - 1) % PER_EXCHANGE == 0:
            lo, hi = REACH, width - REACH
        else:
            lo, hi = lo + REACH, hi - REACH
        applied = step(cur, lo, hi, cur_base)
        if degree == 1:
            nxt = applied
        else:
            nxt = 2.0 * applied - prev[lo - prev_base : hi - prev_base]
        encoding = encoding + series_coef[degree] * nxt[own.start - lo : own.stop - lo]
        prev, prev_base = cur, cur_base
        cur, cur_base = nxt, lo
    return encoding.reshape(count * BS, chans), riders


def attention_kernel(table_ref, q_ref, *refs):
    kv_refs = refs[:NKEY]
    w_ref, out_ref, att_ref = refs[NKEY:]
    lane = lax.broadcasted_iota(jnp.int32, (1, 2 * HD), 1)
    low = lane < HD
    first = (pl.program_id(0) % 2) == 0
    d_head = lax.broadcasted_iota(jnp.int32, (2 * HD, 2 * BS), 0) // HD
    j_head = lax.broadcasted_iota(jnp.int32, (2 * HD, 2 * BS), 1) // BS
    same = d_head == j_head
    for pair in range(HEADS // 2):
        cols = slice(pair * 2 * HD, (pair + 1) * 2 * HD)
        vcols = slice(D + pair * 2 * HD, D + (pair + 1) * 2 * HD)
        ks = jnp.concatenate([r[:, cols] for r in kv_refs], axis=0)
        vs = jnp.concatenate([r[:, vcols] for r in kv_refs], axis=0)
        tile = q_ref[cols, :].astype(jnp.float32)
        turned = pltpu.roll(tile, BS, 1)
        spread = jnp.where(low == first, tile, turned)
        qbd = jnp.where(same, spread, 0.0).astype(jnp.bfloat16)
        scores = jnp.dot(ks, qbd, preferred_element_type=jnp.float32)
        top = jnp.max(scores, axis=0, keepdims=True)
        expd = jnp.exp(scores - top)
        total = jnp.sum(expd, axis=0, keepdims=True)
        weights = (expd * (1.0 / total)).astype(jnp.bfloat16)
        both = lax.dot_general(
            weights, vs, (((0,), (0,)), ((), ())), preferred_element_type=jnp.float32
        )
        merged = jnp.where(low, both[:BS], both[BS:])
        att_ref[:, cols] = merged.astype(jnp.bfloat16)
    out_ref[...] = jnp.dot(att_ref[...], w_ref[...], preferred_element_type=jnp.float32).astype(
        jnp.bfloat16
    )


def attend(queries, kv_sources, table, out_weight):
    count = table.shape[0]
    pairs = HEADS // 2
    in_specs = [pl.BlockSpec((D, 2 * BS), lambda b, t: (0, b // 2))]
    operands = [queries]
    for j, src in enumerate(kv_sources):
        in_specs.append(pl.BlockSpec((BS, 2 * D), lambda b, t, j=j: (t[b, j], 0)))
        operands.append(src)
    in_specs.append(pl.BlockSpec(out_weight.shape, lambda b, t: (0, 0)))
    operands.append(out_weight)
    grid_spec = pltpu.PrefetchScalarGridSpec(
        num_scalar_prefetch=1,
        grid=(count,),
        in_specs=in_specs,
        out_specs=pl.BlockSpec((BS, D), lambda b, t: (b, 0)),
        scratch_shapes=[pltpu.VMEM((BS, D), jnp.bfloat16)],
    )
    return pl.pallas_call(
        attention_kernel,
        grid_spec=grid_spec,
        out_shape=jax.ShapeDtypeStruct((count * BS, D), jnp.bfloat16),
    )(table, *operands)


def on_device(
    node_feats,
    struct_feats,
    op_blocks,
    laplace_index,
    graph_links,
    expander_slot,
    series_coef,
    encode_weight,
    qkv_weight,
    out_weight,
):
    count = op_blocks.shape[0]
    rows = count * BS
    rim = REACH * BS
    first_block = lax.axis_index("seq") * count
    levels = lax.axis_size("seq").bit_length() - 1
    bits = [link * (levels - 1) // (NEXP - 1) for link in range(NEXP)]

    half = rows // 2
    early = [partner(node_feats[:half], "seq", bit) for bit in bits[2:]]
    encoding, (early,) = chebyshev(
        struct_feats, op_blocks, laplace_index, series_coef, first_block, (), early,
    )
    late = [partner(node_feats[half:], "seq", bit) for bit in bits[2:]]
    near_far = partner(node_feats, "seq", bits[1])
    encoding, late, near_far = lax.optimization_barrier((encoding, late, near_far))
    feats_far = [near_far] + [jnp.concatenate([a, b], axis=0) for a, b in zip(early, late)]
    encoding_b = encoding.astype(jnp.bfloat16)

    enc_far = [partner(encoding_b, "seq", bit) for bit in bits[1:]]

    def blend(feats, enc):
        encoded = jnp.dot(enc, encode_weight, preferred_element_type=jnp.float32)
        return (feats.astype(jnp.float32) + encoded).astype(jnp.bfloat16)

    kv_weight = qkv_weight[:, D:]
    blended = blend(node_feats, encoding_b)
    queries = lax.dot_general(
        qkv_weight[:, :D], blended, (((0,), (1,)), ((), ())), preferred_element_type=jnp.float32
    ).astype(jnp.bfloat16) * jnp.asarray(1.0 / HD**0.5, jnp.bfloat16)
    all_blended = jnp.concatenate(
        [shift_rows(blended[rows - rim:], "seq", 1), blended, shift_rows(blended[:rim], "seq", -1)]
        + [blend(f, e) for f, e in zip(feats_far, enc_far)],
        axis=0,
    )
    kv_all = jnp.dot(all_blended, kv_weight, preferred_element_type=jnp.float32).astype(
        jnp.bfloat16
    )
    kv_own = kv_all[rim : rim + rows]
    kv_chip = partner(kv_own, "seq", bits[0])

    near_blocks = count + 2 * REACH
    own_slot = jnp.arange(count, dtype=jnp.int32)[:, None] + REACH
    graph_slot = jnp.clip(graph_links - first_block + REACH, 0, near_blocks - 1)
    far_slot = jnp.clip(expander_slot, 0, count - 1)
    far_base = jnp.asarray([0] + [near_blocks + k * count for k in range(NEXP - 1)], jnp.int32)
    table = jnp.concatenate([own_slot, graph_slot, far_slot + far_base[None, :]], axis=1)
    table = table.astype(jnp.int32)
    sources = [kv_all] * 4 + [kv_chip] + [kv_all] * (NEXP - 1)
    return attend(queries, sources, table, out_weight)


def solution(mesh):
    placed = (
        P(("group", "seq"), None),
        P(("group", "seq"), None),
        P(("group", "seq"), None, None, None),
        P(("group", "seq"), None),
        P(("group", "seq"), None),
        P(("group", "seq"), None),
        P(),
        P(),
        P(),
        P(),
    )
    return jax.shard_map(
        on_device, mesh=mesh, in_specs=placed, out_specs=P(("group", "seq"), None), check_vma=False
    )
```

```python
import functools

import jax
import jax.numpy as jnp
from jax import lax
from jax.experimental import pallas as pl
from jax.experimental.pallas import tpu as pltpu
from jax.sharding import PartitionSpec as P

D = 1024
HEADS = 16
HD = 64
BS = 64
DEG = 8
NEXP = 4
REACH = 2
NKEY = 1 + 3 + NEXP
PER_EXCHANGE = 4


def shift_rows(x, axis, step):
    peers = lax.axis_size(axis)
    if step > 0:
        pairs = [(i, i + step) for i in range(peers - step)]
    else:
        pairs = [(i, i + step) for i in range(-step, peers)]
    return lax.ppermute(x, axis, pairs)


def extended(x, axis, width):
    length = x.shape[0]
    before = shift_rows(x[length - width:], axis, 1)
    after = shift_rows(x[:width], axis, -1)
    return jnp.concatenate([before, x, after], axis=0)


def partner(value, axis, distance):
    mask = 2**distance
    pairs = [(source, source ^ mask) for source in range(lax.axis_size(axis))]
    return lax.ppermute(value, axis, pairs)


def apply_operator(field, op_blocks, laplace_index, first_block):
    count = op_blocks.shape[0]
    padded = extended(field, "seq", REACH * BS)
    pooled = padded.reshape(count + 2 * REACH, BS, field.shape[1])
    position = laplace_index - first_block + REACH
    picked = pooled[position]
    result = jnp.einsum("bjst,bjtc->bsc", op_blocks, picked, precision=lax.Precision.HIGHEST)
    return result.reshape(field.shape)


def chebyshev(struct_feats, op_blocks, laplace_index, series_coef, first_block, riders, later):
    count = op_blocks.shape[0]
    chans = struct_feats.shape[1]
    taps = 2 * REACH + 1
    halo = PER_EXCHANGE * REACH
    block_ids = first_block + jnp.arange(count, dtype=jnp.int32)
    offsets = laplace_index - block_ids[:, None] + REACH
    hit = offsets[:, :, None] == jnp.arange(taps, dtype=jnp.int32)[None, None, :]
    bands = jnp.sum(jnp.where(hit[:, :, :, None, None], op_blocks[:, :, None], 0.0), axis=1)
    bands = bands.transpose(0, 2, 1, 3).reshape(count, BS, taps * BS)
    own_field = struct_feats.reshape(count, BS, chans)
    payload = jnp.concatenate([own_field, bands], axis=2)
    left = shift_rows(payload[count - halo :], "seq", 1)
    right = shift_rows(payload[:halo], "seq", -1)
    edge = halo - REACH
    bands = jnp.concatenate(
        [left[halo - edge :, :, chans:], bands, right[:edge, :, chans:]], axis=0
    )
    field = jnp.concatenate([left[:, :, :chans], own_field, right[:, :, :chans]], axis=0)
    width = field.shape[0]

    def step(values, lo, hi, base):
        stacked = jnp.stack(
            [values[lo - REACH + o - base : hi - REACH + o - base] for o in range(taps)], axis=1
        ).reshape(hi - lo, taps * BS, chans)
        return jnp.einsum(
            "wsk,wkc->wsc", bands[lo - REACH : hi - REACH], stacked,
            precision=lax.Precision.HIGH, preferred_element_type=jnp.float32,
        )

    own = slice(halo, halo + count)
    cur, cur_base = field, 0
    prev, prev_base = None, 0
    encoding = series_coef[0] * field[own]
    for degree in range(1, DEG + 1):
        if degree > 1 and (degree - 1) % PER_EXCHANGE == 0:
            older = prev[own.start - prev_base : own.stop - prev_base]
            packed = jnp.concatenate([older, cur], axis=2)
            left = shift_rows(packed[count - halo :], "seq", 1)
            right = shift_rows(packed[:halo], "seq", -1)
            if later is not None:
                left, right, later = lax.optimization_barrier((left, right, later))
                riders = riders + (later,)
                later = None
            prev = jnp.concatenate(
                [left[halo - edge :, :, :chans], older, right[:edge, :, :chans]], axis=0
            )
            prev_base = REACH
            cur = jnp.concatenate([left[:, :, chans:], cur, right[:, :, chans:]], axis=0)
            cur_base = 0
            lo, hi = 0, width
        if degree == 1 or (degree - 1) % PER_EXCHANGE == 0:
            lo, hi = REACH, width - REACH
        else:
            lo, hi = lo + REACH, hi - REACH
        applied = step(cur, lo, hi, cur_base)
        if degree == 1:
            nxt = applied
        else:
            nxt = 2.0 * applied - prev[lo - prev_base : hi - prev_base]
        encoding = encoding + series_coef[degree] * nxt[own.start - lo : own.stop - lo]
        prev, prev_base = cur, cur_base
        cur, cur_base = nxt, lo
    return encoding.reshape(count * BS, chans), riders


def attention_kernel(table_ref, q_ref, *refs):
    kv_refs = refs[:NKEY]
    w_ref, out_ref, att_ref = refs[NKEY:]
    lane = lax.broadcasted_iota(jnp.int32, (1, 2 * HD), 1)
    low = lane < HD
    first = (pl.program_id(0) % 2) == 0
    d_head = lax.broadcasted_iota(jnp.int32, (2 * HD, 2 * BS), 0) // HD
    j_head = lax.broadcasted_iota(jnp.int32, (2 * HD, 2 * BS), 1) // BS
    same = d_head == j_head
    for pair in range(HEADS // 2):
        cols = slice(pair * 2 * HD, (pair + 1) * 2 * HD)
        vcols = slice(D + pair * 2 * HD, D + (pair + 1) * 2 * HD)
        ks = jnp.concatenate([r[:, cols] for r in kv_refs], axis=0)
        vs = jnp.concatenate([r[:, vcols] for r in kv_refs], axis=0)
        tile = q_ref[cols, :].astype(jnp.float32)
        turned = pltpu.roll(tile, BS, 1)
        spread = jnp.where(low == first, tile, turned)
        qbd = jnp.where(same, spread, 0.0).astype(jnp.bfloat16)
        scores = jnp.dot(ks, qbd, preferred_element_type=jnp.float32)
        top = jnp.max(scores, axis=0, keepdims=True)
        expd = jnp.exp(scores - top)
        total = jnp.sum(expd, axis=0, keepdims=True)
        weights = (expd * (1.0 / total)).astype(jnp.bfloat16)
        both = lax.dot_general(
            weights, vs, (((0,), (0,)), ((), ())), preferred_element_type=jnp.float32
        )
        merged = jnp.where(low, both[:BS], both[BS:])
        att_ref[:, cols] = merged.astype(jnp.bfloat16)
    out_ref[...] = jnp.dot(att_ref[...], w_ref[...], preferred_element_type=jnp.float32).astype(
        jnp.bfloat16
    )


def attend(queries, kv_sources, table, out_weight):
    count = table.shape[0]
    pairs = HEADS // 2
    in_specs = [pl.BlockSpec((D, 2 * BS), lambda b, t: (0, b // 2))]
    operands = [queries]
    for j, src in enumerate(kv_sources):
        in_specs.append(pl.BlockSpec((BS, 2 * D), lambda b, t, j=j: (t[b, j], 0)))
        operands.append(src)
    in_specs.append(pl.BlockSpec(out_weight.shape, lambda b, t: (0, 0)))
    operands.append(out_weight)
    grid_spec = pltpu.PrefetchScalarGridSpec(
        num_scalar_prefetch=1,
        grid=(count,),
        in_specs=in_specs,
        out_specs=pl.BlockSpec((BS, D), lambda b, t: (b, 0)),
        scratch_shapes=[pltpu.VMEM((BS, D), jnp.bfloat16)],
    )
    return pl.pallas_call(
        attention_kernel,
        grid_spec=grid_spec,
        out_shape=jax.ShapeDtypeStruct((count * BS, D), jnp.bfloat16),
    )(table, *operands)


def on_device(
    node_feats,
    struct_feats,
    op_blocks,
    laplace_index,
    graph_links,
    expander_slot,
    series_coef,
    encode_weight,
    qkv_weight,
    out_weight,
):
    count = op_blocks.shape[0]
    rows = count * BS
    rim = REACH * BS
    first_block = lax.axis_index("seq") * count
    levels = lax.axis_size("seq").bit_length() - 1
    bits = [link * (levels - 1) // (NEXP - 1) for link in range(NEXP)]

    half = rows // 2
    early = [partner(node_feats[:half], "seq", bit) for bit in bits[2:]]
    encoding, (early,) = chebyshev(
        struct_feats, op_blocks, laplace_index, series_coef, first_block, (), early,
    )
    late = [partner(node_feats[half:], "seq", bit) for bit in bits[2:]]
    near_far = partner(node_feats, "seq", bits[1])
    encoding, late, near_far = lax.optimization_barrier((encoding, late, near_far))
    feats_far = [near_far] + [jnp.concatenate([a, b], axis=0) for a, b in zip(early, late)]
    encoding_b = encoding.astype(jnp.bfloat16)

    enc_far = [partner(encoding_b, "seq", bit) for bit in bits[1:]]

    def blend(feats, enc):
        encoded = jnp.dot(enc, encode_weight, preferred_element_type=jnp.float32)
        return (feats.astype(jnp.float32) + encoded).astype(jnp.bfloat16)

    kv_weight = qkv_weight[:, D:]
    blended = blend(node_feats, encoding_b)
    queries = lax.dot_general(
        qkv_weight[:, :D], blended, (((0,), (1,)), ((), ())), preferred_element_type=jnp.float32
    ).astype(jnp.bfloat16) * jnp.asarray(1.0 / HD**0.5, jnp.bfloat16)
    near_blended = jnp.concatenate(
        [shift_rows(blended[rows - rim:], "seq", 1), blended, shift_rows(blended[:rim], "seq", -1)],
        axis=0,
    )
    far_blended = jnp.concatenate([blend(f, e) for f, e in zip(feats_far, enc_far)], axis=0)
    kv_near = jnp.dot(near_blended, kv_weight, preferred_element_type=jnp.float32).astype(
        jnp.bfloat16
    )
    kv_own = kv_near[rim : rim + rows]
    kv_chip = partner(kv_own, "seq", bits[0])
    kv_far = jnp.dot(far_blended, kv_weight, preferred_element_type=jnp.float32).astype(
        jnp.bfloat16
    )

    near_blocks = count + 2 * REACH
    own_slot = jnp.arange(count, dtype=jnp.int32)[:, None] + REACH
    graph_slot = jnp.clip(graph_links - first_block + REACH, 0, near_blocks - 1)
    far_slot = jnp.clip(expander_slot, 0, count - 1)
    far_base = jnp.asarray([k * count for k in range(NEXP)], jnp.int32) - count
    far_base = jnp.maximum(far_base, 0)
    table = jnp.concatenate([own_slot, graph_slot, far_slot + far_base[None, :]], axis=1)
    table = table.astype(jnp.int32)
    sources = [kv_near] * 4 + [kv_chip] + [kv_far] * (NEXP - 1)
    return attend(queries, sources, table, out_weight)


def solution(mesh):
    placed = (
        P(("group", "seq"), None),
        P(("group", "seq"), None),
        P(("group", "seq"), None, None, None),
        P(("group", "seq"), None),
        P(("group", "seq"), None),
        P(("group", "seq"), None),
        P(),
        P(),
        P(),
        P(),
    )
    return jax.shard_map(
        on_device, mesh=mesh, in_specs=placed, out_specs=P(("group", "seq"), None), check_vma=False
    )
```

```python
import functools

import jax
import jax.numpy as jnp
from jax import lax
from jax.experimental import pallas as pl
from jax.experimental.pallas import tpu as pltpu
from jax.sharding import PartitionSpec as P

D = 1024
HEADS = 16
HD = 64
BS = 64
DEG = 8
NEXP = 4
REACH = 2
NKEY = 1 + 3 + NEXP
PER_EXCHANGE = 4


def shift_rows(x, axis, step):
    peers = lax.axis_size(axis)
    if step > 0:
        pairs = [(i, i + step) for i in range(peers - step)]
    else:
        pairs = [(i, i + step) for i in range(-step, peers)]
    return lax.ppermute(x, axis, pairs)


def extended(x, axis, width):
    length = x.shape[0]
    before = shift_rows(x[length - width:], axis, 1)
    after = shift_rows(x[:width], axis, -1)
    return jnp.concatenate([before, x, after], axis=0)


def partner(value, axis, distance):
    mask = 2**distance
    pairs = [(source, source ^ mask) for source in range(lax.axis_size(axis))]
    return lax.ppermute(value, axis, pairs)


def apply_operator(field, op_blocks, laplace_index, first_block):
    count = op_blocks.shape[0]
    padded = extended(field, "seq", REACH * BS)
    pooled = padded.reshape(count + 2 * REACH, BS, field.shape[1])
    position = laplace_index - first_block + REACH
    picked = pooled[position]
    result = jnp.einsum("bjst,bjtc->bsc", op_blocks, picked, precision=lax.Precision.HIGHEST)
    return result.reshape(field.shape)


def chebyshev(struct_feats, op_blocks, laplace_index, series_coef, first_block, riders, later):
    count = op_blocks.shape[0]
    chans = struct_feats.shape[1]
    taps = 2 * REACH + 1
    halo = PER_EXCHANGE * REACH
    block_ids = first_block + jnp.arange(count, dtype=jnp.int32)
    offsets = laplace_index - block_ids[:, None] + REACH
    hit = offsets[:, :, None] == jnp.arange(taps, dtype=jnp.int32)[None, None, :]
    bands = jnp.sum(jnp.where(hit[:, :, :, None, None], op_blocks[:, :, None], 0.0), axis=1)
    bands = bands.transpose(0, 2, 1, 3).reshape(count, BS, taps * BS)
    own_field = struct_feats.reshape(count, BS, chans)
    payload = jnp.concatenate([own_field, bands], axis=2)
    left = shift_rows(payload[count - halo :], "seq", 1)
    right = shift_rows(payload[:halo], "seq", -1)
    edge = halo - REACH
    bands = jnp.concatenate(
        [left[halo - edge :, :, chans:], bands, right[:edge, :, chans:]], axis=0
    )
    field = jnp.concatenate([left[:, :, :chans], own_field, right[:, :, :chans]], axis=0)
    width = field.shape[0]

    def step(values, lo, hi, base):
        stacked = jnp.stack(
            [values[lo - REACH + o - base : hi - REACH + o - base] for o in range(taps)], axis=1
        ).reshape(hi - lo, taps * BS, chans)
        return jnp.einsum(
            "wsk,wkc->wsc", bands[lo - REACH : hi - REACH], stacked,
            precision=lax.Precision.HIGH, preferred_element_type=jnp.float32,
        )

    own = slice(halo, halo + count)
    cur, cur_base = field, 0
    prev, prev_base = None, 0
    encoding = series_coef[0] * field[own]
    for degree in range(1, DEG + 1):
        if degree > 1 and (degree - 1) % PER_EXCHANGE == 0:
            older = prev[own.start - prev_base : own.stop - prev_base]
            packed = jnp.concatenate([older, cur], axis=2)
            left = shift_rows(packed[count - halo :], "seq", 1)
            right = shift_rows(packed[:halo], "seq", -1)
            if later is not None:
                left, right, later = lax.optimization_barrier((left, right, later))
                riders = riders + (later,)
                later = None
            prev = jnp.concatenate(
                [left[halo - edge :, :, :chans], older, right[:edge, :, :chans]], axis=0
            )
            prev_base = REACH
            cur = jnp.concatenate([left[:, :, chans:], cur, right[:, :, chans:]], axis=0)
            cur_base = 0
            lo, hi = 0, width
        if degree == 1 or (degree - 1) % PER_EXCHANGE == 0:
            lo, hi = REACH, width - REACH
        else:
            lo, hi = lo + REACH, hi - REACH
        applied = step(cur, lo, hi, cur_base)
        if degree == 1:
            nxt = applied
        else:
            nxt = 2.0 * applied - prev[lo - prev_base : hi - prev_base]
        encoding = encoding + series_coef[degree] * nxt[own.start - lo : own.stop - lo]
        prev, prev_base = cur, cur_base
        cur, cur_base = nxt, lo
    return encoding.reshape(count * BS, chans), riders


def attention_kernel(table_ref, q_ref, *refs):
    kv_refs = refs[:NKEY]
    w_ref, out_ref, att_ref = refs[NKEY:]
    lane = lax.broadcasted_iota(jnp.int32, (1, 2 * HD), 1)
    low = lane < HD
    first = (pl.program_id(0) % 2) == 0
    d_head = lax.broadcasted_iota(jnp.int32, (2 * HD, 2 * BS), 0) // HD
    j_head = lax.broadcasted_iota(jnp.int32, (2 * HD, 2 * BS), 1) // BS
    same = d_head == j_head
    for pair in range(HEADS // 2):
        cols = slice(pair * 2 * HD, (pair + 1) * 2 * HD)
        vcols = slice(D + pair * 2 * HD, D + (pair + 1) * 2 * HD)
        ks = jnp.concatenate([r[:, cols] for r in kv_refs], axis=0)
        vs = jnp.concatenate([r[:, vcols] for r in kv_refs], axis=0)
        tile = q_ref[cols, :].astype(jnp.float32)
        turned = pltpu.roll(tile, BS, 1)
        spread = jnp.where(low == first, tile, turned)
        qbd = jnp.where(same, spread, 0.0).astype(jnp.bfloat16)
        scores = jnp.dot(ks, qbd, preferred_element_type=jnp.float32)
        top = jnp.max(scores, axis=0, keepdims=True)
        expd = jnp.exp(scores - top)
        total = jnp.sum(expd, axis=0, keepdims=True)
        weights = (expd * (1.0 / total)).astype(jnp.bfloat16)
        both = lax.dot_general(
            weights, vs, (((0,), (0,)), ((), ())), preferred_element_type=jnp.float32
        )
        merged = jnp.where(low, both[:BS], both[BS:])
        att_ref[:, cols] = merged.astype(jnp.bfloat16)
    out_ref[...] = jnp.dot(att_ref[...], w_ref[...], preferred_element_type=jnp.float32).astype(
        jnp.bfloat16
    )


def attend(queries, kv_sources, table, out_weight):
    count = table.shape[0]
    pairs = HEADS // 2
    in_specs = [pl.BlockSpec((D, 2 * BS), lambda b, t: (0, b // 2))]
    operands = [queries]
    for j, src in enumerate(kv_sources):
        in_specs.append(pl.BlockSpec((BS, 2 * D), lambda b, t, j=j: (t[b, j], 0)))
        operands.append(src)
    in_specs.append(pl.BlockSpec(out_weight.shape, lambda b, t: (0, 0)))
    operands.append(out_weight)
    grid_spec = pltpu.PrefetchScalarGridSpec(
        num_scalar_prefetch=1,
        grid=(count,),
        in_specs=in_specs,
        out_specs=pl.BlockSpec((BS, D), lambda b, t: (b, 0)),
        scratch_shapes=[pltpu.VMEM((BS, D), jnp.bfloat16)],
    )
    return pl.pallas_call(
        attention_kernel,
        grid_spec=grid_spec,
        out_shape=jax.ShapeDtypeStruct((count * BS, D), jnp.bfloat16),
    )(table, *operands)


def on_device(
    node_feats,
    struct_feats,
    op_blocks,
    laplace_index,
    graph_links,
    expander_slot,
    series_coef,
    encode_weight,
    qkv_weight,
    out_weight,
):
    count = op_blocks.shape[0]
    rows = count * BS
    rim = REACH * BS
    first_block = lax.axis_index("seq") * count
    levels = lax.axis_size("seq").bit_length() - 1
    bits = [link * (levels - 1) // (NEXP - 1) for link in range(NEXP)]

    half = rows * 5 // 8
    early = [partner(node_feats[:half], "seq", bit) for bit in bits[2:]]
    encoding, (early,) = chebyshev(
        struct_feats, op_blocks, laplace_index, series_coef, first_block, (), early,
    )
    late = [partner(node_feats[half:], "seq", bit) for bit in bits[2:]]
    near_far = partner(node_feats, "seq", bits[1])
    encoding, late, near_far = lax.optimization_barrier((encoding, late, near_far))
    feats_far = [near_far] + [jnp.concatenate([a, b], axis=0) for a, b in zip(early, late)]
    encoding_b = encoding.astype(jnp.bfloat16)

    enc_far = [partner(encoding_b, "seq", bit) for bit in bits[1:]]

    def blend(feats, enc):
        encoded = jnp.dot(enc, encode_weight, preferred_element_type=jnp.float32)
        return (feats.astype(jnp.float32) + encoded).astype(jnp.bfloat16)

    kv_weight = qkv_weight[:, D:]
    blended = blend(node_feats, encoding_b)
    queries = lax.dot_general(
        qkv_weight[:, :D], blended, (((0,), (1,)), ((), ())), preferred_element_type=jnp.float32
    ).astype(jnp.bfloat16) * jnp.asarray(1.0 / HD**0.5, jnp.bfloat16)
    all_blended = jnp.concatenate(
        [shift_rows(blended[rows - rim:], "seq", 1), blended, shift_rows(blended[:rim], "seq", -1)]
        + [blend(f, e) for f, e in zip(feats_far, enc_far)],
        axis=0,
    )
    kv_all = jnp.dot(all_blended, kv_weight, preferred_element_type=jnp.float32).astype(
        jnp.bfloat16
    )
    kv_own = kv_all[rim : rim + rows]
    kv_chip = partner(kv_own, "seq", bits[0])

    near_blocks = count + 2 * REACH
    own_slot = jnp.arange(count, dtype=jnp.int32)[:, None] + REACH
    graph_slot = jnp.clip(graph_links - first_block + REACH, 0, near_blocks - 1)
    far_slot = jnp.clip(expander_slot, 0, count - 1)
    far_base = jnp.asarray([0] + [near_blocks + k * count for k in range(NEXP - 1)], jnp.int32)
    table = jnp.concatenate([own_slot, graph_slot, far_slot + far_base[None, :]], axis=1)
    table = table.astype(jnp.int32)
    sources = [kv_all] * 4 + [kv_chip] + [kv_all] * (NEXP - 1)
    return attend(queries, sources, table, out_weight)


def solution(mesh):
    placed = (
        P(("group", "seq"), None),
        P(("group", "seq"), None),
        P(("group", "seq"), None, None, None),
        P(("group", "seq"), None),
        P(("group", "seq"), None),
        P(("group", "seq"), None),
        P(),
        P(),
        P(),
        P(),
    )
    return jax.shard_map(
        on_device, mesh=mesh, in_specs=placed, out_specs=P(("group", "seq"), None), check_vma=False
    )
```

```python
import functools

import jax
import jax.numpy as jnp
from jax import lax
from jax.experimental import pallas as pl
from jax.experimental.pallas import tpu as pltpu
from jax.sharding import PartitionSpec as P

D = 1024
HEADS = 16
HD = 64
BS = 64
DEG = 8
NEXP = 4
REACH = 2
NKEY = 1 + 3 + NEXP
PER_EXCHANGE = 4


def shift_rows(x, axis, step):
    peers = lax.axis_size(axis)
    if step > 0:
        pairs = [(i, i + step) for i in range(peers - step)]
    else:
        pairs = [(i, i + step) for i in range(-step, peers)]
    return lax.ppermute(x, axis, pairs)


def extended(x, axis, width):
    length = x.shape[0]
    before = shift_rows(x[length - width:], axis, 1)
    after = shift_rows(x[:width], axis, -1)
    return jnp.concatenate([before, x, after], axis=0)


def partner(value, axis, distance):
    mask = 2**distance
    pairs = [(source, source ^ mask) for source in range(lax.axis_size(axis))]
    return lax.ppermute(value, axis, pairs)


def apply_operator(field, op_blocks, laplace_index, first_block):
    count = op_blocks.shape[0]
    padded = extended(field, "seq", REACH * BS)
    pooled = padded.reshape(count + 2 * REACH, BS, field.shape[1])
    position = laplace_index - first_block + REACH
    picked = pooled[position]
    result = jnp.einsum("bjst,bjtc->bsc", op_blocks, picked, precision=lax.Precision.HIGHEST)
    return result.reshape(field.shape)


def chebyshev(struct_feats, op_blocks, laplace_index, series_coef, first_block, riders, later):
    count = op_blocks.shape[0]
    chans = struct_feats.shape[1]
    taps = 2 * REACH + 1
    halo = PER_EXCHANGE * REACH
    block_ids = first_block + jnp.arange(count, dtype=jnp.int32)
    offsets = laplace_index - block_ids[:, None] + REACH
    hit = offsets[:, :, None] == jnp.arange(taps, dtype=jnp.int32)[None, None, :]
    bands = jnp.sum(jnp.where(hit[:, :, :, None, None], op_blocks[:, :, None], 0.0), axis=1)
    bands = bands.transpose(0, 2, 1, 3).reshape(count, BS, taps * BS)
    own_field = struct_feats.reshape(count, BS, chans)
    payload = jnp.concatenate([own_field, bands], axis=2)
    left = shift_rows(payload[count - halo :], "seq", 1)
    right = shift_rows(payload[:halo], "seq", -1)
    edge = halo - REACH
    bands = jnp.concatenate(
        [left[halo - edge :, :, chans:], bands, right[:edge, :, chans:]], axis=0
    )
    field = jnp.concatenate([left[:, :, :chans], own_field, right[:, :, :chans]], axis=0)
    width = field.shape[0]

    def step(values, lo, hi, base):
        stacked = jnp.stack(
            [values[lo - REACH + o - base : hi - REACH + o - base] for o in range(taps)], axis=1
        ).reshape(hi - lo, taps * BS, chans)
        return jnp.einsum(
            "wsk,wkc->wsc", bands[lo - REACH : hi - REACH], stacked,
            precision=lax.Precision.HIGH, preferred_element_type=jnp.float32,
        )

    own = slice(halo, halo + count)
    cur, cur_base = field, 0
    prev, prev_base = None, 0
    encoding = series_coef[0] * field[own]
    for degree in range(1, DEG + 1):
        if degree > 1 and (degree - 1) % PER_EXCHANGE == 0:
            older = prev[own.start - prev_base : own.stop - prev_base]
            packed = jnp.concatenate([older, cur], axis=2)
            left = shift_rows(packed[count - halo :], "seq", 1)
            right = shift_rows(packed[:halo], "seq", -1)
            if later is not None:
                left, right, later = lax.optimization_barrier((left, right, later))
                riders = riders + (later,)
                later = None
            prev = jnp.concatenate(
                [left[halo - edge :, :, :chans], older, right[:edge, :, :chans]], axis=0
            )
            prev_base = REACH
            cur = jnp.concatenate([left[:, :, chans:], cur, right[:, :, chans:]], axis=0)
            cur_base = 0
            lo, hi = 0, width
        if degree == 1 or (degree - 1) % PER_EXCHANGE == 0:
            lo, hi = REACH, width - REACH
        else:
            lo, hi = lo + REACH, hi - REACH
        applied = step(cur, lo, hi, cur_base)
        if degree == 1:
            nxt = applied
        else:
            nxt = 2.0 * applied - prev[lo - prev_base : hi - prev_base]
        encoding = encoding + series_coef[degree] * nxt[own.start - lo : own.stop - lo]
        prev, prev_base = cur, cur_base
        cur, cur_base = nxt, lo
    return encoding.reshape(count * BS, chans), riders


def attention_kernel(table_ref, q_ref, *refs):
    kv_refs = refs[:NKEY]
    w_ref, out_ref, att_ref = refs[NKEY:]
    lane = lax.broadcasted_iota(jnp.int32, (1, 2 * HD), 1)
    low = lane < HD
    first = (pl.program_id(0) % 2) == 0
    d_head = lax.broadcasted_iota(jnp.int32, (2 * HD, 2 * BS), 0) // HD
    j_head = lax.broadcasted_iota(jnp.int32, (2 * HD, 2 * BS), 1) // BS
    same = d_head == j_head
    for pair in range(HEADS // 2):
        cols = slice(pair * 2 * HD, (pair + 1) * 2 * HD)
        vcols = slice(D + pair * 2 * HD, D + (pair + 1) * 2 * HD)
        ks = jnp.concatenate([r[:, cols] for r in kv_refs], axis=0)
        vs = jnp.concatenate([r[:, vcols] for r in kv_refs], axis=0)
        tile = q_ref[cols, :].astype(jnp.float32)
        turned = pltpu.roll(tile, BS, 1)
        spread = jnp.where(low == first, tile, turned)
        qbd = jnp.where(same, spread, 0.0).astype(jnp.bfloat16)
        scores = jnp.dot(ks, qbd, preferred_element_type=jnp.float32)
        top = jnp.max(scores, axis=0, keepdims=True)
        expd = jnp.exp(scores - top)
        total = jnp.sum(expd, axis=0, keepdims=True)
        weights = (expd * (1.0 / total)).astype(jnp.bfloat16)
        both = lax.dot_general(
            weights, vs, (((0,), (0,)), ((), ())), preferred_element_type=jnp.float32
        )
        merged = jnp.where(low, both[:BS], both[BS:])
        att_ref[:, cols] = merged.astype(jnp.bfloat16)
    out_ref[...] = jnp.dot(att_ref[...], w_ref[...], preferred_element_type=jnp.float32).astype(
        jnp.bfloat16
    )


def attend(queries, kv_sources, table, out_weight):
    count = table.shape[0]
    pairs = HEADS // 2
    in_specs = [pl.BlockSpec((D, 2 * BS), lambda b, t: (0, b // 2))]
    operands = [queries]
    for j, src in enumerate(kv_sources):
        in_specs.append(pl.BlockSpec((BS, 2 * D), lambda b, t, j=j: (t[b, j], 0)))
        operands.append(src)
    in_specs.append(pl.BlockSpec(out_weight.shape, lambda b, t: (0, 0)))
    operands.append(out_weight)
    grid_spec = pltpu.PrefetchScalarGridSpec(
        num_scalar_prefetch=1,
        grid=(count,),
        in_specs=in_specs,
        out_specs=pl.BlockSpec((BS, D), lambda b, t: (b, 0)),
        scratch_shapes=[pltpu.VMEM((BS, D), jnp.bfloat16)],
    )
    return pl.pallas_call(
        attention_kernel,
        grid_spec=grid_spec,
        out_shape=jax.ShapeDtypeStruct((count * BS, D), jnp.bfloat16),
    )(table, *operands)


def on_device(
    node_feats,
    struct_feats,
    op_blocks,
    laplace_index,
    graph_links,
    expander_slot,
    series_coef,
    encode_weight,
    qkv_weight,
    out_weight,
):
    count = op_blocks.shape[0]
    rows = count * BS
    rim = REACH * BS
    first_block = lax.axis_index("seq") * count
    levels = lax.axis_size("seq").bit_length() - 1
    bits = [link * (levels - 1) // (NEXP - 1) for link in range(NEXP)]

    half = rows * 3 // 8
    early = [partner(node_feats[:half], "seq", bit) for bit in bits[2:]]
    encoding, (early,) = chebyshev(
        struct_feats, op_blocks, laplace_index, series_coef, first_block, (), early,
    )
    late = [partner(node_feats[half:], "seq", bit) for bit in bits[2:]]
    near_far = partner(node_feats, "seq", bits[1])
    encoding, late, near_far = lax.optimization_barrier((encoding, late, near_far))
    feats_far = [near_far] + [jnp.concatenate([a, b], axis=0) for a, b in zip(early, late)]
    encoding_b = encoding.astype(jnp.bfloat16)

    enc_far = [partner(encoding_b, "seq", bit) for bit in bits[1:]]

    def blend(feats, enc):
        encoded = jnp.dot(enc, encode_weight, preferred_element_type=jnp.float32)
        return (feats.astype(jnp.float32) + encoded).astype(jnp.bfloat16)

    kv_weight = qkv_weight[:, D:]
    blended = blend(node_feats, encoding_b)
    queries = lax.dot_general(
        qkv_weight[:, :D], blended, (((0,), (1,)), ((), ())), preferred_element_type=jnp.float32
    ).astype(jnp.bfloat16) * jnp.asarray(1.0 / HD**0.5, jnp.bfloat16)
    all_blended = jnp.concatenate(
        [shift_rows(blended[rows - rim:], "seq", 1), blended, shift_rows(blended[:rim], "seq", -1)]
        + [blend(f, e) for f, e in zip(feats_far, enc_far)],
        axis=0,
    )
    kv_all = jnp.dot(all_blended, kv_weight, preferred_element_type=jnp.float32).astype(
        jnp.bfloat16
    )
    kv_own = kv_all[rim : rim + rows]
    kv_chip = partner(kv_own, "seq", bits[0])

    near_blocks = count + 2 * REACH
    own_slot = jnp.arange(count, dtype=jnp.int32)[:, None] + REACH
    graph_slot = jnp.clip(graph_links - first_block + REACH, 0, near_blocks - 1)
    far_slot = jnp.clip(expander_slot, 0, count - 1)
    far_base = jnp.asarray([0] + [near_blocks + k * count for k in range(NEXP - 1)], jnp.int32)
    table = jnp.concatenate([own_slot, graph_slot, far_slot + far_base[None, :]], axis=1)
    table = table.astype(jnp.int32)
    sources = [kv_all] * 4 + [kv_chip] + [kv_all] * (NEXP - 1)
    return attend(queries, sources, table, out_weight)


def solution(mesh):
    placed = (
        P(("group", "seq"), None),
        P(("group", "seq"), None),
        P(("group", "seq"), None, None, None),
        P(("group", "seq"), None),
        P(("group", "seq"), None),
        P(("group", "seq"), None),
        P(),
        P(),
        P(),
        P(),
    )
    return jax.shard_map(
        on_device, mesh=mesh, in_specs=placed, out_specs=P(("group", "seq"), None), check_vma=False
    )
```

```python
import functools

import jax
import jax.numpy as jnp
from jax import lax
from jax.experimental import pallas as pl
from jax.experimental.pallas import tpu as pltpu
from jax.sharding import PartitionSpec as P

D = 1024
HEADS = 16
HD = 64
BS = 64
DEG = 8
NEXP = 4
REACH = 2
NKEY = 1 + 3 + NEXP
PER_EXCHANGE = 4


def shift_rows(x, axis, step):
    peers = lax.axis_size(axis)
    if step > 0:
        pairs = [(i, i + step) for i in range(peers - step)]
    else:
        pairs = [(i, i + step) for i in range(-step, peers)]
    return lax.ppermute(x, axis, pairs)


def extended(x, axis, width):
    length = x.shape[0]
    before = shift_rows(x[length - width:], axis, 1)
    after = shift_rows(x[:width], axis, -1)
    return jnp.concatenate([before, x, after], axis=0)


def partner(value, axis, distance):
    mask = 2**distance
    pairs = [(source, source ^ mask) for source in range(lax.axis_size(axis))]
    return lax.ppermute(value, axis, pairs)


def apply_operator(field, op_blocks, laplace_index, first_block):
    count = op_blocks.shape[0]
    padded = extended(field, "seq", REACH * BS)
    pooled = padded.reshape(count + 2 * REACH, BS, field.shape[1])
    position = laplace_index - first_block + REACH
    picked = pooled[position]
    result = jnp.einsum("bjst,bjtc->bsc", op_blocks, picked, precision=lax.Precision.HIGHEST)
    return result.reshape(field.shape)


def chebyshev(struct_feats, op_blocks, laplace_index, series_coef, first_block, riders, later):
    count = op_blocks.shape[0]
    chans = struct_feats.shape[1]
    taps = 2 * REACH + 1
    halo = PER_EXCHANGE * REACH
    block_ids = first_block + jnp.arange(count, dtype=jnp.int32)
    offsets = laplace_index - block_ids[:, None] + REACH
    own_field = struct_feats.reshape(count, BS, chans)
    taps_out = []
    for o in range(taps):
        tap = jnp.zeros((count, BS, BS), jnp.float32)
        for j in range(op_blocks.shape[1]):
            tap = tap + jnp.where((offsets[:, j] == o)[:, None, None], op_blocks[:, j], 0.0)
        taps_out.append(tap)
    payload = jnp.concatenate([own_field] + taps_out, axis=2)
    bands = payload[:, :, chans:]
    left = shift_rows(payload[count - halo :], "seq", 1)
    right = shift_rows(payload[:halo], "seq", -1)
    edge = halo - REACH
    bands = jnp.concatenate(
        [left[halo - edge :, :, chans:], bands, right[:edge, :, chans:]], axis=0
    )
    field = jnp.concatenate([left[:, :, :chans], own_field, right[:, :, :chans]], axis=0)
    width = field.shape[0]

    def step(values, lo, hi, base):
        stacked = jnp.stack(
            [values[lo - REACH + o - base : hi - REACH + o - base] for o in range(taps)], axis=1
        ).reshape(hi - lo, taps * BS, chans)
        return jnp.einsum(
            "wsk,wkc->wsc", bands[lo - REACH : hi - REACH], stacked,
            precision=lax.Precision.HIGH, preferred_element_type=jnp.float32,
        )

    own = slice(halo, halo + count)
    cur, cur_base = field, 0
    prev, prev_base = None, 0
    encoding = series_coef[0] * field[own]
    for degree in range(1, DEG + 1):
        if degree > 1 and (degree - 1) % PER_EXCHANGE == 0:
            older = prev[own.start - prev_base : own.stop - prev_base]
            packed = jnp.concatenate([older, cur], axis=2)
            left = shift_rows(packed[count - halo :], "seq", 1)
            right = shift_rows(packed[:halo], "seq", -1)
            if later is not None:
                left, right, later = lax.optimization_barrier((left, right, later))
                riders = riders + (later,)
                later = None
            prev = jnp.concatenate(
                [left[halo - edge :, :, :chans], older, right[:edge, :, :chans]], axis=0
            )
            prev_base = REACH
            cur = jnp.concatenate([left[:, :, chans:], cur, right[:, :, chans:]], axis=0)
            cur_base = 0
            lo, hi = 0, width
        if degree == 1 or (degree - 1) % PER_EXCHANGE == 0:
            lo, hi = REACH, width - REACH
        else:
            lo, hi = lo + REACH, hi - REACH
        applied = step(cur, lo, hi, cur_base)
        if degree == 1:
            nxt = applied
        else:
            nxt = 2.0 * applied - prev[lo - prev_base : hi - prev_base]
        encoding = encoding + series_coef[degree] * nxt[own.start - lo : own.stop - lo]
        prev, prev_base = cur, cur_base
        cur, cur_base = nxt, lo
    return encoding.reshape(count * BS, chans), riders


def attention_kernel(table_ref, q_ref, *refs):
    kv_refs = refs[:NKEY]
    w_ref, out_ref, att_ref = refs[NKEY:]
    lane = lax.broadcasted_iota(jnp.int32, (1, 2 * HD), 1)
    low = lane < HD
    first = (pl.program_id(0) % 2) == 0
    d_head = lax.broadcasted_iota(jnp.int32, (2 * HD, 2 * BS), 0) // HD
    j_head = lax.broadcasted_iota(jnp.int32, (2 * HD, 2 * BS), 1) // BS
    same = d_head == j_head
    for pair in range(HEADS // 2):
        cols = slice(pair * 2 * HD, (pair + 1) * 2 * HD)
        vcols = slice(D + pair * 2 * HD, D + (pair + 1) * 2 * HD)
        ks = jnp.concatenate([r[:, cols] for r in kv_refs], axis=0)
        vs = jnp.concatenate([r[:, vcols] for r in kv_refs], axis=0)
        tile = q_ref[cols, :].astype(jnp.float32)
        turned = pltpu.roll(tile, BS, 1)
        spread = jnp.where(low == first, tile, turned)
        qbd = jnp.where(same, spread, 0.0).astype(jnp.bfloat16)
        scores = jnp.dot(ks, qbd, preferred_element_type=jnp.float32)
        top = jnp.max(scores, axis=0, keepdims=True)
        expd = jnp.exp(scores - top)
        total = jnp.sum(expd, axis=0, keepdims=True)
        weights = (expd * (1.0 / total)).astype(jnp.bfloat16)
        both = lax.dot_general(
            weights, vs, (((0,), (0,)), ((), ())), preferred_element_type=jnp.float32
        )
        merged = jnp.where(low, both[:BS], both[BS:])
        att_ref[:, cols] = merged.astype(jnp.bfloat16)
    out_ref[...] = jnp.dot(att_ref[...], w_ref[...], preferred_element_type=jnp.float32).astype(
        jnp.bfloat16
    )


def attend(queries, kv_sources, table, out_weight):
    count = table.shape[0]
    pairs = HEADS // 2
    in_specs = [pl.BlockSpec((D, 2 * BS), lambda b, t: (0, b // 2))]
    operands = [queries]
    for j, src in enumerate(kv_sources):
        in_specs.append(pl.BlockSpec((BS, 2 * D), lambda b, t, j=j: (t[b, j], 0)))
        operands.append(src)
    in_specs.append(pl.BlockSpec(out_weight.shape, lambda b, t: (0, 0)))
    operands.append(out_weight)
    grid_spec = pltpu.PrefetchScalarGridSpec(
        num_scalar_prefetch=1,
        grid=(count,),
        in_specs=in_specs,
        out_specs=pl.BlockSpec((BS, D), lambda b, t: (b, 0)),
        scratch_shapes=[pltpu.VMEM((BS, D), jnp.bfloat16)],
    )
    return pl.pallas_call(
        attention_kernel,
        grid_spec=grid_spec,
        out_shape=jax.ShapeDtypeStruct((count * BS, D), jnp.bfloat16),
    )(table, *operands)


def on_device(
    node_feats,
    struct_feats,
    op_blocks,
    laplace_index,
    graph_links,
    expander_slot,
    series_coef,
    encode_weight,
    qkv_weight,
    out_weight,
):
    count = op_blocks.shape[0]
    rows = count * BS
    rim = REACH * BS
    first_block = lax.axis_index("seq") * count
    levels = lax.axis_size("seq").bit_length() - 1
    bits = [link * (levels - 1) // (NEXP - 1) for link in range(NEXP)]

    half = rows // 2
    early = [partner(node_feats[:half], "seq", bit) for bit in bits[2:]]
    encoding, (early,) = chebyshev(
        struct_feats, op_blocks, laplace_index, series_coef, first_block, (), early,
    )
    late = [partner(node_feats[half:], "seq", bit) for bit in bits[2:]]
    near_far = partner(node_feats, "seq", bits[1])
    encoding, late, near_far = lax.optimization_barrier((encoding, late, near_far))
    feats_far = [near_far] + [jnp.concatenate([a, b], axis=0) for a, b in zip(early, late)]
    encoding_b = encoding.astype(jnp.bfloat16)

    enc_far = [partner(encoding_b, "seq", bit) for bit in bits[1:]]

    def blend(feats, enc):
        encoded = jnp.dot(enc, encode_weight, preferred_element_type=jnp.float32)
        return (feats.astype(jnp.float32) + encoded).astype(jnp.bfloat16)

    kv_weight = qkv_weight[:, D:]
    blended = blend(node_feats, encoding_b)
    queries = lax.dot_general(
        qkv_weight[:, :D], blended, (((0,), (1,)), ((), ())), preferred_element_type=jnp.float32
    ).astype(jnp.bfloat16) * jnp.asarray(1.0 / HD**0.5, jnp.bfloat16)
    all_blended = jnp.concatenate(
        [shift_rows(blended[rows - rim:], "seq", 1), blended, shift_rows(blended[:rim], "seq", -1)]
        + [blend(f, e) for f, e in zip(feats_far, enc_far)],
        axis=0,
    )
    kv_all = jnp.dot(all_blended, kv_weight, preferred_element_type=jnp.float32).astype(
        jnp.bfloat16
    )
    kv_own = kv_all[rim : rim + rows]
    kv_chip = partner(kv_own, "seq", bits[0])

    near_blocks = count + 2 * REACH
    own_slot = jnp.arange(count, dtype=jnp.int32)[:, None] + REACH
    graph_slot = jnp.clip(graph_links - first_block + REACH, 0, near_blocks - 1)
    far_slot = jnp.clip(expander_slot, 0, count - 1)
    far_base = jnp.asarray([0] + [near_blocks + k * count for k in range(NEXP - 1)], jnp.int32)
    table = jnp.concatenate([own_slot, graph_slot, far_slot + far_base[None, :]], axis=1)
    table = table.astype(jnp.int32)
    sources = [kv_all] * 4 + [kv_chip] + [kv_all] * (NEXP - 1)
    return attend(queries, sources, table, out_weight)


def solution(mesh):
    placed = (
        P(("group", "seq"), None),
        P(("group", "seq"), None),
        P(("group", "seq"), None, None, None),
        P(("group", "seq"), None),
        P(("group", "seq"), None),
        P(("group", "seq"), None),
        P(),
        P(),
        P(),
        P(),
    )
    return jax.shard_map(
        on_device, mesh=mesh, in_specs=placed, out_specs=P(("group", "seq"), None), check_vma=False
    )
```

```python
import functools

import jax
import jax.numpy as jnp
from jax import lax
from jax.experimental import pallas as pl
from jax.experimental.pallas import tpu as pltpu
from jax.sharding import PartitionSpec as P

D = 1024
HEADS = 16
HD = 64
BS = 64
DEG = 8
NEXP = 4
REACH = 2
NKEY = 1 + 3 + NEXP
PER_EXCHANGE = 4


def shift_rows(x, axis, step):
    peers = lax.axis_size(axis)
    if step > 0:
        pairs = [(i, i + step) for i in range(peers - step)]
    else:
        pairs = [(i, i + step) for i in range(-step, peers)]
    return lax.ppermute(x, axis, pairs)


def extended(x, axis, width):
    length = x.shape[0]
    before = shift_rows(x[length - width:], axis, 1)
    after = shift_rows(x[:width], axis, -1)
    return jnp.concatenate([before, x, after], axis=0)


def partner(value, axis, distance):
    mask = 2**distance
    pairs = [(source, source ^ mask) for source in range(lax.axis_size(axis))]
    return lax.ppermute(value, axis, pairs)


def apply_operator(field, op_blocks, laplace_index, first_block):
    count = op_blocks.shape[0]
    padded = extended(field, "seq", REACH * BS)
    pooled = padded.reshape(count + 2 * REACH, BS, field.shape[1])
    position = laplace_index - first_block + REACH
    picked = pooled[position]
    result = jnp.einsum("bjst,bjtc->bsc", op_blocks, picked, precision=lax.Precision.HIGHEST)
    return result.reshape(field.shape)


def chebyshev(struct_feats, op_blocks, laplace_index, series_coef, first_block, riders, later):
    count = op_blocks.shape[0]
    chans = struct_feats.shape[1]
    taps = 2 * REACH + 1
    halo = PER_EXCHANGE * REACH
    block_ids = first_block + jnp.arange(count, dtype=jnp.int32)
    offsets = laplace_index - block_ids[:, None] + REACH
    hit = offsets[:, :, None] == jnp.arange(taps, dtype=jnp.int32)[None, None, :]
    bands = jnp.sum(jnp.where(hit[:, :, :, None, None], op_blocks[:, :, None], 0.0), axis=1)
    bands = bands.transpose(0, 2, 1, 3).reshape(count, BS, taps * BS)
    own_field = struct_feats.reshape(count, BS, chans)
    payload = jnp.concatenate([own_field, bands], axis=2)
    left = shift_rows(payload[count - halo :], "seq", 1)
    right = shift_rows(payload[:halo], "seq", -1)
    edge = halo - REACH
    bands = jnp.concatenate(
        [left[halo - edge :, :, chans:], bands, right[:edge, :, chans:]], axis=0
    )
    field = jnp.concatenate([left[:, :, :chans], own_field, right[:, :, :chans]], axis=0)
    width = field.shape[0]

    def step(values, lo, hi, base):
        stacked = jnp.stack(
            [values[lo - REACH + o - base : hi - REACH + o - base] for o in range(taps)], axis=1
        ).reshape(hi - lo, taps * BS, chans)
        return jnp.einsum(
            "wsk,wkc->wsc", bands[lo - REACH : hi - REACH], stacked,
            precision=lax.Precision.HIGHEST, preferred_element_type=jnp.float32,
        )

    own = slice(halo, halo + count)
    cur, cur_base = field, 0
    prev, prev_base = None, 0
    encoding = series_coef[0] * field[own]
    for degree in range(1, DEG + 1):
        if degree > 1 and (degree - 1) % PER_EXCHANGE == 0:
            older = prev[own.start - prev_base : own.stop - prev_base]
            packed = jnp.concatenate([older, cur], axis=2)
            left = shift_rows(packed[count - halo :], "seq", 1)
            right = shift_rows(packed[:halo], "seq", -1)
            if later is not None:
                left, right, later = lax.optimization_barrier((left, right, later))
                riders = riders + (later,)
                later = None
            prev = jnp.concatenate(
                [left[halo - edge :, :, :chans], older, right[:edge, :, :chans]], axis=0
            )
            prev_base = REACH
            cur = jnp.concatenate([left[:, :, chans:], cur, right[:, :, chans:]], axis=0)
            cur_base = 0
            lo, hi = 0, width
        if degree == 1 or (degree - 1) % PER_EXCHANGE == 0:
            lo, hi = REACH, width - REACH
        else:
            lo, hi = lo + REACH, hi - REACH
        applied = step(cur, lo, hi, cur_base)
        if degree == 1:
            nxt = applied
        else:
            nxt = 2.0 * applied - prev[lo - prev_base : hi - prev_base]
        encoding = encoding + series_coef[degree] * nxt[own.start - lo : own.stop - lo]
        prev, prev_base = cur, cur_base
        cur, cur_base = nxt, lo
    return encoding.reshape(count * BS, chans), riders


def attention_kernel(table_ref, q_ref, *refs):
    kv_refs = refs[:NKEY]
    w_ref, out_ref, att_ref = refs[NKEY:]
    lane = lax.broadcasted_iota(jnp.int32, (1, 2 * HD), 1)
    low = lane < HD
    first = (pl.program_id(0) % 2) == 0
    d_head = lax.broadcasted_iota(jnp.int32, (2 * HD, 2 * BS), 0) // HD
    j_head = lax.broadcasted_iota(jnp.int32, (2 * HD, 2 * BS), 1) // BS
    same = d_head == j_head
    for pair in range(HEADS // 2):
        cols = slice(pair * 2 * HD, (pair + 1) * 2 * HD)
        vcols = slice(D + pair * 2 * HD, D + (pair + 1) * 2 * HD)
        ks = jnp.concatenate([r[:, cols] for r in kv_refs], axis=0)
        vs = jnp.concatenate([r[:, vcols] for r in kv_refs], axis=0)
        tile = q_ref[cols, :].astype(jnp.float32)
        turned = pltpu.roll(tile, BS, 1)
        spread = jnp.where(low == first, tile, turned)
        qbd = jnp.where(same, spread, 0.0).astype(jnp.bfloat16)
        scores = jnp.dot(ks, qbd, preferred_element_type=jnp.float32)
        top = jnp.max(scores, axis=0, keepdims=True)
        expd = jnp.exp(scores - top)
        total = jnp.sum(expd, axis=0, keepdims=True)
        weights = (expd * (1.0 / total)).astype(jnp.bfloat16)
        both = lax.dot_general(
            weights, vs, (((0,), (0,)), ((), ())), preferred_element_type=jnp.float32
        )
        merged = jnp.where(low, both[:BS], both[BS:])
        att_ref[:, cols] = merged.astype(jnp.bfloat16)
    out_ref[...] = jnp.dot(att_ref[...], w_ref[...], preferred_element_type=jnp.float32).astype(
        jnp.bfloat16
    )


def attend(queries, kv_sources, table, out_weight):
    count = table.shape[0]
    pairs = HEADS // 2
    in_specs = [pl.BlockSpec((D, 2 * BS), lambda b, t: (0, b // 2))]
    operands = [queries]
    for j, src in enumerate(kv_sources):
        in_specs.append(pl.BlockSpec((BS, 2 * D), lambda b, t, j=j: (t[b, j], 0)))
        operands.append(src)
    in_specs.append(pl.BlockSpec(out_weight.shape, lambda b, t: (0, 0)))
    operands.append(out_weight)
    grid_spec = pltpu.PrefetchScalarGridSpec(
        num_scalar_prefetch=1,
        grid=(count,),
        in_specs=in_specs,
        out_specs=pl.BlockSpec((BS, D), lambda b, t: (b, 0)),
        scratch_shapes=[pltpu.VMEM((BS, D), jnp.bfloat16)],
    )
    return pl.pallas_call(
        attention_kernel,
        grid_spec=grid_spec,
        out_shape=jax.ShapeDtypeStruct((count * BS, D), jnp.bfloat16),
    )(table, *operands)


def on_device(
    node_feats,
    struct_feats,
    op_blocks,
    laplace_index,
    graph_links,
    expander_slot,
    series_coef,
    encode_weight,
    qkv_weight,
    out_weight,
):
    count = op_blocks.shape[0]
    rows = count * BS
    rim = REACH * BS
    first_block = lax.axis_index("seq") * count
    levels = lax.axis_size("seq").bit_length() - 1
    bits = [link * (levels - 1) // (NEXP - 1) for link in range(NEXP)]

    half = rows // 2
    early = [partner(node_feats[:half], "seq", bit) for bit in bits[2:]]
    encoding, (early,) = chebyshev(
        struct_feats, op_blocks, laplace_index, series_coef, first_block, (), early,
    )
    late = [partner(node_feats[half:], "seq", bit) for bit in bits[2:]]
    near_far = partner(node_feats, "seq", bits[1])
    encoding, late, near_far = lax.optimization_barrier((encoding, late, near_far))
    feats_far = [near_far] + [jnp.concatenate([a, b], axis=0) for a, b in zip(early, late)]
    encoding_b = encoding.astype(jnp.bfloat16)

    enc_far = [partner(encoding_b, "seq", bit) for bit in bits[1:]]

    def blend(feats, enc):
        encoded = jnp.dot(enc, encode_weight, preferred_element_type=jnp.float32)
        return (feats.astype(jnp.float32) + encoded).astype(jnp.bfloat16)

    kv_weight = qkv_weight[:, D:]
    blended = blend(node_feats, encoding_b)
    queries = lax.dot_general(
        qkv_weight[:, :D], blended, (((0,), (1,)), ((), ())), preferred_element_type=jnp.float32
    ).astype(jnp.bfloat16) * jnp.asarray(1.0 / HD**0.5, jnp.bfloat16)
    all_blended = jnp.concatenate(
        [shift_rows(blended[rows - rim:], "seq", 1), blended, shift_rows(blended[:rim], "seq", -1)]
        + [blend(f, e) for f, e in zip(feats_far, enc_far)],
        axis=0,
    )
    kv_all = jnp.dot(all_blended, kv_weight, preferred_element_type=jnp.float32).astype(
        jnp.bfloat16
    )
    kv_own = kv_all[rim : rim + rows]
    kv_chip = partner(kv_own, "seq", bits[0])

    near_blocks = count + 2 * REACH
    own_slot = jnp.arange(count, dtype=jnp.int32)[:, None] + REACH
    graph_slot = jnp.clip(graph_links - first_block + REACH, 0, near_blocks - 1)
    far_slot = jnp.clip(expander_slot, 0, count - 1)
    far_base = jnp.asarray([0] + [near_blocks + k * count for k in range(NEXP - 1)], jnp.int32)
    table = jnp.concatenate([own_slot, graph_slot, far_slot + far_base[None, :]], axis=1)
    table = table.astype(jnp.int32)
    sources = [kv_all] * 4 + [kv_chip] + [kv_all] * (NEXP - 1)
    return attend(queries, sources, table, out_weight)


def solution(mesh):
    placed = (
        P(("group", "seq"), None),
        P(("group", "seq"), None),
        P(("group", "seq"), None, None, None),
        P(("group", "seq"), None),
        P(("group", "seq"), None),
        P(("group", "seq"), None),
        P(),
        P(),
        P(),
        P(),
    )
    return jax.shard_map(
        on_device, mesh=mesh, in_specs=placed, out_specs=P(("group", "seq"), None), check_vma=False
    )
```

```python
import functools

import jax
import jax.numpy as jnp
from jax import lax
from jax.experimental import pallas as pl
from jax.experimental.pallas import tpu as pltpu
from jax.sharding import PartitionSpec as P

D = 1024
HEADS = 16
HD = 64
BS = 64
DEG = 8
NEXP = 4
REACH = 2
NKEY = 1 + 3 + NEXP
PER_EXCHANGE = 4


def shift_rows(x, axis, step):
    peers = lax.axis_size(axis)
    if step > 0:
        pairs = [(i, i + step) for i in range(peers - step)]
    else:
        pairs = [(i, i + step) for i in range(-step, peers)]
    return lax.ppermute(x, axis, pairs)


def extended(x, axis, width):
    length = x.shape[0]
    before = shift_rows(x[length - width:], axis, 1)
    after = shift_rows(x[:width], axis, -1)
    return jnp.concatenate([before, x, after], axis=0)


def partner(value, axis, distance):
    mask = 2**distance
    pairs = [(source, source ^ mask) for source in range(lax.axis_size(axis))]
    return lax.ppermute(value, axis, pairs)


def apply_operator(field, op_blocks, laplace_index, first_block):
    count = op_blocks.shape[0]
    padded = extended(field, "seq", REACH * BS)
    pooled = padded.reshape(count + 2 * REACH, BS, field.shape[1])
    position = laplace_index - first_block + REACH
    picked = pooled[position]
    result = jnp.einsum("bjst,bjtc->bsc", op_blocks, picked, precision=lax.Precision.HIGHEST)
    return result.reshape(field.shape)


def chebyshev(struct_feats, op_blocks, laplace_index, series_coef, first_block, riders, later):
    count = op_blocks.shape[0]
    chans = struct_feats.shape[1]
    taps = 2 * REACH + 1
    halo = PER_EXCHANGE * REACH
    block_ids = first_block + jnp.arange(count, dtype=jnp.int32)
    offsets = laplace_index - block_ids[:, None] + REACH
    hit = offsets[:, :, None] == jnp.arange(taps, dtype=jnp.int32)[None, None, :]
    bands = jnp.sum(jnp.where(hit[:, :, :, None, None], op_blocks[:, :, None], 0.0), axis=1)
    bands = bands.transpose(0, 2, 1, 3).reshape(count, BS, taps * BS)
    own_field = struct_feats.reshape(count, BS, chans)
    payload = jnp.concatenate([own_field, bands], axis=2)
    left = shift_rows(payload[count - halo :], "seq", 1)
    right = shift_rows(payload[:halo], "seq", -1)
    edge = halo - REACH
    bands = jnp.concatenate(
        [left[halo - edge :, :, chans:], bands, right[:edge, :, chans:]], axis=0
    )
    field = jnp.concatenate([left[:, :, :chans], own_field, right[:, :, :chans]], axis=0)
    width = field.shape[0]

    def step(values, lo, hi, base):
        stacked = jnp.stack(
            [values[lo - REACH + o - base : hi - REACH + o - base] for o in range(taps)], axis=1
        ).reshape(hi - lo, taps * BS, chans)
        return jnp.einsum(
            "wsk,wkc->wsc", bands[lo - REACH : hi - REACH], stacked,
            precision=lax.Precision.HIGH, preferred_element_type=jnp.float32,
        )

    own = slice(halo, halo + count)
    cur, cur_base = field, 0
    prev, prev_base = None, 0
    encoding = series_coef[0] * field[own]
    for degree in range(1, DEG + 1):
        if degree > 1 and (degree - 1) % PER_EXCHANGE == 0:
            older = prev[own.start - prev_base : own.stop - prev_base]
            left = shift_rows(
                jnp.concatenate([older[count - edge :], cur[count - halo :]], axis=0), "seq", 1
            )
            right = shift_rows(jnp.concatenate([older[:edge], cur[:halo]], axis=0), "seq", -1)
            if later is not None:
                left, right, later = lax.optimization_barrier((left, right, later))
                riders = riders + (later,)
                later = None
            prev = jnp.concatenate([left[:edge], older, right[:edge]], axis=0)
            prev_base = REACH
            cur = jnp.concatenate([left[edge:], cur, right[edge:]], axis=0)
            cur_base = 0
            lo, hi = 0, width
        if degree == 1 or (degree - 1) % PER_EXCHANGE == 0:
            lo, hi = REACH, width - REACH
        else:
            lo, hi = lo + REACH, hi - REACH
        applied = step(cur, lo, hi, cur_base)
        if degree == 1:
            nxt = applied
        else:
            nxt = 2.0 * applied - prev[lo - prev_base : hi - prev_base]
        encoding = encoding + series_coef[degree] * nxt[own.start - lo : own.stop - lo]
        prev, prev_base = cur, cur_base
        cur, cur_base = nxt, lo
    return encoding.reshape(count * BS, chans), riders


def attention_kernel(table_ref, q_ref, *refs):
    kv_refs = refs[:NKEY]
    w_ref, out_ref, att_ref = refs[NKEY:]
    lane = lax.broadcasted_iota(jnp.int32, (1, 2 * HD), 1)
    low = lane < HD
    first = (pl.program_id(0) % 2) == 0
    d_head = lax.broadcasted_iota(jnp.int32, (2 * HD, 2 * BS), 0) // HD
    j_head = lax.broadcasted_iota(jnp.int32, (2 * HD, 2 * BS), 1) // BS
    same = d_head == j_head
    for pair in range(HEADS // 2):
        cols = slice(pair * 2 * HD, (pair + 1) * 2 * HD)
        vcols = slice(D + pair * 2 * HD, D + (pair + 1) * 2 * HD)
        ks = jnp.concatenate([r[:, cols] for r in kv_refs], axis=0)
        vs = jnp.concatenate([r[:, vcols] for r in kv_refs], axis=0)
        tile = q_ref[cols, :].astype(jnp.float32)
        turned = pltpu.roll(tile, BS, 1)
        spread = jnp.where(low == first, tile, turned)
        qbd = jnp.where(same, spread, 0.0).astype(jnp.bfloat16)
        scores = jnp.dot(ks, qbd, preferred_element_type=jnp.float32)
        top = jnp.max(scores, axis=0, keepdims=True)
        expd = jnp.exp(scores - top)
        total = jnp.sum(expd, axis=0, keepdims=True)
        weights = (expd * (1.0 / total)).astype(jnp.bfloat16)
        both = lax.dot_general(
            weights, vs, (((0,), (0,)), ((), ())), preferred_element_type=jnp.float32
        )
        merged = jnp.where(low, both[:BS], both[BS:])
        att_ref[:, cols] = merged.astype(jnp.bfloat16)
    out_ref[...] = jnp.dot(att_ref[...], w_ref[...], preferred_element_type=jnp.float32).astype(
        jnp.bfloat16
    )


def attend(queries, kv_sources, table, out_weight):
    count = table.shape[0]
    pairs = HEADS // 2
    in_specs = [pl.BlockSpec((D, 2 * BS), lambda b, t: (0, b // 2))]
    operands = [queries]
    for j, src in enumerate(kv_sources):
        in_specs.append(pl.BlockSpec((BS, 2 * D), lambda b, t, j=j: (t[b, j], 0)))
        operands.append(src)
    in_specs.append(pl.BlockSpec(out_weight.shape, lambda b, t: (0, 0)))
    operands.append(out_weight)
    grid_spec = pltpu.PrefetchScalarGridSpec(
        num_scalar_prefetch=1,
        grid=(count,),
        in_specs=in_specs,
        out_specs=pl.BlockSpec((BS, D), lambda b, t: (b, 0)),
        scratch_shapes=[pltpu.VMEM((BS, D), jnp.bfloat16)],
    )
    return pl.pallas_call(
        attention_kernel,
        grid_spec=grid_spec,
        out_shape=jax.ShapeDtypeStruct((count * BS, D), jnp.bfloat16),
    )(table, *operands)


def on_device(
    node_feats,
    struct_feats,
    op_blocks,
    laplace_index,
    graph_links,
    expander_slot,
    series_coef,
    encode_weight,
    qkv_weight,
    out_weight,
):
    count = op_blocks.shape[0]
    rows = count * BS
    rim = REACH * BS
    first_block = lax.axis_index("seq") * count
    levels = lax.axis_size("seq").bit_length() - 1
    bits = [link * (levels - 1) // (NEXP - 1) for link in range(NEXP)]

    half = rows // 2
    early = [partner(node_feats[:half], "seq", bit) for bit in bits[2:]]
    encoding, (early,) = chebyshev(
        struct_feats, op_blocks, laplace_index, series_coef, first_block, (), early,
    )
    late = [partner(node_feats[half:], "seq", bit) for bit in bits[2:]]
    near_far = partner(node_feats, "seq", bits[1])
    encoding, late, near_far = lax.optimization_barrier((encoding, late, near_far))
    feats_far = [near_far] + [jnp.concatenate([a, b], axis=0) for a, b in zip(early, late)]
    encoding_b = encoding.astype(jnp.bfloat16)

    enc_far = [partner(encoding_b, "seq", bit) for bit in bits[1:]]

    def blend(feats, enc):
        encoded = jnp.dot(enc, encode_weight, preferred_element_type=jnp.float32)
        return (feats.astype(jnp.float32) + encoded).astype(jnp.bfloat16)

    kv_weight = qkv_weight[:, D:]
    blended = blend(node_feats, encoding_b)
    queries = lax.dot_general(
        qkv_weight[:, :D], blended, (((0,), (1,)), ((), ())), preferred_element_type=jnp.float32
    ).astype(jnp.bfloat16) * jnp.asarray(1.0 / HD**0.5, jnp.bfloat16)
    all_blended = jnp.concatenate(
        [shift_rows(blended[rows - rim:], "seq", 1), blended, shift_rows(blended[:rim], "seq", -1)]
        + [blend(f, e) for f, e in zip(feats_far, enc_far)],
        axis=0,
    )
    kv_all = jnp.dot(all_blended, kv_weight, preferred_element_type=jnp.float32).astype(
        jnp.bfloat16
    )
    kv_own = kv_all[rim : rim + rows]
    kv_chip = partner(kv_own, "seq", bits[0])

    near_blocks = count + 2 * REACH
    own_slot = jnp.arange(count, dtype=jnp.int32)[:, None] + REACH
    graph_slot = jnp.clip(graph_links - first_block + REACH, 0, near_blocks - 1)
    far_slot = jnp.clip(expander_slot, 0, count - 1)
    far_base = jnp.asarray([0] + [near_blocks + k * count for k in range(NEXP - 1)], jnp.int32)
    table = jnp.concatenate([own_slot, graph_slot, far_slot + far_base[None, :]], axis=1)
    table = table.astype(jnp.int32)
    sources = [kv_all] * 4 + [kv_chip] + [kv_all] * (NEXP - 1)
    return attend(queries, sources, table, out_weight)


def solution(mesh):
    placed = (
        P(("group", "seq"), None),
        P(("group", "seq"), None),
        P(("group", "seq"), None, None, None),
        P(("group", "seq"), None),
        P(("group", "seq"), None),
        P(("group", "seq"), None),
        P(),
        P(),
        P(),
        P(),
    )
    return jax.shard_map(
        on_device, mesh=mesh, in_specs=placed, out_specs=P(("group", "seq"), None), check_vma=False
    )
```
